32 devices in a mesh: groups: 2 (over x), ctx: 16 (over z, y, core).
Axes of the slice: x: 2, y: 2, z: 4, core: 2. Of those that a mesh axis runs over, the one named last changes fastest.
Arguments:
- tokens: bfloat16 [16384, 2048], P(('groups', 'ctx')), parts along dimension 0, may hold values from -14 to 14, as said below
- projected: bfloat16 [16384, 6144], P(('groups', 'ctx')), parts along dimension 0, may hold values from -6 to 6
- short_filter: float32 [3, 6144], replicated, may hold values from -3 to 3
- long_filter: bfloat16 [128, 128], replicated, may hold values from -0.5 to 0.5
- conv_bias: float32 [2048], replicated, may hold values from 0.5 to 1.5
- out_weight: bfloat16 [2048, 2048], P(None, 'ctx'), may hold values from -0.125 to 0.125
Outputs:
- result: bfloat16 [16384, 2048], P(('groups', 'ctx')), parts along dimension 0
The draws below stay inside these ranges and needn't reach their ends.
There are 2 independent parts, one for each index of `groups`. The reference program is written for one: setup_inputs(seed, part) draws one part's arguments, and reference() takes and returns one part's arrays. A program takes and returns all parts, laid end to end along the dimension named above; an argument that names none is the same for every part. Nothing has to cross between parts.
Inputs may be any that keep to these rules, and one draw needn't show every extreme that they name: `tokens`: activations of the residual stream.
All inputs are finite; a program needn't handle non-finite values.
Results may differ from the reference program's by a relative error of at most 0.012.
Values may be sent and summed in bfloat16 or wider, within the bound.
No kernel may reach another device: no remote copies, remote signals or barrier semaphores. Data moves between devices by JAX's collectives and lax.ppermute only.
A program may use at most 128 MiB of HBM per device.

```python
import jax
import jax.numpy as jnp
from jax import lax

D = 2048
CH = 2048
GROUP = 16
GROUPS = 128
SHORT = 3
KLEN = 128
LENGTH = 8192


def draw_tokens(key, part):
    base = jnp.clip(jax.random.normal(jax.random.fold_in(key, 3), (LENGTH, D), jnp.float32), -6.0, 6.0)
    return base.astype(jnp.bfloat16)


def steps_of(rng, extent, shards, least, high):
    def one(dim, blocks):
        steps = jax.random.uniform(jax.random.fold_in(jax.random.fold_in(rng, 6), dim), (blocks,), jnp.float32, least / len(shards), high / len(shards))
        return jnp.repeat(jnp.exp(steps), extent[dim] // blocks).reshape((-1,) + (1,) * (len(extent) - dim - 1))

    gain = one(*shards[0])
    for cut in shards[1:]:
        gain = gain * one(*cut)
    return gain


def bell_draw(own_key, extent, spread, most, pieces=(), held_as=jnp.bfloat16):
    entries = spread * jax.random.normal(own_key, extent, jnp.float32)
    if pieces:
        entries = entries * steps_of(own_key, extent, pieces, -0.22, 0.18)
    return jnp.clip(entries, -most, most).astype(held_as)


def setup_inputs(seed: int = 0, part: int = 0) -> dict:
    splits = jax.random.split(jax.random.key(seed), 7)
    part_keys = jax.random.split(jax.random.fold_in(splits[6], part), 7)
    return {
        "tokens": draw_tokens(jax.random.fold_in(jax.random.fold_in(splits[6], part), 71), part),
        "projected": bell_draw(part_keys[1], (LENGTH, 3 * CH), 1.0, 6.0, ((0, 16),)),
        "short_filter": bell_draw(splits[2], (SHORT, 3 * CH), 0.6, 3.0, (), jnp.float32),
        "long_filter": bell_draw(splits[3], (GROUPS, KLEN), KLEN ** -0.5, 0.5),
        "conv_bias": jnp.clip(jax.random.uniform(splits[4], (CH,), jnp.float32, 0.5, 1.5), 0.5, 1.5),
        "out_weight": bell_draw(splits[5], (CH, D), CH ** -0.5, 0.125, ((1, 16),)),
    }


def reference(tokens, projected, short_filter, long_filter, conv_bias, out_weight):
    padded = jnp.concatenate([jnp.zeros((2, 3 * CH), jnp.bfloat16), projected], axis=0).astype(jnp.float32)
    mixed = short_filter[0] * padded[2:] + short_filter[1] * padded[1:-1] + short_filter[2] * padded[:-2]
    gate_rows = mixed[:, :CH]
    carried = (mixed[:, CH:2 * CH] * mixed[:, 2 * CH:]).astype(jnp.bfloat16)
    carried_pad = jnp.concatenate([jnp.zeros((KLEN - 1, CH), jnp.bfloat16), carried], axis=0)
    channel_taps = jnp.repeat(long_filter.astype(jnp.float32), GROUP, axis=0)

    def add_tap(step, total):
        offset = (KLEN - 1 - step).astype(jnp.int32)
        window = lax.dynamic_slice_in_dim(carried_pad, offset, LENGTH, 0).astype(jnp.float32)
        tap = lax.dynamic_index_in_dim(channel_taps, step.astype(jnp.int32), 1, keepdims=False)
        return total + window * tap[None, :]

    conv = lax.fori_loop(0, KLEN, add_tap, jnp.zeros((LENGTH, CH), jnp.float32))
    gated = (gate_rows * (conv + conv_bias * carried.astype(jnp.float32))).astype(jnp.bfloat16)
    branch = jnp.dot(gated, out_weight, preferred_element_type=jnp.float32)
    return (tokens.astype(jnp.float32) + branch).astype(jnp.bfloat16)
```

```python
import jax
import jax.numpy as jnp
from jax import lax
from jax.sharding import Mesh
from jax.sharding import PartitionSpec as P

CTX = ("chip", "core")


def split_mesh(mesh):
    groups, ctx = mesh.devices.shape
    return Mesh(mesh.devices.reshape(groups, ctx // 2, 2), ("groups",) + CTX)


def shifted(block, distance):
    devices = range(lax.axis_size(CTX))
    route = [(i - distance, i) for i in devices if i - distance in devices]
    return lax.ppermute(block, CTX, route)


def ring_order(chips):
    down = [2 * i for i in range(chips // 2)]
    up = [2 * i + 1 for i in reversed(range(chips // 2))]
    return down + up


def short_mixed(padded, short_filter, row_count):
    source = padded.astype(jnp.float32)
    total = short_filter[0] * source[2 : 2 + row_count]
    total = total + short_filter[1] * source[1 : 1 + row_count]
    return total + short_filter[2] * source[0:row_count]


def long_conv(extended, long_filter, group, row_count):
    tap_count = long_filter.shape[1]
    taps = jnp.repeat(long_filter[:, ::-1].T, group, axis=1)[:, None, :]
    source = extended[extended.shape[0] - row_count - tap_count + 1 :]
    conv = lax.conv_general_dilated(
        source[None],
        taps,
        window_strides=(1,),
        padding="VALID",
        dimension_numbers=("NWC", "WIO", "NWC"),
        feature_group_count=source.shape[1],
        preferred_element_type=jnp.float32,
    )
    return conv[0]


def on_device(tokens, projected, short_filter, long_filter, conv_bias, out_weight):
    row_count = tokens.shape[0]
    channels = out_weight.shape[0]
    group = channels // long_filter.shape[0]
    chips = lax.axis_size("chip")
    width = out_weight.shape[1]

    edge_rows = shifted(projected[row_count - 2 :], 1)
    mixed = short_mixed(jnp.concatenate([edge_rows, projected], axis=0), short_filter, row_count)
    gate_rows = mixed[:, :channels]
    carried = (mixed[:, channels : 2 * channels] * mixed[:, 2 * channels :]).astype(jnp.bfloat16)
    halo = shifted(carried[row_count - 128 :], 1)
    conv = long_conv(jnp.concatenate([halo, carried], axis=0), long_filter, group, row_count)
    gated = (gate_rows * (conv + conv_bias * carried.astype(jnp.float32))).astype(jnp.bfloat16)

    chip = lax.axis_index("chip")
    core = lax.axis_index("core")
    order = ring_order(chips)
    where = [0] * chips
    for position, c in enumerate(order):
        where[c] = position
    order_arr = jnp.array(order, jnp.int32)
    position = jnp.array(where, jnp.int32)[chip]
    forward = [(order[i], order[(i + 1) % chips]) for i in range(chips)]
    backward = [(order[(i + 1) % chips], order[i]) for i in range(chips)]

    result = tokens

    def emit(result, piece, owner_chip, owner_core, start, size):
        column = (owner_chip * 2 + owner_core) * width + start
        rows = lax.dynamic_slice_in_dim(tokens, column, size, 1).astype(jnp.float32)
        out = rows + jnp.dot(gated, piece, preferred_element_type=jnp.float32)
        return lax.dynamic_update_slice_in_dim(result, out.astype(jnp.bfloat16), column, 1)

    def emit_both(result, piece, owner_chip, start=0):
        size = piece.shape[1]
        result = emit(result, piece, owner_chip, core, start, size)
        other = lax.ppermute(piece, "core", [(0, 1), (1, 0)])
        return emit(result, other, owner_chip, 1 - core, start, size)

    result = emit_both(result, out_weight, chip)
    ahead = behind = out_weight
    steps = chips // 2
    for step in range(1, steps + 1):
        last = step == steps and chips % 2 == 0
        if last:
            half = width // 2
            ahead = lax.ppermute(ahead[:, :half], "chip", forward)
            behind = lax.ppermute(behind[:, half:], "chip", backward)
            source = order_arr[(position - step) % chips]
            result = emit_both(result, ahead, source, 0)
            result = emit_both(result, behind, source, half)
        else:
            ahead = lax.ppermute(ahead, "chip", forward)
            behind = lax.ppermute(behind, "chip", backward)
            result = emit_both(result, ahead, order_arr[(position - step) % chips])
            if step < steps or chips % 2:
                result = emit_both(result, behind, order_arr[(position + step) % chips])
    return result


def solution(mesh):
    inner = split_mesh(mesh)
    rows = P(("groups",) + CTX, None)
    placed = (rows, rows, P(), P(), P(), P(None, CTX))
    return jax.shard_map(on_device, mesh=inner, in_specs=placed, out_specs=rows, check_vma=False)
```

```python
import jax
import jax.numpy as jnp
from jax import lax
from jax.experimental import pallas as pl
from jax.experimental.pallas import tpu as pltpu
from jax.sharding import Mesh
from jax.sharding import PartitionSpec as P

CTX = ("chip", "core")
BLOCK = 128
LANES = 128


def split_mesh(mesh):
    groups, ctx = mesh.devices.shape
    return Mesh(mesh.devices.reshape(groups, ctx // 2, 2), ("groups",) + CTX)


def shifted(block, distance):
    devices = range(lax.axis_size(CTX))
    route = [(i - distance, i) for i in devices if i - distance in devices]
    return lax.ppermute(block, CTX, route)


def ring_order(chips):
    down = [2 * i for i in range(chips // 2)]
    up = [2 * i + 1 for i in reversed(range(chips // 2))]
    return down + up


def short_mixed(edge, rows, short_filter):
    previous = jnp.concatenate([edge[1:], rows[:-1]], axis=0).astype(jnp.float32)
    before = jnp.concatenate([edge, rows[:-2]], axis=0).astype(jnp.float32)
    total = short_filter[0] * rows.astype(jnp.float32)
    total = total + short_filter[1] * previous
    return total + short_filter[2] * before


def _gate_kernel(fw_ref, bias_ref, halo_ref, carried_ref, gate_ref, out_ref):
    lanes = carried_ref.shape[1]
    per_tile = fw_ref.shape[0]
    group = lanes // per_tile
    blocks = carried_ref.shape[0] // BLOCK
    owner = lax.broadcasted_iota(jnp.int32, (1, lanes), 1) // group
    toeplitz = []
    for i in range(per_tile):
        v = jnp.broadcast_to(fw_ref[i : i + 1, :], (BLOCK, fw_ref.shape[1]))
        rolled = pltpu.roll(v, 0, 1, stride=1, stride_axis=0)
        toeplitz.append(rolled[:, : 2 * BLOCK].astype(jnp.bfloat16))
    bias = bias_ref[...]
    for b in range(blocks):
        before = halo_ref[...] if b == 0 else carried_ref[BLOCK * (b - 1) : BLOCK * b, :]
        current = carried_ref[BLOCK * b : BLOCK * (b + 1), :]
        window = jnp.concatenate([before, current], axis=0)
        acc = jnp.zeros((BLOCK, lanes), jnp.float32)
        for i in range(per_tile):
            masked = jnp.where(owner == i, window, jnp.zeros_like(window))
            acc = acc + jnp.dot(toeplitz[i], masked, preferred_element_type=jnp.float32)
        gate = gate_ref[BLOCK * b : BLOCK * (b + 1), :]
        direct = bias * current.astype(jnp.float32)
        out_ref[BLOCK * b : BLOCK * (b + 1), :] = (gate * (acc + direct)).astype(out_ref.dtype)


def long_conv_gate(halo, carried, gate_rows, long_filter, conv_bias):
    groups, taps = long_filter.shape
    row_count, channels = carried.shape
    per_tile = LANES // (channels // groups)
    fw = jnp.zeros((groups, 3 * BLOCK), jnp.float32)
    fw = fw.at[:, 1 : 1 + taps].set(long_filter[:, ::-1].astype(jnp.float32))
    return pl.pallas_call(
        _gate_kernel,
        grid=(channels // LANES,),
        in_specs=[
            pl.BlockSpec((per_tile, 3 * BLOCK), lambda j: (j, 0)),
            pl.BlockSpec((1, LANES), lambda j: (0, j)),
            pl.BlockSpec((BLOCK, LANES), lambda j: (0, j)),
            pl.BlockSpec((row_count, LANES), lambda j: (0, j)),
            pl.BlockSpec((row_count, LANES), lambda j: (0, j)),
        ],
        out_specs=pl.BlockSpec((row_count, LANES), lambda j: (0, j)),
        out_shape=jax.ShapeDtypeStruct((row_count, channels), jnp.bfloat16),
    )(fw, conv_bias.reshape(1, channels), halo, carried, gate_rows)


def on_device(tokens, projected, short_filter, long_filter, conv_bias, out_weight):
    row_count = tokens.shape[0]
    channels = out_weight.shape[0]
    chips = lax.axis_size("chip")
    width = out_weight.shape[1]

    chip = lax.axis_index("chip")
    core = lax.axis_index("core")
    order = ring_order(chips)
    where = [0] * chips
    for place, c in enumerate(order):
        where[c] = place
    order_arr = jnp.array(order, jnp.int32)
    position = jnp.array(where, jnp.int32)[chip]
    forward = [(order[i], order[(i + 1) % chips]) for i in range(chips)]
    backward = [(order[(i + 1) % chips], order[i]) for i in range(chips)]
    swap = [(0, 1), (1, 0)]

    def with_partner(piece):
        other = lax.ppermute(piece, "core", swap)
        return (piece, other)

    steps = min(chips, 8) // 2
    ahead = behind = out_weight
    arrived = [(chip, 0, with_partner(out_weight))]

    def ring_step(step, ahead, behind):
        if step == steps and chips % 2 == 0:
            half = width // 2
            ahead = lax.ppermute(ahead[:, :half], "chip", forward)
            behind = lax.ppermute(behind[:, half:], "chip", backward)
            source = order_arr[(position - step) % chips]
            got = [(source, 0, with_partner(ahead)), (source, half, with_partner(behind))]
        else:
            ahead = lax.ppermute(ahead, "chip", forward)
            behind = lax.ppermute(behind, "chip", backward)
            got = [(order_arr[(position - step) % chips], 0, with_partner(ahead))]
            if step < steps or chips % 2:
                got.append((order_arr[(position + step) % chips], 0, with_partner(behind)))
        return ahead, behind, got

    ahead, behind, got = ring_step(1, ahead, behind)
    arrived += got

    edge = shifted(projected[row_count - 2 :], 1)
    mixed = short_mixed(edge, projected, short_filter)
    gate_rows = mixed[:, :channels]
    carried = (mixed[:, channels : 2 * channels] * mixed[:, 2 * channels :]).astype(jnp.bfloat16)
    halo = shifted(carried[row_count - BLOCK :], 1)

    carried, gate_rows, ahead, behind = lax.optimization_barrier((carried, gate_rows, ahead, behind))
    if steps >= 2:
        ahead, behind, got = ring_step(2, ahead, behind)
        arrived += got

    gated = long_conv_gate(halo, carried, gate_rows, long_filter, conv_bias)

    if chips > 8:
        weight = lax.all_gather(out_weight, CTX, axis=1, tiled=True)
        branch = jnp.dot(gated, weight, preferred_element_type=jnp.float32)
        return (tokens.astype(jnp.float32) + branch).astype(jnp.bfloat16)

    result = tokens
    done = 0

    def emit(result, owner_chip, start, pieces):
        mine, other = pieces
        size = mine.shape[1]
        both = jnp.concatenate([mine, other], axis=1)
        out = jnp.dot(gated, both, preferred_element_type=jnp.float32)
        for k, half in ((core, out[:, :size]), (1 - core, out[:, size:])):
            column = (owner_chip * 2 + k) * width + start
            rows = lax.dynamic_slice_in_dim(tokens, column, size, 1).astype(jnp.float32)
            piece = (rows + half).astype(jnp.bfloat16)
            result = lax.dynamic_update_slice_in_dim(result, piece, column, 1)
        return result

    for step in range(3, steps + 1):
        gated, ahead, behind = lax.optimization_barrier((gated, ahead, behind))
        ahead, behind, got = ring_step(step, ahead, behind)
        target = len(arrived)
        while done < target - 2:
            result = emit(result, *arrived[done])
            done += 1
        arrived += got
    while done < len(arrived):
        result = emit(result, *arrived[done])
        done += 1
    return result


def solution(mesh):
    inner = split_mesh(mesh)
    rows = P(("groups",) + CTX, None)
    placed = (rows, rows, P(), P(), P(), P(None, CTX))
    return jax.shard_map(on_device, mesh=inner, in_specs=placed, out_specs=rows, check_vma=False)
```

```python
import jax
import jax.numpy as jnp
from jax import lax
from jax.experimental import pallas as pl
from jax.experimental.pallas import tpu as pltpu
from jax.sharding import Mesh
from jax.sharding import PartitionSpec as P

CTX = ("chip", "core")
BLOCK = 128
LANES = 128


def split_mesh(mesh):
    groups, ctx = mesh.devices.shape
    return Mesh(mesh.devices.reshape(groups, ctx // 2, 2), ("groups",) + CTX)


def shifted(block, distance):
    devices = range(lax.axis_size(CTX))
    route = [(i - distance, i) for i in devices if i - distance in devices]
    return lax.ppermute(block, CTX, route)


def ring_order(chips):
    down = [2 * i for i in range(chips // 2)]
    up = [2 * i + 1 for i in reversed(range(chips // 2))]
    return down + up


def short_mixed(edge, rows, short_filter):
    previous = jnp.concatenate([edge[1:], rows[:-1]], axis=0).astype(jnp.float32)
    before = jnp.concatenate([edge, rows[:-2]], axis=0).astype(jnp.float32)
    total = short_filter[0] * rows.astype(jnp.float32)
    total = total + short_filter[1] * previous
    return total + short_filter[2] * before


def _gate_kernel(fw_ref, bias_ref, halo_ref, carried_ref, gate_ref, out_ref):
    lanes = carried_ref.shape[1]
    per_tile = fw_ref.shape[0]
    group = lanes // per_tile
    blocks = carried_ref.shape[0] // BLOCK
    owner = lax.broadcasted_iota(jnp.int32, (1, lanes), 1) // group
    toeplitz = []
    for i in range(per_tile):
        v = jnp.broadcast_to(fw_ref[i : i + 1, :], (BLOCK, fw_ref.shape[1]))
        rolled = pltpu.roll(v, 0, 1, stride=1, stride_axis=0)
        toeplitz.append(rolled[:, : 2 * BLOCK].astype(jnp.bfloat16))
    bias = bias_ref[...]
    for b in range(blocks):
        before = halo_ref[...] if b == 0 else carried_ref[BLOCK * (b - 1) : BLOCK * b, :]
        current = carried_ref[BLOCK * b : BLOCK * (b + 1), :]
        window = jnp.concatenate([before, current], axis=0)
        acc = jnp.zeros((BLOCK, lanes), jnp.float32)
        for i in range(per_tile):
            masked = jnp.where(owner == i, window, jnp.zeros_like(window))
            acc = acc + jnp.dot(toeplitz[i], masked, preferred_element_type=jnp.float32)
        gate = gate_ref[BLOCK * b : BLOCK * (b + 1), :]
        direct = bias * current.astype(jnp.float32)
        out_ref[BLOCK * b : BLOCK * (b + 1), :] = (gate * (acc + direct)).astype(out_ref.dtype)


def long_conv_gate(halo, carried, gate_rows, long_filter, conv_bias):
    groups, taps = long_filter.shape
    row_count, channels = carried.shape
    per_tile = LANES // (channels // groups)
    fw = jnp.pad(long_filter[:, ::-1].astype(jnp.float32), ((0, 0), (1, 3 * BLOCK - 1 - taps)))
    return pl.pallas_call(
        _gate_kernel,
        grid=(channels // LANES,),
        in_specs=[
            pl.BlockSpec((per_tile, 3 * BLOCK), lambda j: (j, 0)),
            pl.BlockSpec((1, LANES), lambda j: (0, j)),
            pl.BlockSpec((BLOCK, LANES), lambda j: (0, j)),
            pl.BlockSpec((row_count, LANES), lambda j: (0, j)),
            pl.BlockSpec((row_count, LANES), lambda j: (0, j)),
        ],
        out_specs=pl.BlockSpec((row_count, LANES), lambda j: (0, j)),
        out_shape=jax.ShapeDtypeStruct((row_count, channels), jnp.bfloat16),
    )(fw, conv_bias.reshape(1, channels), halo, carried, gate_rows)


def ring_place(c, chips):
    return jnp.where(c % 2 == 0, c // 2, chips - 1 - c // 2)


def ring_chip(q, chips):
    return jnp.where(q < chips // 2, 2 * q, 2 * (chips - 1 - q) + 1)


def carried_of(second, carrier):
    return (second * carrier).astype(jnp.bfloat16)


def on_device(tokens, projected, short_filter, long_filter, conv_bias, out_weight):
    row_count = tokens.shape[0]
    channels = out_weight.shape[0]
    chips = lax.axis_size("chip")
    width = out_weight.shape[1]
    ring = chips % 2 == 0 and chips <= 8

    chip = lax.axis_index("chip")
    core = lax.axis_index("core")
    position = ring_place(chip, chips)
    order = ring_order(chips)
    forward = [(order[i], order[(i + 1) % chips]) for i in range(chips)]
    backward = [(order[(i + 1) % chips], order[i]) for i in range(chips)]
    swap = [(0, 1), (1, 0)]
    steps = chips // 2

    weight = jnp.zeros((channels, chips * 2 * width), out_weight.dtype)

    def place(weight, piece, owner_chip, row=0):
        other = lax.ppermute(piece, "core", swap)
        for k, part in ((core, piece), (1 - core, other)):
            weight = lax.dynamic_update_slice(weight, part, (row, (owner_chip * 2 + k) * width))
        return weight

    def ring_step(step, weight, ahead, behind):
        if step == steps:
            half = channels // 2
            ahead = lax.ppermute(ahead[:half], "chip", forward)
            behind = lax.ppermute(behind[half:], "chip", backward)
            source = ring_chip((position - step) % chips, chips)
            weight = place(weight, ahead, source, 0)
            weight = place(weight, behind, source, half)
        else:
            ahead = lax.ppermute(ahead, "chip", forward)
            behind = lax.ppermute(behind, "chip", backward)
            weight = place(weight, ahead, ring_chip((position - step) % chips, chips))
            weight = place(weight, behind, ring_chip((position + step) % chips, chips))
        return weight, ahead, behind

    ahead = behind = out_weight
    if ring:
        weight = place(weight, out_weight, chip)
        weight, ahead, behind = ring_step(1, weight, ahead, behind)

    tail = projected[row_count - BLOCK - 2 :]
    tail_mixed = [
        short_mixed(tail[:2, k * channels : (k + 1) * channels], tail[2:, k * channels : (k + 1) * channels], short_filter[:, k * channels : (k + 1) * channels])
        for k in (1, 2)
    ]
    halo = shifted(carried_of(*tail_mixed), 1)
    edge = shifted(projected[row_count - 2 :], 1)
    mixed = [
        short_mixed(edge[:, k * channels : (k + 1) * channels], projected[:, k * channels : (k + 1) * channels], short_filter[:, k * channels : (k + 1) * channels])
        for k in (0, 1, 2)
    ]
    gate_rows = mixed[0]
    carried = carried_of(mixed[1], mixed[2])

    carried, gate_rows, ahead, behind = lax.optimization_barrier((carried, gate_rows, ahead, behind))
    if ring and steps >= 2:
        weight, ahead, behind = ring_step(2, weight, ahead, behind)

    gated = long_conv_gate(halo, carried, gate_rows, long_filter, conv_bias)

    if ring:
        gated, ahead, behind = lax.optimization_barrier((gated, ahead, behind))
        for step in range(3, steps + 1):
            weight, ahead, behind = ring_step(step, weight, ahead, behind)
    else:
        weight = lax.all_gather(out_weight, CTX, axis=1, tiled=True)
    branch = jnp.dot(gated, weight, preferred_element_type=jnp.float32)
    return (tokens.astype(jnp.float32) + branch).astype(jnp.bfloat16)


def solution(mesh):
    inner = split_mesh(mesh)
    rows = P(("groups",) + CTX, None)
    placed = (rows, rows, P(), P(), P(), P(None, CTX))
    return jax.shard_map(on_device, mesh=inner, in_specs=placed, out_specs=rows, check_vma=False)
```

```python
import jax
import jax.numpy as jnp
from jax import lax
from jax.experimental import pallas as pl
from jax.experimental.pallas import tpu as pltpu
from jax.sharding import Mesh
from jax.sharding import PartitionSpec as P

CTX = ("chip", "core")
BLOCK = 128
LANES = 128


def split_mesh(mesh):
    groups, ctx = mesh.devices.shape
    return Mesh(mesh.devices.reshape(groups, ctx // 2, 2), ("groups",) + CTX)


def shifted(block, distance):
    devices = range(lax.axis_size(CTX))
    route = [(i - distance, i) for i in devices if i - distance in devices]
    return lax.ppermute(block, CTX, route)


def ring_order(chips):
    down = [2 * i for i in range(chips // 2)]
    up = [2 * i + 1 for i in reversed(range(chips // 2))]
    return down + up


def short_mixed(edge, rows, short_filter):
    previous = jnp.concatenate([edge[1:], rows[:-1]], axis=0).astype(jnp.float32)
    before = jnp.concatenate([edge, rows[:-2]], axis=0).astype(jnp.float32)
    total = short_filter[0] * rows.astype(jnp.float32)
    total = total + short_filter[1] * previous
    return total + short_filter[2] * before


def _gate_kernel(fw_ref, bias_ref, sf_ref, edge_ref, halo_ref, gate_ref, second_ref, carrier_ref, out_ref):
    lanes = out_ref.shape[1]
    per_tile = fw_ref.shape[0]
    group = lanes // per_tile
    row_count = out_ref.shape[0]
    blocks = row_count // BLOCK
    row = lax.broadcasted_iota(jnp.int32, (row_count, lanes), 0)

    def mixed(k, ref):
        x = ref[...].astype(jnp.float32)
        edge = edge_ref[k].astype(jnp.float32)
        taps = sf_ref[k]
        previous = jnp.where(row == 0, edge[1:2], pltpu.roll(x, 1, 0))
        before = jnp.where(row == 0, edge[0:1], jnp.where(row == 1, edge[1:2], pltpu.roll(x, 2, 0)))
        total = taps[0:1] * x
        total = total + taps[1:2] * previous
        return total + taps[2:3] * before

    gate_rows = mixed(0, gate_ref)
    carried = (mixed(1, second_ref) * mixed(2, carrier_ref)).astype(jnp.bfloat16)

    owner = lax.broadcasted_iota(jnp.int32, (1, lanes), 1) // group
    toeplitz = []
    for i in range(per_tile):
        v = jnp.broadcast_to(fw_ref[i : i + 1, :], (BLOCK, fw_ref.shape[1]))
        rolled = pltpu.roll(v, 0, 1, stride=1, stride_axis=0)
        toeplitz.append(rolled[:, : 2 * BLOCK].astype(jnp.bfloat16))
    bias = bias_ref[...]
    for b in range(blocks):
        before = halo_ref[...] if b == 0 else carried[BLOCK * (b - 1) : BLOCK * b]
        current = carried[BLOCK * b : BLOCK * (b + 1)]
        window = jnp.concatenate([before, current], axis=0)
        acc = jnp.zeros((BLOCK, lanes), jnp.float32)
        for i in range(per_tile):
            masked = jnp.where(owner == i, window, jnp.zeros_like(window))
            acc = acc + jnp.dot(toeplitz[i], masked, preferred_element_type=jnp.float32)
        gate = gate_rows[BLOCK * b : BLOCK * (b + 1)]
        direct = bias * current.astype(jnp.float32)
        out_ref[BLOCK * b : BLOCK * (b + 1), :] = (gate * (acc + direct)).astype(out_ref.dtype)


def hyena_gate(halo, edge, projected, short_filter, long_filter, conv_bias):
    groups, taps = long_filter.shape
    row_count = projected.shape[0]
    channels = halo.shape[1]
    per_tile = LANES // (channels // groups)
    tiles = channels // LANES
    fw = jnp.pad(long_filter[:, ::-1].astype(jnp.float32), ((0, 0), (1, 3 * BLOCK - 1 - taps)))
    edges = edge.reshape(2, 3, channels).transpose(1, 0, 2)
    filters = short_filter.reshape(3, 3, channels).transpose(1, 0, 2)
    column = lambda k: pl.BlockSpec((row_count, LANES), lambda j: (0, j + k * tiles))
    return pl.pallas_call(
        _gate_kernel,
        grid=(tiles,),
        in_specs=[
            pl.BlockSpec((per_tile, 3 * BLOCK), lambda j: (j, 0)),
            pl.BlockSpec((1, LANES), lambda j: (0, j)),
            pl.BlockSpec((3, 3, LANES), lambda j: (0, 0, j)),
            pl.BlockSpec((3, 2, LANES), lambda j: (0, 0, j)),
            pl.BlockSpec((BLOCK, LANES), lambda j: (0, j)),
            column(0),
            column(1),
            column(2),
        ],
        out_specs=pl.BlockSpec((row_count, LANES), lambda j: (0, j)),
        out_shape=jax.ShapeDtypeStruct((row_count, channels), jnp.bfloat16),
    )(fw, conv_bias.reshape(1, channels), filters, edges, halo, projected, projected, projected)


def ring_place(c, chips):
    return jnp.where(c % 2 == 0, c // 2, chips - 1 - c // 2)


def ring_chip(q, chips):
    return jnp.where(q < chips // 2, 2 * q, 2 * (chips - 1 - q) + 1)


def carried_of(second, carrier):
    return (second * carrier).astype(jnp.bfloat16)


def on_device(tokens, projected, short_filter, long_filter, conv_bias, out_weight):
    row_count = tokens.shape[0]
    channels = out_weight.shape[0]
    chips = lax.axis_size("chip")
    width = out_weight.shape[1]
    ring = chips % 2 == 0 and chips <= 8

    chip = lax.axis_index("chip")
    core = lax.axis_index("core")
    position = ring_place(chip, chips)
    order = ring_order(chips)
    forward = [(order[i], order[(i + 1) % chips]) for i in range(chips)]
    backward = [(order[(i + 1) % chips], order[i]) for i in range(chips)]
    swap = [(0, 1), (1, 0)]
    steps = chips // 2

    weight = jnp.zeros((channels, chips * 2 * width), out_weight.dtype)

    def place(weight, piece, owner_chip, row=0):
        other = lax.ppermute(piece, "core", swap)
        for k, part in ((core, piece), (1 - core, other)):
            weight = lax.dynamic_update_slice(weight, part, (row, (owner_chip * 2 + k) * width))
        return weight

    def ring_step(step, weight, ahead, behind):
        if step == steps:
            half = channels // 2
            ahead = lax.ppermute(ahead[:half], "chip", forward)
            behind = lax.ppermute(behind[half:], "chip", backward)
            source = ring_chip((position - step) % chips, chips)
            weight = place(weight, ahead, source, 0)
            weight = place(weight, behind, source, half)
        else:
            ahead = lax.ppermute(ahead, "chip", forward)
            behind = lax.ppermute(behind, "chip", backward)
            weight = place(weight, ahead, ring_chip((position - step) % chips, chips))
            weight = place(weight, behind, ring_chip((position + step) % chips, chips))
        return weight, ahead, behind

    ahead = behind = out_weight
    if ring:
        weight = place(weight, out_weight, chip)
        weight, ahead, behind = ring_step(1, weight, ahead, behind)

    tail = projected[row_count - BLOCK - 2 :]
    tail_mixed = [
        short_mixed(tail[:2, k * channels : (k + 1) * channels], tail[2:, k * channels : (k + 1) * channels], short_filter[:, k * channels : (k + 1) * channels])
        for k in (1, 2)
    ]
    halo = shifted(carried_of(*tail_mixed), 1)
    edge = shifted(projected[row_count - 2 :], 1)
    halo, edge, ahead, behind = lax.optimization_barrier((halo, edge, ahead, behind))
    if ring and steps >= 2:
        weight, ahead, behind = ring_step(2, weight, ahead, behind)

    gated = hyena_gate(halo, edge, projected, short_filter, long_filter, conv_bias)

    if ring:
        gated, ahead, behind = lax.optimization_barrier((gated, ahead, behind))
        for step in range(3, steps + 1):
            weight, ahead, behind = ring_step(step, weight, ahead, behind)
    else:
        weight = lax.all_gather(out_weight, CTX, axis=1, tiled=True)
    branch = jnp.dot(gated, weight, preferred_element_type=jnp.float32)
    return (tokens.astype(jnp.float32) + branch).astype(jnp.bfloat16)


def solution(mesh):
    inner = split_mesh(mesh)
    rows = P(("groups",) + CTX, None)
    placed = (rows, rows, P(), P(), P(), P(None, CTX))
    return jax.shard_map(on_device, mesh=inner, in_specs=placed, out_specs=rows, check_vma=False)
```

```python
import jax
import jax.numpy as jnp
from jax import lax
from jax.experimental import pallas as pl
from jax.experimental.pallas import tpu as pltpu
from jax.sharding import Mesh
from jax.sharding import PartitionSpec as P

CTX = ("chip", "core")
BLOCK = 128
LANES = 128


def split_mesh(mesh):
    groups, ctx = mesh.devices.shape
    return Mesh(mesh.devices.reshape(groups, ctx // 2, 2), ("groups",) + CTX)


def shifted(block, distance):
    devices = range(lax.axis_size(CTX))
    route = [(i - distance, i) for i in devices if i - distance in devices]
    return lax.ppermute(block, CTX, route)


def ring_order(chips):
    down = [2 * i for i in range(chips // 2)]
    up = [2 * i + 1 for i in reversed(range(chips // 2))]
    return down + up


def short_mixed(edge, rows, short_filter):
    previous = jnp.concatenate([edge[1:], rows[:-1]], axis=0).astype(jnp.float32)
    before = jnp.concatenate([edge, rows[:-2]], axis=0).astype(jnp.float32)
    total = short_filter[0] * rows.astype(jnp.float32)
    total = total + short_filter[1] * previous
    return total + short_filter[2] * before


def _gate_kernel(fw_ref, bias_ref, sf_ref, edge_ref, halo_ref, gate_ref, second_ref, carrier_ref, out_ref):
    lanes = out_ref.shape[1]
    per_tile = fw_ref.shape[0]
    group = lanes // per_tile
    row_count = out_ref.shape[0]
    blocks = row_count // BLOCK
    row = lax.broadcasted_iota(jnp.int32, (row_count, lanes), 0)

    def mixed(k, ref):
        x = ref[...].astype(jnp.float32)
        edge = edge_ref[k].astype(jnp.float32)
        taps = sf_ref[k]
        previous = jnp.where(row == 0, edge[1:2], pltpu.roll(x, 1, 0))
        before = jnp.where(row == 0, edge[0:1], jnp.where(row == 1, edge[1:2], pltpu.roll(x, 2, 0)))
        total = taps[0:1] * x
        total = total + taps[1:2] * previous
        return total + taps[2:3] * before

    gate_rows = mixed(0, gate_ref)
    carried = (mixed(1, second_ref) * mixed(2, carrier_ref)).astype(jnp.bfloat16)

    owner = lax.broadcasted_iota(jnp.int32, (1, lanes), 1) // group
    toeplitz = []
    for i in range(per_tile):
        v = jnp.broadcast_to(fw_ref[i : i + 1, :], (BLOCK, fw_ref.shape[1]))
        rolled = pltpu.roll(v, 0, 1, stride=1, stride_axis=0)
        toeplitz.append(rolled[:, : 2 * BLOCK].astype(jnp.bfloat16))
    bias = bias_ref[...]
    for b in range(blocks):
        before = halo_ref[...] if b == 0 else carried[BLOCK * (b - 1) : BLOCK * b]
        current = carried[BLOCK * b : BLOCK * (b + 1)]
        window = jnp.concatenate([before, current], axis=0)
        acc = jnp.zeros((BLOCK, lanes), jnp.float32)
        for i in range(per_tile):
            masked = jnp.where(owner == i, window, jnp.zeros_like(window))
            acc = acc + jnp.dot(toeplitz[i], masked, preferred_element_type=jnp.float32)
        gate = gate_rows[BLOCK * b : BLOCK * (b + 1)]
        direct = bias * current.astype(jnp.float32)
        out_ref[BLOCK * b : BLOCK * (b + 1), :] = (gate * (acc + direct)).astype(out_ref.dtype)


def hyena_gate(halo, edge, projected, short_filter, long_filter, conv_bias, part, parts):
    groups, taps = long_filter.shape
    row_count = projected.shape[0]
    channels = halo.shape[1]
    per_tile = LANES // (channels // groups)
    tiles = channels // LANES
    share = tiles // parts
    first = part * share
    fw = jnp.pad(long_filter[:, ::-1].astype(jnp.float32), ((0, 0), (1, 3 * BLOCK - 1 - taps)))
    edges = edge.reshape(2, 3, channels).transpose(1, 0, 2)
    filters = short_filter.reshape(3, 3, channels).transpose(1, 0, 2)
    column = lambda k: pl.BlockSpec((row_count, LANES), lambda j: (0, first + j + k * tiles))
    return pl.pallas_call(
        _gate_kernel,
        grid=(share,),
        in_specs=[
            pl.BlockSpec((per_tile, 3 * BLOCK), lambda j: (first + j, 0)),
            pl.BlockSpec((1, LANES), lambda j: (0, first + j)),
            pl.BlockSpec((3, 3, LANES), lambda j: (0, 0, first + j)),
            pl.BlockSpec((3, 2, LANES), lambda j: (0, 0, first + j)),
            pl.BlockSpec((BLOCK, LANES), lambda j: (0, first + j)),
            column(0),
            column(1),
            column(2),
        ],
        out_specs=pl.BlockSpec((row_count, LANES), lambda j: (0, j)),
        out_shape=jax.ShapeDtypeStruct((row_count, share * LANES), jnp.bfloat16),
    )(fw, conv_bias.reshape(1, channels), filters, edges, halo, projected, projected, projected)


def ring_place(c, chips):
    return jnp.where(c % 2 == 0, c // 2, chips - 1 - c // 2)


def ring_chip(q, chips):
    return jnp.where(q < chips // 2, 2 * q, 2 * (chips - 1 - q) + 1)


def carried_of(second, carrier):
    return (second * carrier).astype(jnp.bfloat16)


def on_device(tokens, projected, short_filter, long_filter, conv_bias, out_weight):
    row_count = tokens.shape[0]
    channels = out_weight.shape[0]
    chips = lax.axis_size("chip")
    width = out_weight.shape[1]
    ring = chips % 2 == 0 and chips <= 8

    chip = lax.axis_index("chip")
    core = lax.axis_index("core")
    position = ring_place(chip, chips)
    order = ring_order(chips)
    forward = [(order[i], order[(i + 1) % chips]) for i in range(chips)]
    backward = [(order[(i + 1) % chips], order[i]) for i in range(chips)]
    swap = [(0, 1), (1, 0)]
    steps = chips // 2

    weight = jnp.zeros((channels, chips * 2 * width), out_weight.dtype)

    def place(weight, piece, owner_chip, row=0):
        other = lax.ppermute(piece, "core", swap)
        for k, part in ((core, piece), (1 - core, other)):
            weight = lax.dynamic_update_slice(weight, part, (row, (owner_chip * 2 + k) * width))
        return weight

    def ring_step(step, weight, ahead, behind):
        if step == steps:
            half = channels // 2
            ahead = lax.ppermute(ahead[:half], "chip", forward)
            behind = lax.ppermute(behind[half:], "chip", backward)
            source = ring_chip((position - step) % chips, chips)
            weight = place(weight, ahead, source, 0)
            weight = place(weight, behind, source, half)
        else:
            ahead = lax.ppermute(ahead, "chip", forward)
            behind = lax.ppermute(behind, "chip", backward)
            weight = place(weight, ahead, ring_chip((position - step) % chips, chips))
            weight = place(weight, behind, ring_chip((position + step) % chips, chips))
        return weight, ahead, behind

    ahead = behind = out_weight
    if ring:
        weight = place(weight, out_weight, chip)
        weight, ahead, behind = ring_step(1, weight, ahead, behind)

    tail = projected[row_count - BLOCK - 2 :]
    tail_mixed = [
        short_mixed(tail[:2, k * channels : (k + 1) * channels], tail[2:, k * channels : (k + 1) * channels], short_filter[:, k * channels : (k + 1) * channels])
        for k in (1, 2)
    ]
    halo = shifted(carried_of(*tail_mixed), 1)
    edge = shifted(projected[row_count - 2 :], 1)
    halo, edge, ahead, behind = lax.optimization_barrier((halo, edge, ahead, behind))
    if ring and steps >= 2:
        weight, ahead, behind = ring_step(2, weight, ahead, behind)

    inputs = (halo, edge, projected, short_filter, long_filter, conv_bias)
    first = hyena_gate(*inputs, 0, 2)
    if ring:
        first, ahead, behind, inputs = lax.optimization_barrier((first, ahead, behind, inputs))
        if steps >= 3:
            weight, ahead, behind = ring_step(3, weight, ahead, behind)
    second = hyena_gate(*inputs, 1, 2)
    if ring:
        second, ahead, behind = lax.optimization_barrier((second, ahead, behind))
        for step in range(4, steps + 1):
            weight, ahead, behind = ring_step(step, weight, ahead, behind)
    else:
        weight = lax.all_gather(out_weight, CTX, axis=1, tiled=True)
    gated = jnp.concatenate([first, second], axis=1)
    branch = jnp.dot(gated, weight, preferred_element_type=jnp.float32)
    return (tokens.astype(jnp.float32) + branch).astype(jnp.bfloat16)


def solution(mesh):
    inner = split_mesh(mesh)
    rows = P(("groups",) + CTX, None)
    placed = (rows, rows, P(), P(), P(), P(None, CTX))
    return jax.shard_map(on_device, mesh=inner, in_specs=placed, out_specs=rows, check_vma=False)
```

```python
import jax
import jax.numpy as jnp
from jax import lax
from jax.experimental import pallas as pl
from jax.experimental.pallas import tpu as pltpu
from jax.sharding import Mesh
from jax.sharding import PartitionSpec as P

CTX = ("chip", "core")
BLOCK = 128
LANES = 128


def split_mesh(mesh):
    groups, ctx = mesh.devices.shape
    return Mesh(mesh.devices.reshape(groups, ctx // 2, 2), ("groups",) + CTX)


def shifted(block, distance):
    devices = range(lax.axis_size(CTX))
    route = [(i - distance, i) for i in devices if i - distance in devices]
    return lax.ppermute(block, CTX, route)


def ring_order(chips):
    down = [2 * i for i in range(chips // 2)]
    up = [2 * i + 1 for i in reversed(range(chips // 2))]
    return down + up


def short_mixed(edge, rows, short_filter):
    previous = jnp.concatenate([edge[1:], rows[:-1]], axis=0).astype(jnp.float32)
    before = jnp.concatenate([edge, rows[:-2]], axis=0).astype(jnp.float32)
    total = short_filter[0] * rows.astype(jnp.float32)
    total = total + short_filter[1] * previous
    return total + short_filter[2] * before


def _gate_kernel(fw_ref, bias_ref, sf_ref, edge_ref, halo_ref, gate_ref, second_ref, carrier_ref, out_ref):
    lanes = out_ref.shape[1]
    per_tile = fw_ref.shape[0]
    group = lanes // per_tile
    row_count = out_ref.shape[0]
    blocks = row_count // BLOCK
    row = lax.broadcasted_iota(jnp.int32, (row_count, lanes), 0)

    def mixed(k, ref):
        x = ref[...].astype(jnp.float32)
        edge = edge_ref[k].astype(jnp.float32)
        taps = sf_ref[k]
        previous = jnp.where(row == 0, edge[1:2], pltpu.roll(x, 1, 0))
        before = jnp.where(row == 0, edge[0:1], jnp.where(row == 1, edge[1:2], pltpu.roll(x, 2, 0)))
        total = taps[0:1] * x
        total = total + taps[1:2] * previous
        return total + taps[2:3] * before

    gate_rows = mixed(0, gate_ref)
    carried = (mixed(1, second_ref) * mixed(2, carrier_ref)).astype(jnp.bfloat16)

    owner = lax.broadcasted_iota(jnp.int32, (1, lanes), 1) // group
    toeplitz = []
    for i in range(per_tile):
        v = jnp.broadcast_to(fw_ref[i : i + 1, :], (BLOCK, fw_ref.shape[1]))
        rolled = pltpu.roll(v, 0, 1, stride=1, stride_axis=0)
        toeplitz.append(rolled[:, : 2 * BLOCK].astype(jnp.bfloat16))
    bias = bias_ref[...]
    for b in range(blocks):
        before = halo_ref[...] if b == 0 else carried[BLOCK * (b - 1) : BLOCK * b]
        current = carried[BLOCK * b : BLOCK * (b + 1)]
        window = jnp.concatenate([before, current], axis=0)
        acc = jnp.zeros((BLOCK, lanes), jnp.float32)
        for i in range(per_tile):
            masked = jnp.where(owner == i, window, jnp.zeros_like(window))
            acc = acc + jnp.dot(toeplitz[i], masked, preferred_element_type=jnp.float32)
        gate = gate_rows[BLOCK * b : BLOCK * (b + 1)]
        direct = bias * current.astype(jnp.float32)
        out_ref[BLOCK * b : BLOCK * (b + 1), :] = (gate * (acc + direct)).astype(out_ref.dtype)


def hyena_gate(halo, edge, projected, short_filter, long_filter, conv_bias, part, parts):
    groups, taps = long_filter.shape
    row_count = projected.shape[0]
    channels = halo.shape[1]
    per_tile = LANES // (channels // groups)
    tiles = channels // LANES
    share = tiles // parts
    first = part * share
    fw = jnp.pad(long_filter[:, ::-1].astype(jnp.float32), ((0, 0), (1, 3 * BLOCK - 1 - taps)))
    edges = edge.reshape(2, 3, channels).transpose(1, 0, 2)
    filters = short_filter.reshape(3, 3, channels).transpose(1, 0, 2)
    column = lambda k: pl.BlockSpec((row_count, LANES), lambda j: (0, first + j + k * tiles))
    return pl.pallas_call(
        _gate_kernel,
        grid=(share,),
        in_specs=[
            pl.BlockSpec((per_tile, 3 * BLOCK), lambda j: (first + j, 0)),
            pl.BlockSpec((1, LANES), lambda j: (0, first + j)),
            pl.BlockSpec((3, 3, LANES), lambda j: (0, 0, first + j)),
            pl.BlockSpec((3, 2, LANES), lambda j: (0, 0, first + j)),
            pl.BlockSpec((BLOCK, LANES), lambda j: (0, first + j)),
            column(0),
            column(1),
            column(2),
        ],
        out_specs=pl.BlockSpec((row_count, LANES), lambda j: (0, j)),
        out_shape=jax.ShapeDtypeStruct((row_count, share * LANES), jnp.bfloat16),
    )(fw, conv_bias.reshape(1, channels), filters, edges, halo, projected, projected, projected)


def ring_place(c, chips):
    return jnp.where(c % 2 == 0, c // 2, chips - 1 - c // 2)


def ring_chip(q, chips):
    return jnp.where(q < chips // 2, 2 * q, 2 * (chips - 1 - q) + 1)


def carried_of(second, carrier):
    return (second * carrier).astype(jnp.bfloat16)


def on_device(tokens, projected, short_filter, long_filter, conv_bias, out_weight):
    row_count = tokens.shape[0]
    channels = out_weight.shape[0]
    chips = lax.axis_size("chip")
    width = out_weight.shape[1]
    ring = chips % 2 == 0 and chips <= 8

    chip = lax.axis_index("chip")
    core = lax.axis_index("core")
    position = ring_place(chip, chips)
    order = ring_order(chips)
    forward = [(order[i], order[(i + 1) % chips]) for i in range(chips)]
    backward = [(order[(i + 1) % chips], order[i]) for i in range(chips)]
    swap = [(0, 1), (1, 0)]
    steps = chips // 2

    weight = jnp.zeros((channels, chips * 2 * width), out_weight.dtype)

    def put(weight, piece, other, owner_chip, row=0):
        for k, part in ((core, piece), (1 - core, other)):
            weight = lax.dynamic_update_slice(weight, part, (row, (owner_chip * 2 + k) * width))
        return weight

    def place(weight, piece, owner_chip, row=0):
        return put(weight, piece, lax.ppermute(piece, "core", swap), owner_chip, row)

    def ring_step(step, weight, ahead, behind):
        if step == steps:
            half = channels // 2
            ahead = lax.ppermute(ahead[:half], "chip", forward)
            behind = lax.ppermute(behind[half:], "chip", backward)
            sources = (ring_chip((position - step) % chips, chips),) * 2
            rows = (0, half)
        else:
            ahead = lax.ppermute(ahead, "chip", forward)
            behind = lax.ppermute(behind, "chip", backward)
            sources = (ring_chip((position - step) % chips, chips), ring_chip((position + step) % chips, chips))
            rows = (0, 0)
        others = lax.ppermute(jnp.stack([ahead, behind]), "core", swap)
        weight = put(weight, ahead, others[0], sources[0], rows[0])
        weight = put(weight, behind, others[1], sources[1], rows[1])
        return weight, ahead, behind

    ahead = behind = out_weight
    if ring:
        weight = place(weight, out_weight, chip)
        weight, ahead, behind = ring_step(1, weight, ahead, behind)

    tail = projected[row_count - BLOCK - 2 :]
    tail_mixed = [
        short_mixed(tail[:2, k * channels : (k + 1) * channels], tail[2:, k * channels : (k + 1) * channels], short_filter[:, k * channels : (k + 1) * channels])
        for k in (1, 2)
    ]
    halo = shifted(carried_of(*tail_mixed), 1)
    edge = shifted(projected[row_count - 2 :], 1)
    halo, edge, ahead, behind = lax.optimization_barrier((halo, edge, ahead, behind))
    if ring and steps >= 2:
        weight, ahead, behind = ring_step(2, weight, ahead, behind)

    inputs = (halo, edge, projected, short_filter, long_filter, conv_bias)
    first = hyena_gate(*inputs, 0, 2)
    if ring:
        first, ahead, behind, inputs = lax.optimization_barrier((first, ahead, behind, inputs))
        if steps >= 3:
            weight, ahead, behind = ring_step(3, weight, ahead, behind)
    second = hyena_gate(*inputs, 1, 2)
    if ring:
        second, ahead, behind = lax.optimization_barrier((second, ahead, behind))
        for step in range(4, steps + 1):
            weight, ahead, behind = ring_step(step, weight, ahead, behind)
    else:
        weight = lax.all_gather(out_weight, CTX, axis=1, tiled=True)
    gated = jnp.concatenate([first, second], axis=1)
    branch = jnp.dot(gated, weight, preferred_element_type=jnp.float32)
    return (tokens.astype(jnp.float32) + branch).astype(jnp.bfloat16)


def solution(mesh):
    inner = split_mesh(mesh)
    rows = P(("groups",) + CTX, None)
    placed = (rows, rows, P(), P(), P(), P(None, CTX))
    return jax.shard_map(on_device, mesh=inner, in_specs=placed, out_specs=rows, check_vma=False)
```

```python
import functools

import jax
import jax.numpy as jnp
from jax import lax
from jax.experimental import pallas as pl
from jax.experimental.pallas import tpu as pltpu
from jax.sharding import Mesh
from jax.sharding import PartitionSpec as P

CTX = ("chip", "core")
BLOCK = 128
LANES = 128


def split_mesh(mesh):
    groups, ctx = mesh.devices.shape
    return Mesh(mesh.devices.reshape(groups, ctx // 2, 2), ("groups",) + CTX)


def shifted(block, distance):
    devices = range(lax.axis_size(CTX))
    route = [(i - distance, i) for i in devices if i - distance in devices]
    return lax.ppermute(block, CTX, route)


def ring_order(chips):
    down = [2 * i for i in range(chips // 2)]
    up = [2 * i + 1 for i in reversed(range(chips // 2))]
    return down + up


def short_mixed(edge, rows, short_filter):
    previous = jnp.concatenate([edge[1:], rows[:-1]], axis=0).astype(jnp.float32)
    before = jnp.concatenate([edge, rows[:-2]], axis=0).astype(jnp.float32)
    total = short_filter[0] * rows.astype(jnp.float32)
    total = total + short_filter[1] * previous
    return total + short_filter[2] * before


def _gate_kernel(fw_ref, bias_ref, sf_ref, edge_ref, halo_ref, gate_ref, second_ref, carrier_ref, out_ref):
    lanes = out_ref.shape[1]
    per_tile = fw_ref.shape[0]
    group = lanes // per_tile
    row_count = out_ref.shape[0]
    blocks = row_count // BLOCK
    row = lax.broadcasted_iota(jnp.int32, (row_count, lanes), 0)

    def mixed(k, ref):
        x = ref[...].astype(jnp.float32)
        edge = edge_ref[k].astype(jnp.float32)
        taps = sf_ref[k]
        previous = jnp.where(row == 0, edge[1:2], pltpu.roll(x, 1, 0))
        before = jnp.where(row == 0, edge[0:1], jnp.where(row == 1, edge[1:2], pltpu.roll(x, 2, 0)))
        total = taps[0:1] * x
        total = total + taps[1:2] * previous
        return total + taps[2:3] * before

    gate_rows = mixed(0, gate_ref)
    carried = (mixed(1, second_ref) * mixed(2, carrier_ref)).astype(jnp.bfloat16)

    owner = lax.broadcasted_iota(jnp.int32, (1, lanes), 1) // group
    toeplitz = []
    for i in range(per_tile):
        v = jnp.broadcast_to(fw_ref[i : i + 1, :], (BLOCK, fw_ref.shape[1]))
        rolled = pltpu.roll(v, 0, 1, stride=1, stride_axis=0)
        toeplitz.append(rolled[:, : 2 * BLOCK].astype(jnp.bfloat16))
    bias = bias_ref[...]
    for b in range(blocks):
        before = halo_ref[...] if b == 0 else carried[BLOCK * (b - 1) : BLOCK * b]
        current = carried[BLOCK * b : BLOCK * (b + 1)]
        window = jnp.concatenate([before, current], axis=0)
        acc = jnp.zeros((BLOCK, lanes), jnp.float32)
        for i in range(per_tile):
            masked = jnp.where(owner == i, window, jnp.zeros_like(window))
            acc = acc + jnp.dot(toeplitz[i], masked, preferred_element_type=jnp.float32)
        gate = gate_rows[BLOCK * b : BLOCK * (b + 1)]
        direct = bias * current.astype(jnp.float32)
        out_ref[BLOCK * b : BLOCK * (b + 1), :] = (gate * (acc + direct)).astype(out_ref.dtype)


def hyena_gate(halo, edge, projected, short_filter, long_filter, conv_bias, part, parts):
    groups, taps = long_filter.shape
    row_count = projected.shape[0]
    channels = halo.shape[1]
    per_tile = LANES // (channels // groups)
    tiles = channels // LANES
    share = tiles // parts
    first = part * share
    fw = jnp.pad(long_filter[:, ::-1].astype(jnp.float32), ((0, 0), (1, 3 * BLOCK - 1 - taps)))
    edges = edge.reshape(2, 3, channels).transpose(1, 0, 2)
    filters = short_filter.reshape(3, 3, channels).transpose(1, 0, 2)
    column = lambda k: pl.BlockSpec((row_count, LANES), lambda j: (0, first + j + k * tiles))
    return pl.pallas_call(
        _gate_kernel,
        grid=(share,),
        in_specs=[
            pl.BlockSpec((per_tile, 3 * BLOCK), lambda j: (first + j, 0)),
            pl.BlockSpec((1, LANES), lambda j: (0, first + j)),
            pl.BlockSpec((3, 3, LANES), lambda j: (0, 0, first + j)),
            pl.BlockSpec((3, 2, LANES), lambda j: (0, 0, first + j)),
            pl.BlockSpec((BLOCK, LANES), lambda j: (0, first + j)),
            column(0),
            column(1),
            column(2),
        ],
        out_specs=pl.BlockSpec((row_count, LANES), lambda j: (0, j)),
        out_shape=jax.ShapeDtypeStruct((row_count, share * LANES), jnp.bfloat16),
    )(fw, conv_bias.reshape(1, channels), filters, edges, halo, projected, projected, projected)


def _project_kernel(layout, carry, cols_ref, gated_ref, tokens_ref, *refs):
    count = sum(len(parts) for parts in layout)
    prev = refs[:carry]
    pieces = refs[carry : carry + count]
    out_ref, wbuf, sems = refs[carry + count :]
    if carry:
        out_ref[...] = prev[0][...]
    copies = []
    index = 0
    for slot, parts in enumerate(layout):
        group = []
        for part, (row, rows) in enumerate(parts):
            target = wbuf.at[slot % 2, pl.ds(row, rows)]
            group.append(pltpu.make_async_copy(pieces[index], target, sems.at[slot % 2, part]))
            index += 1
        copies.append(group)
    for c in copies[0]:
        c.start()
    width = wbuf.shape[2]
    for slot in range(len(layout)):
        for c in copies[slot]:
            c.wait()
        if slot + 1 < len(layout):
            for c in copies[slot + 1]:
                c.start()
        column = pl.multiple_of(cols_ref[slot] * width, width)
        acc = jnp.dot(gated_ref[...], wbuf[slot % 2], preferred_element_type=jnp.float32)
        rows = tokens_ref[:, pl.ds(column, width)].astype(jnp.float32)
        out_ref[:, pl.ds(column, width)] = (rows + acc).astype(out_ref.dtype)


def project(gated, tokens, slots, previous=None):
    layout = tuple(tuple((row, piece.shape[0]) for piece, row in parts) for _, parts in slots)
    cols = jnp.stack([jnp.asarray(c, jnp.int32) for c, _ in slots])
    pieces = [piece for _, parts in slots for piece, _ in parts]
    carry = 0 if previous is None else 1
    channels, width = gated.shape[1], pieces[0].shape[1]
    full = lambda i, cols: (0, 0)
    in_specs = [pl.BlockSpec(gated.shape, full), pl.BlockSpec(tokens.shape, full)]
    in_specs += [pl.BlockSpec(tokens.shape, full)] * carry
    in_specs += [pl.BlockSpec(memory_space=pl.ANY)] * len(pieces)
    operands = [gated, tokens] + ([previous] if carry else []) + pieces
    return pl.pallas_call(
        functools.partial(_project_kernel, layout, carry),
        grid_spec=pltpu.PrefetchScalarGridSpec(
            num_scalar_prefetch=1,
            grid=(1,),
            in_specs=in_specs,
            out_specs=pl.BlockSpec(tokens.shape, full),
            scratch_shapes=[
                pltpu.VMEM((2, channels, width), pieces[0].dtype),
                pltpu.SemaphoreType.DMA((2, 2)),
            ],
        ),
        out_shape=jax.ShapeDtypeStruct(tokens.shape, tokens.dtype),
        input_output_aliases={3: 0} if carry else {},
        compiler_params=pltpu.CompilerParams(vmem_limit_bytes=48 * 1024 * 1024),
    )(cols, *operands)


def ring_place(c, chips):
    return jnp.where(c % 2 == 0, c // 2, chips - 1 - c // 2)


def ring_chip(q, chips):
    return jnp.where(q < chips // 2, 2 * q, 2 * (chips - 1 - q) + 1)


def carried_of(second, carrier):
    return (second * carrier).astype(jnp.bfloat16)


def on_device(tokens, projected, short_filter, long_filter, conv_bias, out_weight):
    row_count = tokens.shape[0]
    channels = out_weight.shape[0]
    chips = lax.axis_size("chip")
    ring = chips % 2 == 0 and chips <= 8 and out_weight.shape[1] == LANES

    chip = lax.axis_index("chip")
    core = lax.axis_index("core")
    position = ring_place(chip, chips)
    order = ring_order(chips)
    forward = [(order[i], order[(i + 1) % chips]) for i in range(chips)]
    backward = [(order[(i + 1) % chips], order[i]) for i in range(chips)]
    swap = [(0, 1), (1, 0)]
    steps = chips // 2
    slots = []

    def add(piece, owner_chip):
        other = lax.ppermute(piece, "core", swap)
        slots.append((owner_chip * 2 + core, [(piece, 0)]))
        slots.append((owner_chip * 2 + 1 - core, [(other, 0)]))

    def ring_step(step, ahead, behind):
        if step == steps:
            half = channels // 2
            ahead = lax.ppermute(ahead[:half], "chip", forward)
            behind = lax.ppermute(behind[half:], "chip", backward)
            source = ring_chip((position - step) % chips, chips)
            top, bottom = lax.ppermute(ahead, "core", swap), lax.ppermute(behind, "core", swap)
            slots.append((source * 2 + core, [(ahead, 0), (behind, half)]))
            slots.append((source * 2 + 1 - core, [(top, 0), (bottom, half)]))
        else:
            ahead = lax.ppermute(ahead, "chip", forward)
            behind = lax.ppermute(behind, "chip", backward)
            add(ahead, ring_chip((position - step) % chips, chips))
            add(behind, ring_chip((position + step) % chips, chips))
        return ahead, behind

    ahead = behind = out_weight
    if ring:
        add(out_weight, chip)
        ahead, behind = ring_step(1, ahead, behind)

    tail = projected[row_count - BLOCK - 2 :]
    tail_mixed = [
        short_mixed(tail[:2, k * channels : (k + 1) * channels], tail[2:, k * channels : (k + 1) * channels], short_filter[:, k * channels : (k + 1) * channels])
        for k in (1, 2)
    ]
    halo = shifted(carried_of(*tail_mixed), 1)
    edge = shifted(projected[row_count - 2 :], 1)
    halo, edge, ahead, behind = lax.optimization_barrier((halo, edge, ahead, behind))
    if ring and steps >= 2:
        ahead, behind = ring_step(2, ahead, behind)

    inputs = (halo, edge, projected, short_filter, long_filter, conv_bias)
    first = hyena_gate(*inputs, 0, 2)
    if ring:
        first, ahead, behind, inputs = lax.optimization_barrier((first, ahead, behind, inputs))
        if steps >= 3:
            ahead, behind = ring_step(3, ahead, behind)
    second = hyena_gate(*inputs, 1, 2)
    gated = jnp.concatenate([first, second], axis=1)
    if not ring:
        weight = lax.all_gather(out_weight, CTX, axis=1, tiled=True)
        branch = jnp.dot(gated, weight, preferred_element_type=jnp.float32)
        return (tokens.astype(jnp.float32) + branch).astype(jnp.bfloat16)
    gated, ahead, behind = lax.optimization_barrier((gated, ahead, behind))
    early = len(slots)
    for step in range(4, steps + 1):
        ahead, behind = ring_step(step, ahead, behind)
    result = project(gated, tokens, slots[:early])
    if len(slots) > early:
        result = project(gated, tokens, slots[early:], result)
    return result


def solution(mesh):
    inner = split_mesh(mesh)
    rows = P(("groups",) + CTX, None)
    placed = (rows, rows, P(), P(), P(), P(None, CTX))
    return jax.shard_map(on_device, mesh=inner, in_specs=placed, out_specs=rows, check_vma=False)
```

```python
import jax
import jax.numpy as jnp
from jax import lax
from jax.experimental import pallas as pl
from jax.experimental.pallas import tpu as pltpu
from jax.sharding import Mesh
from jax.sharding import PartitionSpec as P

CTX = ("chip", "core")
BLOCK = 128
LANES = 128


def split_mesh(mesh):
    groups, ctx = mesh.devices.shape
    return Mesh(mesh.devices.reshape(groups, ctx // 2, 2), ("groups",) + CTX)


def shifted(block, distance):
    devices = range(lax.axis_size(CTX))
    route = [(i - distance, i) for i in devices if i - distance in devices]
    return lax.ppermute(block, CTX, route)


def ring_order(chips):
    down = [2 * i for i in range(chips // 2)]
    up = [2 * i + 1 for i in reversed(range(chips // 2))]
    return down + up


def short_mixed(edge, rows, short_filter):
    previous = jnp.concatenate([edge[1:], rows[:-1]], axis=0).astype(jnp.float32)
    before = jnp.concatenate([edge, rows[:-2]], axis=0).astype(jnp.float32)
    total = short_filter[0] * rows.astype(jnp.float32)
    total = total + short_filter[1] * previous
    return total + short_filter[2] * before


def _gate_kernel(fw_ref, bias_ref, sf_ref, edge_ref, halo_ref, gate_ref, second_ref, carrier_ref, out_ref):
    lanes = out_ref.shape[1]
    per_tile = fw_ref.shape[0]
    group = lanes // per_tile
    row_count = out_ref.shape[0]
    blocks = row_count // BLOCK
    row = lax.broadcasted_iota(jnp.int32, (row_count, lanes), 0)

    def mixed(k, ref):
        x = ref[...].astype(jnp.float32)
        edge = edge_ref[k].astype(jnp.float32)
        taps = sf_ref[k]
        previous = jnp.where(row == 0, edge[1:2], pltpu.roll(x, 1, 0))
        before = jnp.where(row == 0, edge[0:1], jnp.where(row == 1, edge[1:2], pltpu.roll(x, 2, 0)))
        total = taps[0:1] * x
        total = total + taps[1:2] * previous
        return total + taps[2:3] * before

    gate_rows = mixed(0, gate_ref)
    carried = (mixed(1, second_ref) * mixed(2, carrier_ref)).astype(jnp.bfloat16)

    owner = lax.broadcasted_iota(jnp.int32, (1, lanes), 1) // group
    toeplitz = []
    for i in range(per_tile):
        v = jnp.broadcast_to(fw_ref[i : i + 1, :], (BLOCK, fw_ref.shape[1]))
        rolled = pltpu.roll(v, 0, 1, stride=1, stride_axis=0)
        toeplitz.append(rolled[:, : 2 * BLOCK].astype(jnp.bfloat16))
    bias = bias_ref[...]
    for b in range(blocks):
        before = halo_ref[...] if b == 0 else carried[BLOCK * (b - 1) : BLOCK * b]
        current = carried[BLOCK * b : BLOCK * (b + 1)]
        window = jnp.concatenate([before, current], axis=0)
        acc = jnp.zeros((BLOCK, lanes), jnp.float32)
        for i in range(per_tile):
            masked = jnp.where(owner == i, window, jnp.zeros_like(window))
            acc = acc + jnp.dot(toeplitz[i], masked, preferred_element_type=jnp.float32)
        gate = gate_rows[BLOCK * b : BLOCK * (b + 1)]
        direct = bias * current.astype(jnp.float32)
        out_ref[BLOCK * b : BLOCK * (b + 1), :] = (gate * (acc + direct)).astype(out_ref.dtype)


def hyena_gate(halo, edge, projected, short_filter, long_filter, conv_bias, part, parts):
    groups, taps = long_filter.shape
    row_count = projected.shape[0]
    channels = halo.shape[1]
    per_tile = LANES // (channels // groups)
    tiles = channels // LANES
    share = tiles // parts
    first = part * share
    fw = jnp.pad(long_filter[:, ::-1].astype(jnp.float32), ((0, 0), (1, 3 * BLOCK - 1 - taps)))
    edges = edge.reshape(2, 3, channels).transpose(1, 0, 2)
    filters = short_filter.reshape(3, 3, channels).transpose(1, 0, 2)
    column = lambda k: pl.BlockSpec((row_count, LANES), lambda j: (0, first + j + k * tiles))
    return pl.pallas_call(
        _gate_kernel,
        grid=(share,),
        in_specs=[
            pl.BlockSpec((per_tile, 3 * BLOCK), lambda j: (first + j, 0)),
            pl.BlockSpec((1, LANES), lambda j: (0, first + j)),
            pl.BlockSpec((3, 3, LANES), lambda j: (0, 0, first + j)),
            pl.BlockSpec((3, 2, LANES), lambda j: (0, 0, first + j)),
            pl.BlockSpec((BLOCK, LANES), lambda j: (0, first + j)),
            column(0),
            column(1),
            column(2),
        ],
        out_specs=pl.BlockSpec((row_count, LANES), lambda j: (0, j)),
        out_shape=jax.ShapeDtypeStruct((row_count, share * LANES), jnp.bfloat16),
    )(fw, conv_bias.reshape(1, channels), filters, edges, halo, projected, projected, projected)


def ring_place(c, chips):
    return jnp.where(c % 2 == 0, c // 2, chips - 1 - c // 2)


def ring_chip(q, chips):
    return jnp.where(q < chips // 2, 2 * q, 2 * (chips - 1 - q) + 1)


def carried_of(second, carrier):
    return (second * carrier).astype(jnp.bfloat16)


def on_device(tokens, projected, short_filter, long_filter, conv_bias, out_weight):
    row_count = tokens.shape[0]
    channels = out_weight.shape[0]
    chips = lax.axis_size("chip")
    width = out_weight.shape[1]
    ring = chips % 2 == 0 and chips <= 8

    chip = lax.axis_index("chip")
    core = lax.axis_index("core")
    position = ring_place(chip, chips)
    order = ring_order(chips)
    forward = [(order[i], order[(i + 1) % chips]) for i in range(chips)]
    backward = [(order[(i + 1) % chips], order[i]) for i in range(chips)]
    swap = [(0, 1), (1, 0)]
    steps = chips // 2

    slots = []

    def add(piece, owner_chip):
        other = lax.ppermute(piece, "core", swap)
        slots.append((owner_chip * 2 + core, piece))
        slots.append((owner_chip * 2 + 1 - core, other))

    def ring_step(step, ahead, behind):
        if step == steps:
            half = channels // 2
            ahead = lax.ppermute(ahead[:half], "chip", forward)
            behind = lax.ppermute(behind[half:], "chip", backward)
            source = ring_chip((position - step) % chips, chips)
            add(jnp.concatenate([ahead, behind], axis=0), source)
        else:
            ahead = lax.ppermute(ahead, "chip", forward)
            behind = lax.ppermute(behind, "chip", backward)
            add(ahead, ring_chip((position - step) % chips, chips))
            add(behind, ring_chip((position + step) % chips, chips))
        return ahead, behind

    ahead = behind = out_weight
    if ring:
        add(out_weight, chip)
        ahead, behind = ring_step(1, ahead, behind)

    tail = projected[row_count - BLOCK - 2 :]
    tail_mixed = [
        short_mixed(tail[:2, k * channels : (k + 1) * channels], tail[2:, k * channels : (k + 1) * channels], short_filter[:, k * channels : (k + 1) * channels])
        for k in (1, 2)
    ]
    halo = shifted(carried_of(*tail_mixed), 1)
    edge = shifted(projected[row_count - 2 :], 1)
    halo, edge, ahead, behind = lax.optimization_barrier((halo, edge, ahead, behind))
    if ring and steps >= 2:
        ahead, behind = ring_step(2, ahead, behind)

    inputs = (halo, edge, projected, short_filter, long_filter, conv_bias)
    first = hyena_gate(*inputs, 0, 2)
    if ring:
        first, ahead, behind, inputs = lax.optimization_barrier((first, ahead, behind, inputs))
        if steps >= 3:
            ahead, behind = ring_step(3, ahead, behind)
    second = hyena_gate(*inputs, 1, 2)
    gated = jnp.concatenate([first, second], axis=1)
    if not ring:
        weight = lax.all_gather(out_weight, CTX, axis=1, tiled=True)
        branch = jnp.dot(gated, weight, preferred_element_type=jnp.float32)
        return (tokens.astype(jnp.float32) + branch).astype(jnp.bfloat16)
    gated, ahead, behind = lax.optimization_barrier((gated, ahead, behind))
    early = len(slots)
    for step in range(4, steps + 1):
        ahead, behind = ring_step(step, ahead, behind)
    chunks = [slots[:early], slots[early:]] if len(slots) > early else [slots]
    parts = []
    for chunk in chunks:
        weight = jnp.concatenate([piece for _, piece in chunk], axis=1)
        parts.append(jnp.dot(gated, weight, preferred_element_type=jnp.float32))
    branch = jnp.concatenate(parts, axis=1)
    blocks = len(slots)
    owners = jnp.stack([jnp.asarray(c, jnp.int32) for c, _ in slots])
    inverse = jnp.sum(
        jnp.where(owners[None, :] == jnp.arange(blocks, dtype=jnp.int32)[:, None], jnp.arange(blocks, dtype=jnp.int32)[None, :], 0),
        axis=1,
    )
    width = out_weight.shape[1]
    ordered = jnp.take(branch.reshape(row_count, blocks, width), inverse, axis=1).reshape(row_count, blocks * width)
    return (tokens.astype(jnp.float32) + ordered).astype(jnp.bfloat16)


def solution(mesh):
    inner = split_mesh(mesh)
    rows = P(("groups",) + CTX, None)
    placed = (rows, rows, P(), P(), P(), P(None, CTX))
    return jax.shard_map(on_device, mesh=inner, in_specs=placed, out_specs=rows, check_vma=False)
```

```python
import jax
import jax.numpy as jnp
from jax import lax
from jax.experimental import pallas as pl
from jax.experimental.pallas import tpu as pltpu
from jax.sharding import Mesh
from jax.sharding import PartitionSpec as P

CTX = ("chip", "core")
BLOCK = 128
LANES = 128


def split_mesh(mesh):
    groups, ctx = mesh.devices.shape
    return Mesh(mesh.devices.reshape(groups, ctx // 2, 2), ("groups",) + CTX)


def shifted(block, distance):
    devices = range(lax.axis_size(CTX))
    route = [(i - distance, i) for i in devices if i - distance in devices]
    return lax.ppermute(block, CTX, route)


def ring_order(chips):
    down = [2 * i for i in range(chips // 2)]
    up = [2 * i + 1 for i in reversed(range(chips // 2))]
    return down + up


def short_mixed(edge, rows, short_filter):
    previous = jnp.concatenate([edge[1:], rows[:-1]], axis=0).astype(jnp.float32)
    before = jnp.concatenate([edge, rows[:-2]], axis=0).astype(jnp.float32)
    total = short_filter[0] * rows.astype(jnp.float32)
    total = total + short_filter[1] * previous
    return total + short_filter[2] * before


def _gate_kernel(fw_ref, bias_ref, sf_ref, edge_ref, halo_ref, gate_ref, second_ref, carrier_ref, out_ref):
    lanes = out_ref.shape[1]
    per_tile = fw_ref.shape[0]
    group = lanes // per_tile
    row_count = out_ref.shape[0]
    blocks = row_count // BLOCK
    row = lax.broadcasted_iota(jnp.int32, (row_count, lanes), 0)

    def mixed(k, ref):
        x = ref[...].astype(jnp.float32)
        edge = edge_ref[k].astype(jnp.float32)
        taps = sf_ref[k]
        previous = jnp.where(row == 0, edge[1:2], pltpu.roll(x, 1, 0))
        before = jnp.where(row == 0, edge[0:1], jnp.where(row == 1, edge[1:2], pltpu.roll(x, 2, 0)))
        total = taps[0:1] * x
        total = total + taps[1:2] * previous
        return total + taps[2:3] * before

    gate_rows = mixed(0, gate_ref)
    carried = (mixed(1, second_ref) * mixed(2, carrier_ref)).astype(jnp.bfloat16)

    owner = lax.broadcasted_iota(jnp.int32, (1, lanes), 1) // group
    toeplitz = []
    for i in range(per_tile):
        v = jnp.broadcast_to(fw_ref[i : i + 1, :], (BLOCK, fw_ref.shape[1]))
        rolled = pltpu.roll(v, 0, 1, stride=1, stride_axis=0)
        toeplitz.append(rolled[:, : 2 * BLOCK].astype(jnp.bfloat16))
    bias = bias_ref[...]
    for b in range(blocks):
        before = halo_ref[...] if b == 0 else carried[BLOCK * (b - 1) : BLOCK * b]
        current = carried[BLOCK * b : BLOCK * (b + 1)]
        window = jnp.concatenate([before, current], axis=0)
        acc = jnp.zeros((BLOCK, lanes), jnp.float32)
        for i in range(per_tile):
            masked = jnp.where(owner == i, window, jnp.zeros_like(window))
            acc = acc + jnp.dot(toeplitz[i], masked, preferred_element_type=jnp.float32)
        gate = gate_rows[BLOCK * b : BLOCK * (b + 1)]
        direct = bias * current.astype(jnp.float32)
        out_ref[BLOCK * b : BLOCK * (b + 1), :] = (gate * (acc + direct)).astype(out_ref.dtype)


def hyena_gate(halo, edge, projected, short_filter, long_filter, conv_bias, part, parts):
    groups, taps = long_filter.shape
    row_count = projected.shape[0]
    channels = halo.shape[1]
    per_tile = LANES // (channels // groups)
    tiles = channels // LANES
    share = tiles // parts
    first = part * share
    fw = jnp.pad(long_filter[:, ::-1].astype(jnp.float32), ((0, 0), (1, 3 * BLOCK - 1 - taps)))
    edges = edge.reshape(2, 3, channels).transpose(1, 0, 2)
    filters = short_filter.reshape(3, 3, channels).transpose(1, 0, 2)
    column = lambda k: pl.BlockSpec((row_count, LANES), lambda j: (0, first + j + k * tiles))
    return pl.pallas_call(
        _gate_kernel,
        grid=(share,),
        in_specs=[
            pl.BlockSpec((per_tile, 3 * BLOCK), lambda j: (first + j, 0)),
            pl.BlockSpec((1, LANES), lambda j: (0, first + j)),
            pl.BlockSpec((3, 3, LANES), lambda j: (0, 0, first + j)),
            pl.BlockSpec((3, 2, LANES), lambda j: (0, 0, first + j)),
            pl.BlockSpec((BLOCK, LANES), lambda j: (0, first + j)),
            column(0),
            column(1),
            column(2),
        ],
        out_specs=pl.BlockSpec((row_count, LANES), lambda j: (0, j)),
        out_shape=jax.ShapeDtypeStruct((row_count, share * LANES), jnp.bfloat16),
    )(fw, conv_bias.reshape(1, channels), filters, edges, halo, projected, projected, projected)


def ring_place(c, chips):
    return jnp.where(c % 2 == 0, c // 2, chips - 1 - c // 2)


def ring_chip(q, chips):
    return jnp.where(q < chips // 2, 2 * q, 2 * (chips - 1 - q) + 1)


def carried_of(second, carrier):
    return (second * carrier).astype(jnp.bfloat16)


def on_device(tokens, projected, short_filter, long_filter, conv_bias, out_weight):
    row_count = tokens.shape[0]
    channels = out_weight.shape[0]
    chips = lax.axis_size("chip")
    width = out_weight.shape[1]
    ring = chips % 2 == 0 and chips <= 8

    chip = lax.axis_index("chip")
    core = lax.axis_index("core")
    position = ring_place(chip, chips)
    order = ring_order(chips)
    forward = [(order[i], order[(i + 1) % chips]) for i in range(chips)]
    backward = [(order[(i + 1) % chips], order[i]) for i in range(chips)]
    swap = [(0, 1), (1, 0)]
    steps = chips // 2

    weight = jnp.zeros((channels, chips * 2 * width), out_weight.dtype)
    first_core = core == 0
    clockwise = [(order[i] * 2, order[(i + 1) % chips] * 2) for i in range(chips)]
    counter = [(order[(i + 1) % chips] * 2 + 1, order[i] * 2 + 1) for i in range(chips)]

    def place(weight, pair, owner_chip):
        return lax.dynamic_update_slice(weight, pair, (0, owner_chip * 2 * width))

    def ring_step(step, weight, held):
        last = step == steps
        route = clockwise if last else clockwise + counter
        held = lax.ppermute(held, CTX, route)
        ahead = ring_chip((position - step) % chips, chips)
        if last:
            given = lax.ppermute(held, "core", [(0, 1)])
            return place(weight, jnp.where(first_core, held, given), ahead), held
        behind = ring_chip((position + step) % chips, chips)
        given = lax.ppermute(held, "core", swap)
        weight = place(weight, held, jnp.where(first_core, ahead, behind))
        weight = place(weight, given, jnp.where(first_core, behind, ahead))
        return weight, held

    held = out_weight
    if ring:
        partner = lax.ppermute(out_weight, "core", swap)
        held = jnp.where(
            first_core,
            jnp.concatenate([out_weight, partner], axis=1),
            jnp.concatenate([partner, out_weight], axis=1),
        )
        weight = place(weight, held, chip)
        weight, held = ring_step(1, weight, held)

    tail = projected[row_count - BLOCK - 2 :]
    tail_mixed = [
        short_mixed(tail[:2, k * channels : (k + 1) * channels], tail[2:, k * channels : (k + 1) * channels], short_filter[:, k * channels : (k + 1) * channels])
        for k in (1, 2)
    ]
    halo = shifted(carried_of(*tail_mixed), 1)
    edge = shifted(projected[row_count - 2 :], 1)
    halo, edge, held = lax.optimization_barrier((halo, edge, held))
    if ring and steps >= 2:
        weight, held = ring_step(2, weight, held)

    inputs = (halo, edge, projected, short_filter, long_filter, conv_bias)
    first = hyena_gate(*inputs, 0, 2)
    if ring:
        first, held, inputs = lax.optimization_barrier((first, held, inputs))
        if steps >= 3:
            weight, held = ring_step(3, weight, held)
    second = hyena_gate(*inputs, 1, 2)
    if ring:
        second, held = lax.optimization_barrier((second, held))
        for step in range(4, steps + 1):
            weight, held = ring_step(step, weight, held)
    else:
        weight = lax.all_gather(out_weight, CTX, axis=1, tiled=True)
    gated = jnp.concatenate([first, second], axis=1)
    branch = jnp.dot(gated, weight, preferred_element_type=jnp.float32)
    return (tokens.astype(jnp.float32) + branch).astype(jnp.bfloat16)


def solution(mesh):
    inner = split_mesh(mesh)
    rows = P(("groups",) + CTX, None)
    placed = (rows, rows, P(), P(), P(), P(None, CTX))
    return jax.shard_map(on_device, mesh=inner, in_specs=placed, out_specs=rows, check_vma=False)
```

```python
import jax
import jax.numpy as jnp
from jax import lax
from jax.experimental import pallas as pl
from jax.experimental.pallas import tpu as pltpu
from jax.sharding import Mesh
from jax.sharding import PartitionSpec as P

CTX = ("chip", "core")
BLOCK = 128
LANES = 128


def split_mesh(mesh):
    groups, ctx = mesh.devices.shape
    return Mesh(mesh.devices.reshape(groups, ctx // 2, 2), ("groups",) + CTX)


def shifted(block, distance):
    devices = range(lax.axis_size(CTX))
    route = [(i - distance, i) for i in devices if i - distance in devices]
    return lax.ppermute(block, CTX, route)


def ring_order(chips):
    down = [2 * i for i in range(chips // 2)]
    up = [2 * i + 1 for i in reversed(range(chips // 2))]
    return down + up


def short_mixed(edge, rows, short_filter):
    previous = jnp.concatenate([edge[1:], rows[:-1]], axis=0).astype(jnp.float32)
    before = jnp.concatenate([edge, rows[:-2]], axis=0).astype(jnp.float32)
    total = short_filter[0] * rows.astype(jnp.float32)
    total = total + short_filter[1] * previous
    return total + short_filter[2] * before


def _gate_kernel(fw_ref, bias_ref, sf_ref, edge_ref, halo_ref, gate_ref, second_ref, carrier_ref, out_ref):
    lanes = out_ref.shape[1]
    per_tile = fw_ref.shape[0]
    group = lanes // per_tile
    row_count = out_ref.shape[0]
    blocks = row_count // BLOCK
    row = lax.broadcasted_iota(jnp.int32, (row_count, lanes), 0)

    def mixed(k, ref):
        x = ref[...].astype(jnp.float32)
        edge = edge_ref[k].astype(jnp.float32)
        taps = sf_ref[k]
        previous = jnp.where(row == 0, edge[1:2], pltpu.roll(x, 1, 0))
        before = jnp.where(row == 0, edge[0:1], jnp.where(row == 1, edge[1:2], pltpu.roll(x, 2, 0)))
        total = taps[0:1] * x
        total = total + taps[1:2] * previous
        return total + taps[2:3] * before

    gate_rows = mixed(0, gate_ref)
    carried = (mixed(1, second_ref) * mixed(2, carrier_ref)).astype(jnp.bfloat16)

    owner = lax.broadcasted_iota(jnp.int32, (1, lanes), 1) // group
    toeplitz = []
    for i in range(per_tile):
        v = jnp.broadcast_to(fw_ref[i : i + 1, :], (BLOCK, fw_ref.shape[1]))
        rolled = pltpu.roll(v, 0, 1, stride=1, stride_axis=0)
        toeplitz.append(rolled[:, : 2 * BLOCK].astype(jnp.bfloat16))
    stacked = jnp.concatenate(toeplitz, axis=1)
    columns = []
    for b in range(blocks):
        before = halo_ref[...] if b == 0 else carried[BLOCK * (b - 1) : BLOCK * b]
        window = jnp.concatenate([before, carried[BLOCK * b : BLOCK * (b + 1)]], axis=0)
        zero = jnp.zeros_like(window)
        columns.append(jnp.concatenate([jnp.where(owner == i, window, zero) for i in range(per_tile)], axis=0))
    conv = jnp.dot(stacked, jnp.concatenate(columns, axis=1), preferred_element_type=jnp.float32)
    bias = bias_ref[...]
    for b in range(blocks):
        current = carried[BLOCK * b : BLOCK * (b + 1)]
        gate = gate_rows[BLOCK * b : BLOCK * (b + 1)]
        direct = bias * current.astype(jnp.float32)
        acc = conv[:, BLOCK * b : BLOCK * (b + 1)]
        out_ref[BLOCK * b : BLOCK * (b + 1), :] = (gate * (acc + direct)).astype(out_ref.dtype)


def hyena_gate(halo, edge, projected, short_filter, long_filter, conv_bias, part, parts):
    groups, taps = long_filter.shape
    row_count = projected.shape[0]
    channels = halo.shape[1]
    per_tile = LANES // (channels // groups)
    tiles = channels // LANES
    share = tiles // parts
    first = part * share
    fw = jnp.pad(long_filter[:, ::-1].astype(jnp.float32), ((0, 0), (1, 3 * BLOCK - 1 - taps)))
    edges = edge.reshape(2, 3, channels).transpose(1, 0, 2)
    filters = short_filter.reshape(3, 3, channels).transpose(1, 0, 2)
    column = lambda k: pl.BlockSpec((row_count, LANES), lambda j: (0, first + j + k * tiles))
    return pl.pallas_call(
        _gate_kernel,
        grid=(share,),
        in_specs=[
            pl.BlockSpec((per_tile, 3 * BLOCK), lambda j: (first + j, 0)),
            pl.BlockSpec((1, LANES), lambda j: (0, first + j)),
            pl.BlockSpec((3, 3, LANES), lambda j: (0, 0, first + j)),
            pl.BlockSpec((3, 2, LANES), lambda j: (0, 0, first + j)),
            pl.BlockSpec((BLOCK, LANES), lambda j: (0, first + j)),
            column(0),
            column(1),
            column(2),
        ],
        out_specs=pl.BlockSpec((row_count, LANES), lambda j: (0, j)),
        out_shape=jax.ShapeDtypeStruct((row_count, share * LANES), jnp.bfloat16),
    )(fw, conv_bias.reshape(1, channels), filters, edges, halo, projected, projected, projected)


def ring_place(c, chips):
    return jnp.where(c % 2 == 0, c // 2, chips - 1 - c // 2)


def ring_chip(q, chips):
    return jnp.where(q < chips // 2, 2 * q, 2 * (chips - 1 - q) + 1)


def carried_of(second, carrier):
    return (second * carrier).astype(jnp.bfloat16)


def on_device(tokens, projected, short_filter, long_filter, conv_bias, out_weight):
    row_count = tokens.shape[0]
    channels = out_weight.shape[0]
    chips = lax.axis_size("chip")
    width = out_weight.shape[1]
    ring = chips % 2 == 0 and chips <= 8

    chip = lax.axis_index("chip")
    core = lax.axis_index("core")
    position = ring_place(chip, chips)
    order = ring_order(chips)
    forward = [(order[i], order[(i + 1) % chips]) for i in range(chips)]
    backward = [(order[(i + 1) % chips], order[i]) for i in range(chips)]
    swap = [(0, 1), (1, 0)]
    steps = chips // 2

    weight = jnp.zeros((channels, chips * 2 * width), out_weight.dtype)

    def place(weight, piece, owner_chip, row=0):
        other = lax.ppermute(piece, "core", swap)
        for k, part in ((core, piece), (1 - core, other)):
            weight = lax.dynamic_update_slice(weight, part, (row, (owner_chip * 2 + k) * width))
        return weight

    def ring_step(step, weight, ahead, behind):
        if step == steps:
            half = channels // 2
            ahead = lax.ppermute(ahead[:half], "chip", forward)
            behind = lax.ppermute(behind[half:], "chip", backward)
            source = ring_chip((position - step) % chips, chips)
            weight = place(weight, ahead, source, 0)
            weight = place(weight, behind, source, half)
        else:
            ahead = lax.ppermute(ahead, "chip", forward)
            behind = lax.ppermute(behind, "chip", backward)
            weight = place(weight, ahead, ring_chip((position - step) % chips, chips))
            weight = place(weight, behind, ring_chip((position + step) % chips, chips))
        return weight, ahead, behind

    ahead = behind = out_weight
    if ring:
        weight = place(weight, out_weight, chip)
        weight, ahead, behind = ring_step(1, weight, ahead, behind)

    tail = projected[row_count - BLOCK - 2 :]
    tail_mixed = [
        short_mixed(tail[:2, k * channels : (k + 1) * channels], tail[2:, k * channels : (k + 1) * channels], short_filter[:, k * channels : (k + 1) * channels])
        for k in (1, 2)
    ]
    halo = shifted(carried_of(*tail_mixed), 1)
    edge = shifted(projected[row_count - 2 :], 1)
    halo, edge, ahead, behind = lax.optimization_barrier((halo, edge, ahead, behind))
    if ring and steps >= 2:
        weight, ahead, behind = ring_step(2, weight, ahead, behind)

    inputs = (halo, edge, projected, short_filter, long_filter, conv_bias)
    first = hyena_gate(*inputs, 0, 2)
    if ring:
        first, ahead, behind, inputs = lax.optimization_barrier((first, ahead, behind, inputs))
        if steps >= 3:
            weight, ahead, behind = ring_step(3, weight, ahead, behind)
    second = hyena_gate(*inputs, 1, 2)
    if ring:
        second, ahead, behind = lax.optimization_barrier((second, ahead, behind))
        for step in range(4, steps + 1):
            weight, ahead, behind = ring_step(step, weight, ahead, behind)
    else:
        weight = lax.all_gather(out_weight, CTX, axis=1, tiled=True)
    gated = jnp.concatenate([first, second], axis=1)
    branch = jnp.dot(gated, weight, preferred_element_type=jnp.float32)
    return (tokens.astype(jnp.float32) + branch).astype(jnp.bfloat16)


def solution(mesh):
    inner = split_mesh(mesh)
    rows = P(("groups",) + CTX, None)
    placed = (rows, rows, P(), P(), P(), P(None, CTX))
    return jax.shard_map(on_device, mesh=inner, in_specs=placed, out_specs=rows, check_vma=False)
```

```python
import jax
import jax.numpy as jnp
from jax import lax
from jax.experimental import pallas as pl
from jax.experimental.pallas import tpu as pltpu
from jax.sharding import Mesh
from jax.sharding import PartitionSpec as P

CTX = ("chip", "core")
BLOCK = 128
LANES = 128


def split_mesh(mesh):
    groups, ctx = mesh.devices.shape
    return Mesh(mesh.devices.reshape(groups, ctx // 2, 2), ("groups",) + CTX)


def shifted(block, distance):
    devices = range(lax.axis_size(CTX))
    route = [(i - distance, i) for i in devices if i - distance in devices]
    return lax.ppermute(block, CTX, route)


def ring_order(chips):
    down = [2 * i for i in range(chips // 2)]
    up = [2 * i + 1 for i in reversed(range(chips // 2))]
    return down + up


def short_mixed(edge, rows, short_filter):
    previous = jnp.concatenate([edge[1:], rows[:-1]], axis=0).astype(jnp.float32)
    before = jnp.concatenate([edge, rows[:-2]], axis=0).astype(jnp.float32)
    total = short_filter[0] * rows.astype(jnp.float32)
    total = total + short_filter[1] * previous
    return total + short_filter[2] * before


def _gate_kernel(fw_ref, bias_ref, sf_ref, edge_ref, halo_ref, gate_ref, second_ref, carrier_ref, out_ref):
    lanes = out_ref.shape[1]
    per_tile = fw_ref.shape[0]
    group = lanes // per_tile
    row_count = out_ref.shape[0]
    blocks = row_count // BLOCK
    row = lax.broadcasted_iota(jnp.int32, (row_count, lanes), 0)

    def mixed(k, ref):
        x = ref[...].astype(jnp.float32)
        edge = edge_ref[k].astype(jnp.float32)
        taps = sf_ref[k]
        previous = jnp.where(row == 0, edge[1:2], pltpu.roll(x, 1, 0))
        before = jnp.where(row == 0, edge[0:1], jnp.where(row == 1, edge[1:2], pltpu.roll(x, 2, 0)))
        total = taps[0:1] * x
        total = total + taps[1:2] * previous
        return total + taps[2:3] * before

    gate_rows = mixed(0, gate_ref)
    carried = (mixed(1, second_ref) * mixed(2, carrier_ref)).astype(jnp.bfloat16)

    owner = lax.broadcasted_iota(jnp.int32, (1, lanes), 1) // group
    toeplitz = []
    for i in range(per_tile):
        v = jnp.broadcast_to(fw_ref[i : i + 1, :], (BLOCK, fw_ref.shape[1]))
        rolled = pltpu.roll(v, 0, 1, stride=1, stride_axis=0)
        toeplitz.append(rolled[:, : 2 * BLOCK].astype(jnp.bfloat16))
    stacked = jnp.concatenate(toeplitz, axis=1)
    columns = []
    for b in range(blocks):
        before = halo_ref[...] if b == 0 else carried[BLOCK * (b - 1) : BLOCK * b]
        window = jnp.concatenate([before, carried[BLOCK * b : BLOCK * (b + 1)]], axis=0)
        zero = jnp.zeros_like(window)
        columns.append(jnp.concatenate([jnp.where(owner == i, window, zero) for i in range(per_tile)], axis=0))
    conv = jnp.dot(stacked, jnp.concatenate(columns, axis=1), preferred_element_type=jnp.float32)
    bias = bias_ref[...]
    for b in range(blocks):
        current = carried[BLOCK * b : BLOCK * (b + 1)]
        gate = gate_rows[BLOCK * b : BLOCK * (b + 1)]
        direct = bias * current.astype(jnp.float32)
        acc = conv[:, BLOCK * b : BLOCK * (b + 1)]
        out_ref[BLOCK * b : BLOCK * (b + 1), :] = (gate * (acc + direct)).astype(out_ref.dtype)


def hyena_gate(halo, edge, projected, short_filter, long_filter, conv_bias, part, parts):
    groups, taps = long_filter.shape
    row_count = projected.shape[0]
    channels = halo.shape[1]
    per_tile = LANES // (channels // groups)
    tiles = channels // LANES
    share = tiles // parts
    first = part * share
    fw = jnp.pad(long_filter[:, ::-1].astype(jnp.float32), ((0, 0), (1, 3 * BLOCK - 1 - taps)))
    edges = edge.reshape(2, 3, channels).transpose(1, 0, 2)
    filters = short_filter.reshape(3, 3, channels).transpose(1, 0, 2)
    column = lambda k: pl.BlockSpec((row_count, LANES), lambda j: (0, first + j + k * tiles))
    return pl.pallas_call(
        _gate_kernel,
        grid=(share,),
        in_specs=[
            pl.BlockSpec((per_tile, 3 * BLOCK), lambda j: (first + j, 0)),
            pl.BlockSpec((1, LANES), lambda j: (0, first + j)),
            pl.BlockSpec((3, 3, LANES), lambda j: (0, 0, first + j)),
            pl.BlockSpec((3, 2, LANES), lambda j: (0, 0, first + j)),
            pl.BlockSpec((BLOCK, LANES), lambda j: (0, first + j)),
            column(0),
            column(1),
            column(2),
        ],
        out_specs=pl.BlockSpec((row_count, LANES), lambda j: (0, j)),
        out_shape=jax.ShapeDtypeStruct((row_count, share * LANES), jnp.bfloat16),
    )(fw, conv_bias.reshape(1, channels), filters, edges, halo, projected, projected, projected)


def ring_place(c, chips):
    return jnp.where(c % 2 == 0, c // 2, chips - 1 - c // 2)


def ring_chip(q, chips):
    return jnp.where(q < chips // 2, 2 * q, 2 * (chips - 1 - q) + 1)


def carried_of(second, carrier):
    return (second * carrier).astype(jnp.bfloat16)


def on_device(tokens, projected, short_filter, long_filter, conv_bias, out_weight):
    row_count = tokens.shape[0]
    channels = out_weight.shape[0]
    chips = lax.axis_size("chip")
    width = out_weight.shape[1]
    ring = chips % 2 == 0 and chips <= 8

    chip = lax.axis_index("chip")
    core = lax.axis_index("core")
    position = ring_place(chip, chips)
    order = ring_order(chips)
    forward = [(order[i], order[(i + 1) % chips]) for i in range(chips)]
    backward = [(order[(i + 1) % chips], order[i]) for i in range(chips)]
    swap = [(0, 1), (1, 0)]
    steps = chips // 2

    weight = jnp.zeros((chips * 2 * width, channels), out_weight.dtype)

    def place(weight, piece, owner_chip, row=0):
        other = lax.ppermute(piece, "core", swap)
        for k, part in ((core, piece), (1 - core, other)):
            weight = lax.dynamic_update_slice(weight, part, ((owner_chip * 2 + k) * width, row))
        return weight

    def ring_step(step, weight, ahead, behind):
        if step == steps:
            half = channels // 2
            ahead = lax.ppermute(ahead[:, :half], "chip", forward)
            behind = lax.ppermute(behind[:, half:], "chip", backward)
            source = ring_chip((position - step) % chips, chips)
            weight = place(weight, ahead, source, 0)
            weight = place(weight, behind, source, half)
        else:
            ahead = lax.ppermute(ahead, "chip", forward)
            behind = lax.ppermute(behind, "chip", backward)
            weight = place(weight, ahead, ring_chip((position - step) % chips, chips))
            weight = place(weight, behind, ring_chip((position + step) % chips, chips))
        return weight, ahead, behind

    ahead = behind = out_weight.T
    if ring:
        weight = place(weight, ahead, chip)
        weight, ahead, behind = ring_step(1, weight, ahead, behind)

    tail = projected[row_count - BLOCK - 2 :]
    tail_mixed = [
        short_mixed(tail[:2, k * channels : (k + 1) * channels], tail[2:, k * channels : (k + 1) * channels], short_filter[:, k * channels : (k + 1) * channels])
        for k in (1, 2)
    ]
    halo = shifted(carried_of(*tail_mixed), 1)
    edge = shifted(projected[row_count - 2 :], 1)
    halo, edge, ahead, behind = lax.optimization_barrier((halo, edge, ahead, behind))
    if ring and steps >= 2:
        weight, ahead, behind = ring_step(2, weight, ahead, behind)

    inputs = (halo, edge, projected, short_filter, long_filter, conv_bias)
    first = hyena_gate(*inputs, 0, 2)
    if ring:
        first, ahead, behind, inputs = lax.optimization_barrier((first, ahead, behind, inputs))
        if steps >= 3:
            weight, ahead, behind = ring_step(3, weight, ahead, behind)
    second = hyena_gate(*inputs, 1, 2)
    if ring:
        second, ahead, behind = lax.optimization_barrier((second, ahead, behind))
        for step in range(4, steps + 1):
            weight, ahead, behind = ring_step(step, weight, ahead, behind)
    else:
        weight = lax.all_gather(out_weight.T, CTX, axis=0, tiled=True)
    gated = jnp.concatenate([first, second], axis=1)
    branch = lax.dot_general(gated, weight, (((1,), (1,)), ((), ())), preferred_element_type=jnp.float32)
    return (tokens.astype(jnp.float32) + branch).astype(jnp.bfloat16)


def solution(mesh):
    inner = split_mesh(mesh)
    rows = P(("groups",) + CTX, None)
    placed = (rows, rows, P(), P(), P(), P(None, CTX))
    return jax.shard_map(on_device, mesh=inner, in_specs=placed, out_specs=rows, check_vma=False)
```

```python
import jax
import jax.numpy as jnp
from jax import lax
from jax.experimental import pallas as pl
from jax.experimental.pallas import tpu as pltpu
from jax.sharding import Mesh
from jax.sharding import PartitionSpec as P

CTX = ("chip", "core")
BLOCK = 128
LANES = 128


def split_mesh(mesh):
    groups, ctx = mesh.devices.shape
    return Mesh(mesh.devices.reshape(groups, ctx // 2, 2), ("groups",) + CTX)


def shifted(block, distance):
    devices = range(lax.axis_size(CTX))
    route = [(i - distance, i) for i in devices if i - distance in devices]
    return lax.ppermute(block, CTX, route)


def ring_order(chips):
    down = [2 * i for i in range(chips // 2)]
    up = [2 * i + 1 for i in reversed(range(chips // 2))]
    return down + up


def short_mixed(edge, rows, short_filter):
    previous = jnp.concatenate([edge[1:], rows[:-1]], axis=0).astype(jnp.float32)
    before = jnp.concatenate([edge, rows[:-2]], axis=0).astype(jnp.float32)
    total = short_filter[0] * rows.astype(jnp.float32)
    total = total + short_filter[1] * previous
    return total + short_filter[2] * before


def _gate_kernel(fw_ref, bias_ref, sf_ref, edge_ref, halo_ref, gate_ref, second_ref, carrier_ref, out_ref):
    lanes = out_ref.shape[1]
    per_tile = fw_ref.shape[0]
    group = lanes // per_tile
    row_count = out_ref.shape[0]
    blocks = row_count // BLOCK
    row = lax.broadcasted_iota(jnp.int32, (row_count, lanes), 0)

    def mixed(k, ref):
        x = ref[...].astype(jnp.float32)
        edge = edge_ref[k].astype(jnp.float32)
        taps = sf_ref[k]
        previous = jnp.where(row == 0, edge[1:2], pltpu.roll(x, 1, 0))
        before = jnp.where(row == 0, edge[0:1], jnp.where(row == 1, edge[1:2], pltpu.roll(x, 2, 0)))
        total = taps[0:1] * x
        total = total + taps[1:2] * previous
        return total + taps[2:3] * before

    gate_rows = mixed(0, gate_ref)
    carried = (mixed(1, second_ref) * mixed(2, carrier_ref)).astype(jnp.bfloat16)

    owner = lax.broadcasted_iota(jnp.int32, (1, lanes), 1) // group
    toeplitz = []
    for i in range(per_tile):
        v = jnp.broadcast_to(fw_ref[i : i + 1, :], (BLOCK, fw_ref.shape[1]))
        rolled = pltpu.roll(v, 0, 1, stride=1, stride_axis=0)
        toeplitz.append(rolled[:, : 2 * BLOCK].astype(jnp.bfloat16))
    stacked = jnp.concatenate(toeplitz, axis=1)
    columns = []
    for b in range(blocks):
        before = halo_ref[...] if b == 0 else carried[BLOCK * (b - 1) : BLOCK * b]
        window = jnp.concatenate([before, carried[BLOCK * b : BLOCK * (b + 1)]], axis=0)
        zero = jnp.zeros_like(window)
        columns.append(jnp.concatenate([jnp.where(owner == i, window, zero) for i in range(per_tile)], axis=0))
    conv = jnp.dot(stacked, jnp.concatenate(columns, axis=1), preferred_element_type=jnp.float32)
    bias = bias_ref[...]
    for b in range(blocks):
        current = carried[BLOCK * b : BLOCK * (b + 1)]
        gate = gate_rows[BLOCK * b : BLOCK * (b + 1)]
        direct = bias * current.astype(jnp.float32)
        acc = conv[:, BLOCK * b : BLOCK * (b + 1)]
        out_ref[BLOCK * b : BLOCK * (b + 1), :] = (gate * (acc + direct)).astype(out_ref.dtype)


def hyena_gate(halo, edge, projected, short_filter, long_filter, conv_bias, part, parts):
    groups, taps = long_filter.shape
    row_count = projected.shape[0]
    channels = halo.shape[1]
    per_tile = LANES // (channels // groups)
    tiles = channels // LANES
    share = tiles // parts
    first = part * share
    fw = jnp.pad(long_filter[:, ::-1].astype(jnp.float32), ((0, 0), (1, 3 * BLOCK - 1 - taps)))
    edges = edge.reshape(2, 3, channels).transpose(1, 0, 2)
    filters = short_filter.reshape(3, 3, channels).transpose(1, 0, 2)
    column = lambda k: pl.BlockSpec((row_count, LANES), lambda j: (0, first + j + k * tiles))
    return pl.pallas_call(
        _gate_kernel,
        grid=(share,),
        in_specs=[
            pl.BlockSpec((per_tile, 3 * BLOCK), lambda j: (first + j, 0)),
            pl.BlockSpec((1, LANES), lambda j: (0, first + j)),
            pl.BlockSpec((3, 3, LANES), lambda j: (0, 0, first + j)),
            pl.BlockSpec((3, 2, LANES), lambda j: (0, 0, first + j)),
            pl.BlockSpec((BLOCK, LANES), lambda j: (0, first + j)),
            column(0),
            column(1),
            column(2),
        ],
        out_specs=pl.BlockSpec((row_count, LANES), lambda j: (0, j)),
        out_shape=jax.ShapeDtypeStruct((row_count, share * LANES), jnp.bfloat16),
    )(fw, conv_bias.reshape(1, channels), filters, edges, halo, projected, projected, projected)


def ring_place(c, chips):
    return jnp.where(c % 2 == 0, c // 2, chips - 1 - c // 2)


def ring_chip(q, chips):
    return jnp.where(q < chips // 2, 2 * q, 2 * (chips - 1 - q) + 1)


def carried_of(second, carrier):
    return (second * carrier).astype(jnp.bfloat16)


def on_device(tokens, projected, short_filter, long_filter, conv_bias, out_weight):
    row_count = tokens.shape[0]
    channels = out_weight.shape[0]
    chips = lax.axis_size("chip")
    width = out_weight.shape[1]
    ring = chips % 2 == 0 and chips <= 8

    chip = lax.axis_index("chip")
    core = lax.axis_index("core")
    position = ring_place(chip, chips)
    order = ring_order(chips)
    forward = [(order[i], order[(i + 1) % chips]) for i in range(chips)]
    backward = [(order[(i + 1) % chips], order[i]) for i in range(chips)]
    swap = [(0, 1), (1, 0)]
    steps = chips // 2

    weight = jnp.zeros((chips * 2 * width, channels), out_weight.dtype)

    def place(weight, piece, owner_chip, row=0):
        other = lax.ppermute(piece, "core", swap)
        pair = jnp.where(core == 0, jnp.concatenate([piece, other]), jnp.concatenate([other, piece]))
        return lax.dynamic_update_slice(weight, pair, (owner_chip * 2 * width, row))

    def ring_step(step, weight, ahead, behind):
        if step == steps:
            half = channels // 2
            ahead = lax.ppermute(ahead[:, :half], "chip", forward)
            behind = lax.ppermute(behind[:, half:], "chip", backward)
            source = ring_chip((position - step) % chips, chips)
            weight = place(weight, ahead, source, 0)
            weight = place(weight, behind, source, half)
        else:
            ahead = lax.ppermute(ahead, "chip", forward)
            behind = lax.ppermute(behind, "chip", backward)
            weight = place(weight, ahead, ring_chip((position - step) % chips, chips))
            weight = place(weight, behind, ring_chip((position + step) % chips, chips))
        return weight, ahead, behind

    ahead = behind = out_weight.T
    if ring:
        weight = place(weight, ahead, chip)
        weight, ahead, behind = ring_step(1, weight, ahead, behind)

    tail = projected[row_count - BLOCK - 2 :]
    tail_mixed = [
        short_mixed(tail[:2, k * channels : (k + 1) * channels], tail[2:, k * channels : (k + 1) * channels], short_filter[:, k * channels : (k + 1) * channels])
        for k in (1, 2)
    ]
    halo = shifted(carried_of(*tail_mixed), 1)
    edge = shifted(projected[row_count - 2 :], 1)
    halo, edge, ahead, behind = lax.optimization_barrier((halo, edge, ahead, behind))
    if ring and steps >= 2:
        weight, ahead, behind = ring_step(2, weight, ahead, behind)

    inputs = (halo, edge, projected, short_filter, long_filter, conv_bias)
    first = hyena_gate(*inputs, 0, 2)
    if ring:
        first, ahead, behind, inputs = lax.optimization_barrier((first, ahead, behind, inputs))
        if steps >= 3:
            weight, ahead, behind = ring_step(3, weight, ahead, behind)
    second = hyena_gate(*inputs, 1, 2)
    if ring:
        second, ahead, behind = lax.optimization_barrier((second, ahead, behind))
        for step in range(4, steps + 1):
            weight, ahead, behind = ring_step(step, weight, ahead, behind)
    else:
        weight = lax.all_gather(out_weight.T, CTX, axis=0, tiled=True)
    gated = jnp.concatenate([first, second], axis=1)
    branch = lax.dot_general(gated, weight, (((1,), (1,)), ((), ())), preferred_element_type=jnp.float32)
    return (tokens.astype(jnp.float32) + branch).astype(jnp.bfloat16)


def solution(mesh):
    inner = split_mesh(mesh)
    rows = P(("groups",) + CTX, None)
    placed = (rows, rows, P(), P(), P(), P(None, CTX))
    return jax.shard_map(on_device, mesh=inner, in_specs=placed, out_specs=rows, check_vma=False)
```

```python
import jax
import jax.numpy as jnp
from jax import lax
from jax.experimental import pallas as pl
from jax.experimental.pallas import tpu as pltpu
from jax.sharding import Mesh
from jax.sharding import PartitionSpec as P

CTX = ("chip", "core")
BLOCK = 128
LANES = 128


def split_mesh(mesh):
    groups, ctx = mesh.devices.shape
    return Mesh(mesh.devices.reshape(groups, ctx // 2, 2), ("groups",) + CTX)


def shifted(block, distance):
    devices = range(lax.axis_size(CTX))
    route = [(i - distance, i) for i in devices if i - distance in devices]
    return lax.ppermute(block, CTX, route)


def ring_order(chips):
    down = [2 * i for i in range(chips // 2)]
    up = [2 * i + 1 for i in reversed(range(chips // 2))]
    return down + up


def short_mixed(edge, rows, short_filter):
    previous = jnp.concatenate([edge[1:], rows[:-1]], axis=0).astype(jnp.float32)
    before = jnp.concatenate([edge, rows[:-2]], axis=0).astype(jnp.float32)
    total = short_filter[0] * rows.astype(jnp.float32)
    total = total + short_filter[1] * previous
    return total + short_filter[2] * before


def _gate_kernel(fw_ref, bias_ref, sf_ref, edge_ref, halo_ref, gate_ref, second_ref, carrier_ref, out_ref):
    lanes = out_ref.shape[1]
    per_tile = fw_ref.shape[0]
    group = lanes // per_tile
    row_count = out_ref.shape[0]
    blocks = row_count // BLOCK
    row = lax.broadcasted_iota(jnp.int32, (row_count, lanes), 0)

    def mixed(k, ref):
        x = ref[...].astype(jnp.float32)
        edge = edge_ref[k].astype(jnp.float32)
        taps = sf_ref[k]
        previous = jnp.where(row == 0, edge[1:2], pltpu.roll(x, 1, 0))
        before = jnp.where(row == 0, edge[0:1], jnp.where(row == 1, edge[1:2], pltpu.roll(x, 2, 0)))
        total = taps[0:1] * x
        total = total + taps[1:2] * previous
        return total + taps[2:3] * before

    gate_rows = mixed(0, gate_ref)
    carried = (mixed(1, second_ref) * mixed(2, carrier_ref)).astype(jnp.bfloat16)

    owner = lax.broadcasted_iota(jnp.int32, (1, lanes), 1) // group
    toeplitz = []
    for i in range(per_tile):
        v = jnp.broadcast_to(fw_ref[i : i + 1, :], (BLOCK, fw_ref.shape[1]))
        rolled = pltpu.roll(v, 0, 1, stride=1, stride_axis=0)
        toeplitz.append(rolled[:, : 2 * BLOCK].astype(jnp.bfloat16))
    stacked = jnp.concatenate(toeplitz, axis=1)
    columns = []
    for b in range(blocks):
        before = halo_ref[...] if b == 0 else carried[BLOCK * (b - 1) : BLOCK * b]
        window = jnp.concatenate([before, carried[BLOCK * b : BLOCK * (b + 1)]], axis=0)
        zero = jnp.zeros_like(window)
        columns.append(jnp.concatenate([jnp.where(owner == i, window, zero) for i in range(per_tile)], axis=0))
    conv = jnp.dot(stacked, jnp.concatenate(columns, axis=1), preferred_element_type=jnp.float32)
    bias = bias_ref[...]
    for b in range(blocks):
        current = carried[BLOCK * b : BLOCK * (b + 1)]
        gate = gate_rows[BLOCK * b : BLOCK * (b + 1)]
        direct = bias * current.astype(jnp.float32)
        acc = conv[:, BLOCK * b : BLOCK * (b + 1)]
        out_ref[BLOCK * b : BLOCK * (b + 1), :] = (gate * (acc + direct)).astype(out_ref.dtype)


def hyena_gate(halo, edge, projected, short_filter, long_filter, conv_bias, part, parts):
    groups, taps = long_filter.shape
    row_count = projected.shape[0]
    channels = halo.shape[1]
    per_tile = LANES // (channels // groups)
    tiles = channels // LANES
    share = tiles // parts
    first = part * share
    fw = jnp.pad(long_filter[:, ::-1].astype(jnp.float32), ((0, 0), (1, 3 * BLOCK - 1 - taps)))
    edges = edge.reshape(2, 3, channels).transpose(1, 0, 2)
    filters = short_filter.reshape(3, 3, channels).transpose(1, 0, 2)
    column = lambda k: pl.BlockSpec((row_count, LANES), lambda j: (0, first + j + k * tiles))
    return pl.pallas_call(
        _gate_kernel,
        grid=(share,),
        in_specs=[
            pl.BlockSpec((per_tile, 3 * BLOCK), lambda j: (first + j, 0)),
            pl.BlockSpec((1, LANES), lambda j: (0, first + j)),
            pl.BlockSpec((3, 3, LANES), lambda j: (0, 0, first + j)),
            pl.BlockSpec((3, 2, LANES), lambda j: (0, 0, first + j)),
            pl.BlockSpec((BLOCK, LANES), lambda j: (0, first + j)),
            column(0),
            column(1),
            column(2),
        ],
        out_specs=pl.BlockSpec((row_count, LANES), lambda j: (0, j)),
        out_shape=jax.ShapeDtypeStruct((row_count, share * LANES), jnp.bfloat16),
    )(fw, conv_bias.reshape(1, channels), filters, edges, halo, projected, projected, projected)


def ring_place(c, chips):
    return jnp.where(c % 2 == 0, c // 2, chips - 1 - c // 2)


def ring_chip(q, chips):
    return jnp.where(q < chips // 2, 2 * q, 2 * (chips - 1 - q) + 1)


def carried_of(second, carrier):
    return (second * carrier).astype(jnp.bfloat16)


def on_device(tokens, projected, short_filter, long_filter, conv_bias, out_weight):
    row_count = tokens.shape[0]
    channels = out_weight.shape[0]
    chips = lax.axis_size("chip")
    width = out_weight.shape[1]
    ring = chips % 2 == 0 and chips <= 8

    chip = lax.axis_index("chip")
    core = lax.axis_index("core")
    position = ring_place(chip, chips)
    order = ring_order(chips)
    forward = [(order[i], order[(i + 1) % chips]) for i in range(chips)]
    backward = [(order[(i + 1) % chips], order[i]) for i in range(chips)]
    swap = [(0, 1), (1, 0)]
    steps = chips // 2

    weight = None

    pending = []

    def place(weight, piece, owner_chip, row=0):
        other = lax.ppermute(piece, "core", swap)
        for k, part in ((core, piece), (1 - core, other)):
            pending.append((part, (owner_chip * 2 + k) * width, row))
        return weight

    def settle(weight):
        for part, column, row in pending:
            weight = lax.dynamic_update_slice(weight, part, (column, row))
        pending.clear()
        return weight

    def ring_step(step, weight, ahead, behind):
        if step == steps:
            half = channels // 2
            ahead = lax.ppermute(ahead[:, :half], "chip", forward)
            behind = lax.ppermute(behind[:, half:], "chip", backward)
            source = ring_chip((position - step) % chips, chips)
            weight = place(weight, ahead, source, 0)
            weight = place(weight, behind, source, half)
        else:
            ahead = lax.ppermute(ahead, "chip", forward)
            behind = lax.ppermute(behind, "chip", backward)
            weight = place(weight, ahead, ring_chip((position - step) % chips, chips))
            weight = place(weight, behind, ring_chip((position + step) % chips, chips))
        return weight, ahead, behind

    ahead = behind = out_weight.T
    if ring:
        weight = place(weight, ahead, chip)
        weight, ahead, behind = ring_step(1, weight, ahead, behind)

    tail = projected[row_count - BLOCK - 2 :]
    tail_mixed = [
        short_mixed(tail[:2, k * channels : (k + 1) * channels], tail[2:, k * channels : (k + 1) * channels], short_filter[:, k * channels : (k + 1) * channels])
        for k in (1, 2)
    ]
    halo = shifted(carried_of(*tail_mixed), 1)
    edge = shifted(projected[row_count - 2 :], 1)
    halo, edge, ahead, behind = lax.optimization_barrier((halo, edge, ahead, behind))
    if ring and steps >= 2:
        weight, ahead, behind = ring_step(2, weight, ahead, behind)

    inputs = (halo, edge, projected, short_filter, long_filter, conv_bias)
    first = hyena_gate(*inputs, 0, 2)
    if ring:
        first, ahead, behind, inputs = lax.optimization_barrier((first, ahead, behind, inputs))
        weight = jnp.full((chips * 2 * width, channels), first[0, 0] * 0, out_weight.dtype)
        weight = settle(weight)
        if steps >= 3:
            weight, ahead, behind = ring_step(3, weight, ahead, behind)
    second = hyena_gate(*inputs, 1, 2)
    if ring:
        second, ahead, behind = lax.optimization_barrier((second, ahead, behind))
        for step in range(4, steps + 1):
            weight, ahead, behind = ring_step(step, weight, ahead, behind)
        weight = settle(weight)
    else:
        weight = lax.all_gather(out_weight.T, CTX, axis=0, tiled=True)
    gated = jnp.concatenate([first, second], axis=1)
    branch = lax.dot_general(gated, weight, (((1,), (1,)), ((), ())), preferred_element_type=jnp.float32)
    return (tokens.astype(jnp.float32) + branch).astype(jnp.bfloat16)


def solution(mesh):
    inner = split_mesh(mesh)
    rows = P(("groups",) + CTX, None)
    placed = (rows, rows, P(), P(), P(), P(None, CTX))
    return jax.shard_map(on_device, mesh=inner, in_specs=placed, out_specs=rows, check_vma=False)
```

```python
import jax
import jax.numpy as jnp
from jax import lax
from jax.experimental import pallas as pl
from jax.experimental.pallas import tpu as pltpu
from jax.sharding import Mesh
from jax.sharding import PartitionSpec as P

CTX = ("chip", "core")
BLOCK = 128
LANES = 128


def split_mesh(mesh):
    groups, ctx = mesh.devices.shape
    return Mesh(mesh.devices.reshape(groups, ctx // 2, 2), ("groups",) + CTX)


def shifted(block, distance):
    devices = range(lax.axis_size(CTX))
    route = [(i - distance, i) for i in devices if i - distance in devices]
    return lax.ppermute(block, CTX, route)


def ring_order(chips):
    down = [2 * i for i in range(chips // 2)]
    up = [2 * i + 1 for i in reversed(range(chips // 2))]
    return down + up


def short_mixed(edge, rows, short_filter):
    previous = jnp.concatenate([edge[1:], rows[:-1]], axis=0).astype(jnp.float32)
    before = jnp.concatenate([edge, rows[:-2]], axis=0).astype(jnp.float32)
    total = short_filter[0] * rows.astype(jnp.float32)
    total = total + short_filter[1] * previous
    return total + short_filter[2] * before


def _gate_kernel(fw_ref, bias_ref, sf_ref, edge_ref, halo_ref, gate_ref, second_ref, carrier_ref, out_ref):
    lanes = out_ref.shape[1]
    per_tile = fw_ref.shape[0]
    group = lanes // per_tile
    row_count = out_ref.shape[0]
    blocks = row_count // BLOCK
    row = lax.broadcasted_iota(jnp.int32, (row_count, lanes), 0)

    def mixed(k, ref):
        x = ref[...].astype(jnp.float32)
        edge = edge_ref[k].astype(jnp.float32)
        taps = sf_ref[k]
        previous = jnp.where(row == 0, edge[1:2], pltpu.roll(x, 1, 0))
        before = jnp.where(row == 0, edge[0:1], jnp.where(row == 1, edge[1:2], pltpu.roll(x, 2, 0)))
        total = taps[0:1] * x
        total = total + taps[1:2] * previous
        return total + taps[2:3] * before

    gate_rows = mixed(0, gate_ref)
    carried = (mixed(1, second_ref) * mixed(2, carrier_ref)).astype(jnp.bfloat16)

    owner = lax.broadcasted_iota(jnp.int32, (1, lanes), 1) // group
    toeplitz = []
    for i in range(per_tile):
        v = jnp.broadcast_to(fw_ref[i : i + 1, :], (BLOCK, fw_ref.shape[1]))
        rolled = pltpu.roll(v, 0, 1, stride=1, stride_axis=0)
        toeplitz.append(rolled[:, : 2 * BLOCK].astype(jnp.bfloat16))
    stacked = jnp.concatenate(toeplitz, axis=1)
    columns = []
    for b in range(blocks):
        before = halo_ref[...] if b == 0 else carried[BLOCK * (b - 1) : BLOCK * b]
        window = jnp.concatenate([before, carried[BLOCK * b : BLOCK * (b + 1)]], axis=0)
        zero = jnp.zeros_like(window)
        columns.append(jnp.concatenate([jnp.where(owner == i, window, zero) for i in range(per_tile)], axis=0))
    conv = jnp.dot(stacked, jnp.concatenate(columns, axis=1), preferred_element_type=jnp.float32)
    bias = bias_ref[...]
    for b in range(blocks):
        current = carried[BLOCK * b : BLOCK * (b + 1)]
        gate = gate_rows[BLOCK * b : BLOCK * (b + 1)]
        direct = bias * current.astype(jnp.float32)
        acc = conv[:, BLOCK * b : BLOCK * (b + 1)]
        out_ref[BLOCK * b : BLOCK * (b + 1), :] = (gate * (acc + direct)).astype(out_ref.dtype)


def hyena_gate(halo, edge, projected, short_filter, long_filter, conv_bias, part, parts):
    groups, taps = long_filter.shape
    row_count = projected.shape[0]
    channels = halo.shape[1]
    per_tile = LANES // (channels // groups)
    tiles = channels // LANES
    share = tiles // parts
    first = part * share
    fw = jnp.pad(long_filter[:, ::-1].astype(jnp.float32), ((0, 0), (1, 3 * BLOCK - 1 - taps)))
    edges = edge.reshape(2, 3, channels).transpose(1, 0, 2)
    filters = short_filter.reshape(3, 3, channels).transpose(1, 0, 2)
    column = lambda k: pl.BlockSpec((row_count, LANES), lambda j: (0, first + j + k * tiles))
    return pl.pallas_call(
        _gate_kernel,
        grid=(share,),
        in_specs=[
            pl.BlockSpec((per_tile, 3 * BLOCK), lambda j: (first + j, 0)),
            pl.BlockSpec((1, LANES), lambda j: (0, first + j)),
            pl.BlockSpec((3, 3, LANES), lambda j: (0, 0, first + j)),
            pl.BlockSpec((3, 2, LANES), lambda j: (0, 0, first + j)),
            pl.BlockSpec((BLOCK, LANES), lambda j: (0, first + j)),
            column(0),
            column(1),
            column(2),
        ],
        out_specs=pl.BlockSpec((row_count, LANES), lambda j: (0, j)),
        out_shape=jax.ShapeDtypeStruct((row_count, share * LANES), jnp.bfloat16),
    )(fw, conv_bias.reshape(1, channels), filters, edges, halo, projected, projected, projected)


def ring_place(c, chips):
    return jnp.where(c % 2 == 0, c // 2, chips - 1 - c // 2)


def ring_chip(q, chips):
    return jnp.where(q < chips // 2, 2 * q, 2 * (chips - 1 - q) + 1)


def carried_of(second, carrier):
    return (second * carrier).astype(jnp.bfloat16)


def on_device(tokens, projected, short_filter, long_filter, conv_bias, out_weight):
    row_count = tokens.shape[0]
    channels = out_weight.shape[0]
    chips = lax.axis_size("chip")
    width = out_weight.shape[1]
    ring = chips % 2 == 0 and chips <= 8

    chip = lax.axis_index("chip")
    core = lax.axis_index("core")
    position = ring_place(chip, chips)
    order = ring_order(chips)
    forward = [(order[i], order[(i + 1) % chips]) for i in range(chips)]
    backward = [(order[(i + 1) % chips], order[i]) for i in range(chips)]
    swap = [(0, 1), (1, 0)]
    steps = chips // 2

    weight = jnp.zeros((chips * 2, width, channels), out_weight.dtype)

    def place(weight, piece, owner_chip, row=0):
        other = lax.ppermute(piece, "core", swap)
        for k, part in ((core, piece), (1 - core, other)):
            weight = lax.dynamic_update_slice(weight, part[None], (owner_chip * 2 + k, 0, row))
        return weight

    def ring_step(step, weight, ahead, behind):
        if step == steps:
            half = channels // 2
            ahead = lax.ppermute(ahead[:, :half], "chip", forward)
            behind = lax.ppermute(behind[:, half:], "chip", backward)
            source = ring_chip((position - step) % chips, chips)
            weight = place(weight, ahead, source, 0)
            weight = place(weight, behind, source, half)
        else:
            ahead = lax.ppermute(ahead, "chip", forward)
            behind = lax.ppermute(behind, "chip", backward)
            weight = place(weight, ahead, ring_chip((position - step) % chips, chips))
            weight = place(weight, behind, ring_chip((position + step) % chips, chips))
        return weight, ahead, behind

    ahead = behind = out_weight.T
    if ring:
        weight = place(weight, ahead, chip)
        weight, ahead, behind = ring_step(1, weight, ahead, behind)

    tail = projected[row_count - BLOCK - 2 :]
    tail_mixed = [
        short_mixed(tail[:2, k * channels : (k + 1) * channels], tail[2:, k * channels : (k + 1) * channels], short_filter[:, k * channels : (k + 1) * channels])
        for k in (1, 2)
    ]
    halo = shifted(carried_of(*tail_mixed), 1)
    edge = shifted(projected[row_count - 2 :], 1)
    halo, edge, ahead, behind = lax.optimization_barrier((halo, edge, ahead, behind))
    if ring and steps >= 2:
        weight, ahead, behind = ring_step(2, weight, ahead, behind)

    inputs = (halo, edge, projected, short_filter, long_filter, conv_bias)
    first = hyena_gate(*inputs, 0, 2)
    if ring:
        first, ahead, behind, inputs = lax.optimization_barrier((first, ahead, behind, inputs))
        if steps >= 3:
            weight, ahead, behind = ring_step(3, weight, ahead, behind)
    second = hyena_gate(*inputs, 1, 2)
    if ring:
        second, ahead, behind = lax.optimization_barrier((second, ahead, behind))
        for step in range(4, steps + 1):
            weight, ahead, behind = ring_step(step, weight, ahead, behind)
    else:
        weight = lax.all_gather(out_weight.T, CTX, axis=0, tiled=True)
    weight = weight.reshape(-1, channels)
    gated = jnp.concatenate([first, second], axis=1)
    branch = lax.dot_general(gated, weight, (((1,), (1,)), ((), ())), preferred_element_type=jnp.float32)
    return (tokens.astype(jnp.float32) + branch).astype(jnp.bfloat16)


def solution(mesh):
    inner = split_mesh(mesh)
    rows = P(("groups",) + CTX, None)
    placed = (rows, rows, P(), P(), P(), P(None, CTX))
    return jax.shard_map(on_device, mesh=inner, in_specs=placed, out_specs=rows, check_vma=False)
```

```python
import jax
import jax.numpy as jnp
from jax import lax
from jax.experimental import pallas as pl
from jax.experimental.pallas import tpu as pltpu
from jax.sharding import Mesh
from jax.sharding import PartitionSpec as P

CTX = ("chip", "core")
BLOCK = 128
LANES = 128


def split_mesh(mesh):
    groups, ctx = mesh.devices.shape
    return Mesh(mesh.devices.reshape(groups, ctx // 2, 2), ("groups",) + CTX)


def shifted(block, distance):
    devices = range(lax.axis_size(CTX))
    route = [(i - distance, i) for i in devices if i - distance in devices]
    return lax.ppermute(block, CTX, route)


def ring_order(chips):
    down = [2 * i for i in range(chips // 2)]
    up = [2 * i + 1 for i in reversed(range(chips // 2))]
    return down + up


def short_mixed(edge, rows, short_filter):
    previous = jnp.concatenate([edge[1:], rows[:-1]], axis=0).astype(jnp.float32)
    before = jnp.concatenate([edge, rows[:-2]], axis=0).astype(jnp.float32)
    total = short_filter[0] * rows.astype(jnp.float32)
    total = total + short_filter[1] * previous
    return total + short_filter[2] * before


def _gate_kernel(fw_ref, bias_ref, sf_ref, edge_ref, halo_ref, gate_ref, second_ref, carrier_ref, out_ref):
    lanes = out_ref.shape[1]
    per_tile = fw_ref.shape[0]
    group = lanes // per_tile
    row_count = out_ref.shape[0]
    blocks = row_count // BLOCK
    row = lax.broadcasted_iota(jnp.int32, (row_count, lanes), 0)

    def mixed(k, ref):
        x = ref[...].astype(jnp.float32)
        edge = edge_ref[k].astype(jnp.float32)
        taps = sf_ref[k]
        previous = jnp.where(row == 0, edge[1:2], pltpu.roll(x, 1, 0))
        before = jnp.where(row == 0, edge[0:1], jnp.where(row == 1, edge[1:2], pltpu.roll(x, 2, 0)))
        total = taps[0:1] * x
        total = total + taps[1:2] * previous
        return total + taps[2:3] * before

    gate_rows = mixed(0, gate_ref)
    carried = (mixed(1, second_ref) * mixed(2, carrier_ref)).astype(jnp.bfloat16)

    owner = lax.broadcasted_iota(jnp.int32, (1, lanes), 1) // group
    toeplitz = []
    for i in range(per_tile):
        v = jnp.broadcast_to(fw_ref[i : i + 1, :], (BLOCK, fw_ref.shape[1]))
        rolled = pltpu.roll(v, 0, 1, stride=1, stride_axis=0)
        toeplitz.append(rolled[:, : 2 * BLOCK].astype(jnp.bfloat16))
    stacked = jnp.concatenate(toeplitz, axis=1)
    columns = []
    for b in range(blocks):
        before = halo_ref[...] if b == 0 else carried[BLOCK * (b - 1) : BLOCK * b]
        window = jnp.concatenate([before, carried[BLOCK * b : BLOCK * (b + 1)]], axis=0)
        zero = jnp.zeros_like(window)
        columns.append(jnp.concatenate([jnp.where(owner == i, window, zero) for i in range(per_tile)], axis=0))
    conv = jnp.dot(stacked, jnp.concatenate(columns, axis=1), preferred_element_type=jnp.float32)
    bias = bias_ref[...]
    for b in range(blocks):
        current = carried[BLOCK * b : BLOCK * (b + 1)]
        gate = gate_rows[BLOCK * b : BLOCK * (b + 1)]
        direct = bias * current.astype(jnp.float32)
        acc = conv[:, BLOCK * b : BLOCK * (b + 1)]
        out_ref[BLOCK * b : BLOCK * (b + 1), :] = (gate * (acc + direct)).astype(out_ref.dtype)


def gate_operands(edge, short_filter, long_filter):
    taps = long_filter.shape[1]
    channels = edge.shape[1]
    fw = jnp.pad(long_filter[:, ::-1].astype(jnp.float32), ((0, 0), (1, 3 * BLOCK - 1 - taps)))
    edges = edge.reshape(2, 3, channels).transpose(1, 0, 2)
    filters = short_filter.reshape(3, 3, channels).transpose(1, 0, 2)
    return fw, edges, filters


def hyena_gate(halo, projected, fw, edges, filters, conv_bias, part, parts):
    groups = fw.shape[0]
    row_count = projected.shape[0]
    channels = halo.shape[1]
    per_tile = LANES // (channels // groups)
    tiles = channels // LANES
    share = tiles // parts
    first = part * share
    column = lambda k: pl.BlockSpec((row_count, LANES), lambda j: (0, first + j + k * tiles))
    return pl.pallas_call(
        _gate_kernel,
        grid=(share,),
        in_specs=[
            pl.BlockSpec((per_tile, 3 * BLOCK), lambda j: (first + j, 0)),
            pl.BlockSpec((1, LANES), lambda j: (0, first + j)),
            pl.BlockSpec((3, 3, LANES), lambda j: (0, 0, first + j)),
            pl.BlockSpec((3, 2, LANES), lambda j: (0, 0, first + j)),
            pl.BlockSpec((BLOCK, LANES), lambda j: (0, first + j)),
            column(0),
            column(1),
            column(2),
        ],
        out_specs=pl.BlockSpec((row_count, LANES), lambda j: (0, j)),
        out_shape=jax.ShapeDtypeStruct((row_count, share * LANES), jnp.bfloat16),
    )(fw, conv_bias.reshape(1, channels), filters, edges, halo, projected, projected, projected)


def ring_place(c, chips):
    return jnp.where(c % 2 == 0, c // 2, chips - 1 - c // 2)


def ring_chip(q, chips):
    return jnp.where(q < chips // 2, 2 * q, 2 * (chips - 1 - q) + 1)


def carried_of(second, carrier):
    return (second * carrier).astype(jnp.bfloat16)


def on_device(tokens, projected, short_filter, long_filter, conv_bias, out_weight):
    row_count = tokens.shape[0]
    channels = out_weight.shape[0]
    chips = lax.axis_size("chip")
    width = out_weight.shape[1]
    ring = chips % 2 == 0 and chips <= 8

    chip = lax.axis_index("chip")
    core = lax.axis_index("core")
    position = ring_place(chip, chips)
    order = ring_order(chips)
    forward = [(order[i], order[(i + 1) % chips]) for i in range(chips)]
    backward = [(order[(i + 1) % chips], order[i]) for i in range(chips)]
    swap = [(0, 1), (1, 0)]
    steps = chips // 2

    weight = jnp.zeros((chips * 2 * width, channels), out_weight.dtype)

    def place(weight, piece, owner_chip, row=0):
        other = lax.ppermute(piece, "core", swap)
        for k, part in ((core, piece), (1 - core, other)):
            weight = lax.dynamic_update_slice(weight, part, ((owner_chip * 2 + k) * width, row))
        return weight

    def ring_step(step, weight, ahead, behind):
        if step == steps:
            half = channels // 2
            ahead = lax.ppermute(ahead[:, :half], "chip", forward)
            behind = lax.ppermute(behind[:, half:], "chip", backward)
            source = ring_chip((position - step) % chips, chips)
            weight = place(weight, ahead, source, 0)
            weight = place(weight, behind, source, half)
        else:
            ahead = lax.ppermute(ahead, "chip", forward)
            behind = lax.ppermute(behind, "chip", backward)
            weight = place(weight, ahead, ring_chip((position - step) % chips, chips))
            weight = place(weight, behind, ring_chip((position + step) % chips, chips))
        return weight, ahead, behind

    ahead = behind = out_weight.T
    if ring:
        weight = place(weight, ahead, chip)
        weight, ahead, behind = ring_step(1, weight, ahead, behind)

    tail = projected[row_count - BLOCK - 2 :]
    tail_mixed = [
        short_mixed(tail[:2, k * channels : (k + 1) * channels], tail[2:, k * channels : (k + 1) * channels], short_filter[:, k * channels : (k + 1) * channels])
        for k in (1, 2)
    ]
    packed = jnp.concatenate([carried_of(*tail_mixed), projected[row_count - 2 :].reshape(-1, channels)], axis=0)
    packed = shifted(packed, 1)
    halo, edge = packed[:BLOCK], packed[BLOCK:]
    halo, edge, ahead, behind = lax.optimization_barrier((halo, edge, ahead, behind))
    if ring and steps >= 2:
        weight, ahead, behind = ring_step(2, weight, ahead, behind)

    inputs = (halo, projected) + gate_operands(edge, short_filter, long_filter) + (conv_bias,)
    first = hyena_gate(*inputs, 0, 2)
    if ring:
        first, ahead, behind, inputs = lax.optimization_barrier((first, ahead, behind, inputs))
        if steps >= 3:
            weight, ahead, behind = ring_step(3, weight, ahead, behind)
    second = hyena_gate(*inputs, 1, 2)
    if ring:
        second, ahead, behind = lax.optimization_barrier((second, ahead, behind))
        for step in range(4, steps + 1):
            weight, ahead, behind = ring_step(step, weight, ahead, behind)
    else:
        weight = lax.all_gather(out_weight.T, CTX, axis=0, tiled=True)
    gated = jnp.concatenate([first, second], axis=1)
    branch = lax.dot_general(gated, weight, (((1,), (1,)), ((), ())), preferred_element_type=jnp.float32)
    return (tokens.astype(jnp.float32) + branch).astype(jnp.bfloat16)


def solution(mesh):
    inner = split_mesh(mesh)
    rows = P(("groups",) + CTX, None)
    placed = (rows, rows, P(), P(), P(), P(None, CTX))
    return jax.shard_map(on_device, mesh=inner, in_specs=placed, out_specs=rows, check_vma=False)
```

```python
import jax
import jax.numpy as jnp
from jax import lax
from jax.experimental import pallas as pl
from jax.experimental.pallas import tpu as pltpu
from jax.sharding import Mesh
from jax.sharding import PartitionSpec as P

CTX = ("chip", "core")
BLOCK = 128
LANES = 128


def split_mesh(mesh):
    groups, ctx = mesh.devices.shape
    return Mesh(mesh.devices.reshape(groups, ctx // 2, 2), ("groups",) + CTX)


def shifted(block, distance):
    devices = range(lax.axis_size(CTX))
    route = [(i - distance, i) for i in devices if i - distance in devices]
    return lax.ppermute(block, CTX, route)


def ring_order(chips):
    down = [2 * i for i in range(chips // 2)]
    up = [2 * i + 1 for i in reversed(range(chips // 2))]
    return down + up


def short_mixed(edge, rows, short_filter):
    previous = jnp.concatenate([edge[1:], rows[:-1]], axis=0).astype(jnp.float32)
    before = jnp.concatenate([edge, rows[:-2]], axis=0).astype(jnp.float32)
    total = short_filter[0] * rows.astype(jnp.float32)
    total = total + short_filter[1] * previous
    return total + short_filter[2] * before


def _gate_kernel(fw_ref, bias_ref, sf_ref, edge_ref, halo_ref, gate_ref, second_ref, carrier_ref, out_ref):
    lanes = out_ref.shape[1]
    per_tile = fw_ref.shape[0]
    group = lanes // per_tile
    row_count = out_ref.shape[0]
    blocks = row_count // BLOCK
    row = lax.broadcasted_iota(jnp.int32, (row_count, lanes), 0)

    def mixed(k, ref):
        x = ref[...].astype(jnp.float32)
        edge = edge_ref[k].astype(jnp.float32)
        taps = sf_ref[k]
        previous = jnp.where(row == 0, edge[1:2], pltpu.roll(x, 1, 0))
        before = jnp.where(row == 0, edge[0:1], jnp.where(row == 1, edge[1:2], pltpu.roll(x, 2, 0)))
        total = taps[0:1] * x
        total = total + taps[1:2] * previous
        return total + taps[2:3] * before

    gate_rows = mixed(0, gate_ref)
    carried = (mixed(1, second_ref) * mixed(2, carrier_ref)).astype(jnp.bfloat16)

    owner = lax.broadcasted_iota(jnp.int32, (1, lanes), 1) // group
    toeplitz = []
    for i in range(per_tile):
        v = jnp.broadcast_to(fw_ref[i : i + 1, :], (BLOCK, fw_ref.shape[1]))
        rolled = pltpu.roll(v, 0, 1, stride=1, stride_axis=0)
        toeplitz.append(rolled[:, : 2 * BLOCK].astype(jnp.bfloat16))
    stacked = jnp.concatenate(toeplitz, axis=1)
    columns = []
    for b in range(blocks):
        before = halo_ref[...] if b == 0 else carried[BLOCK * (b - 1) : BLOCK * b]
        window = jnp.concatenate([before, carried[BLOCK * b : BLOCK * (b + 1)]], axis=0)
        zero = jnp.zeros_like(window)
        columns.append(jnp.concatenate([jnp.where(owner == i, window, zero) for i in range(per_tile)], axis=0))
    conv = jnp.dot(stacked, jnp.concatenate(columns, axis=1), preferred_element_type=jnp.float32)
    bias = bias_ref[...]
    for b in range(blocks):
        current = carried[BLOCK * b : BLOCK * (b + 1)]
        gate = gate_rows[BLOCK * b : BLOCK * (b + 1)]
        direct = bias * current.astype(jnp.float32)
        acc = conv[:, BLOCK * b : BLOCK * (b + 1)]
        out_ref[BLOCK * b : BLOCK * (b + 1), :] = (gate * (acc + direct)).astype(out_ref.dtype)


def gate_operands(edge, short_filter, long_filter):
    taps = long_filter.shape[1]
    channels = edge.shape[1]
    fw = jnp.pad(long_filter[:, ::-1].astype(jnp.float32), ((0, 0), (1, 3 * BLOCK - 1 - taps)))
    edges = edge.reshape(2, 3, channels).transpose(1, 0, 2)
    filters = short_filter.reshape(3, 3, channels).transpose(1, 0, 2)
    return fw, edges, filters


def hyena_gate(halo, projected, fw, edges, filters, conv_bias, part, parts):
    groups = fw.shape[0]
    row_count = projected.shape[0]
    channels = halo.shape[1]
    per_tile = LANES // (channels // groups)
    tiles = channels // LANES
    share = tiles // parts
    first = part * share
    column = lambda k: pl.BlockSpec((row_count, LANES), lambda j: (0, first + j + k * tiles))
    return pl.pallas_call(
        _gate_kernel,
        grid=(share,),
        in_specs=[
            pl.BlockSpec((per_tile, 3 * BLOCK), lambda j: (first + j, 0)),
            pl.BlockSpec((1, LANES), lambda j: (0, first + j)),
            pl.BlockSpec((3, 3, LANES), lambda j: (0, 0, first + j)),
            pl.BlockSpec((3, 2, LANES), lambda j: (0, 0, first + j)),
            pl.BlockSpec((BLOCK, LANES), lambda j: (0, first + j)),
            column(0),
            column(1),
            column(2),
        ],
        out_specs=pl.BlockSpec((row_count, LANES), lambda j: (0, j)),
        out_shape=jax.ShapeDtypeStruct((row_count, share * LANES), jnp.bfloat16),
    )(fw, conv_bias.reshape(1, channels), filters, edges, halo, projected, projected, projected)


def ring_place(c, chips):
    return jnp.where(c % 2 == 0, c // 2, chips - 1 - c // 2)


def ring_chip(q, chips):
    return jnp.where(q < chips // 2, 2 * q, 2 * (chips - 1 - q) + 1)


def carried_of(second, carrier):
    return (second * carrier).astype(jnp.bfloat16)


def on_device(tokens, projected, short_filter, long_filter, conv_bias, out_weight):
    row_count = tokens.shape[0]
    channels = out_weight.shape[0]
    chips = lax.axis_size("chip")
    width = out_weight.shape[1]
    ring = chips % 2 == 0 and chips <= 8

    chip = lax.axis_index("chip")
    core = lax.axis_index("core")
    position = ring_place(chip, chips)
    order = ring_order(chips)
    forward = [(order[i], order[(i + 1) % chips]) for i in range(chips)]
    backward = [(order[(i + 1) % chips], order[i]) for i in range(chips)]
    swap = [(0, 1), (1, 0)]
    steps = chips // 2

    weight = jnp.zeros((chips * 2 * width, channels), out_weight.dtype)

    def place(weight, piece, owner_chip, row=0):
        other = lax.ppermute(piece, "core", swap)
        for k, part in ((core, piece), (1 - core, other)):
            weight = lax.dynamic_update_slice(weight, part, ((owner_chip * 2 + k) * width, row))
        return weight

    def ring_step(step, weight, ahead, behind):
        if step == steps:
            half = channels // 2
            ahead = lax.ppermute(ahead[:, :half], "chip", forward)
            behind = lax.ppermute(behind[:, half:], "chip", backward)
            source = ring_chip((position - step) % chips, chips)
            weight = place(weight, ahead, source, 0)
            weight = place(weight, behind, source, half)
        else:
            ahead = lax.ppermute(ahead, "chip", forward)
            behind = lax.ppermute(behind, "chip", backward)
            weight = place(weight, ahead, ring_chip((position - step) % chips, chips))
            weight = place(weight, behind, ring_chip((position + step) % chips, chips))
        return weight, ahead, behind

    ahead = behind = out_weight.T
    if ring:
        weight = place(weight, ahead, chip)
        weight, ahead, behind = ring_step(1, weight, ahead, behind)

    tail = projected[row_count - BLOCK - 2 :]
    tail_mixed = [
        short_mixed(tail[:2, k * channels : (k + 1) * channels], tail[2:, k * channels : (k + 1) * channels], short_filter[:, k * channels : (k + 1) * channels])
        for k in (1, 2)
    ]
    packed = jnp.concatenate([carried_of(*tail_mixed), projected[row_count - 2 :].reshape(-1, channels)], axis=0)
    packed = shifted(packed, 1)
    halo, edge = packed[:BLOCK], packed[BLOCK:]
    halo, edge, ahead, behind = lax.optimization_barrier((halo, edge, ahead, behind))
    if ring and steps >= 2:
        weight, ahead, behind = ring_step(2, weight, ahead, behind)

    inputs = (halo, projected) + gate_operands(edge, short_filter, long_filter) + (conv_bias,)
    pieces = [hyena_gate(*inputs, 0, 4), hyena_gate(*inputs, 1, 4)]
    if ring:
        pieces, ahead, behind, inputs = lax.optimization_barrier((pieces, ahead, behind, inputs))
        if steps >= 3:
            weight, ahead, behind = ring_step(3, weight, ahead, behind)
    pieces.append(hyena_gate(*inputs, 2, 4))
    if ring:
        pieces, ahead, behind, inputs = lax.optimization_barrier((pieces, ahead, behind, inputs))
        for step in range(4, steps + 1):
            weight, ahead, behind = ring_step(step, weight, ahead, behind)
    pieces.append(hyena_gate(*inputs, 3, 4))
    if not ring:
        weight = lax.all_gather(out_weight.T, CTX, axis=0, tiled=True)
    gated = jnp.concatenate(pieces, axis=1)
    branch = lax.dot_general(gated, weight, (((1,), (1,)), ((), ())), preferred_element_type=jnp.float32)
    return (tokens.astype(jnp.float32) + branch).astype(jnp.bfloat16)


def solution(mesh):
    inner = split_mesh(mesh)
    rows = P(("groups",) + CTX, None)
    placed = (rows, rows, P(), P(), P(), P(None, CTX))
    return jax.shard_map(on_device, mesh=inner, in_specs=placed, out_specs=rows, check_vma=False)
```

```python
import jax
import jax.numpy as jnp
from jax import lax
from jax.experimental import pallas as pl
from jax.experimental.pallas import tpu as pltpu
from jax.sharding import Mesh
from jax.sharding import PartitionSpec as P

CTX = ("chip", "core")
BLOCK = 128
LANES = 128


def split_mesh(mesh):
    groups, ctx = mesh.devices.shape
    return Mesh(mesh.devices.reshape(groups, ctx // 2, 2), ("groups",) + CTX)


def shifted(block, distance):
    devices = range(lax.axis_size(CTX))
    route = [(i - distance, i) for i in devices if i - distance in devices]
    return lax.ppermute(block, CTX, route)


def ring_order(chips):
    down = [2 * i for i in range(chips // 2)]
    up = [2 * i + 1 for i in reversed(range(chips // 2))]
    return down + up


def short_mixed(edge, rows, short_filter):
    previous = jnp.concatenate([edge[1:], rows[:-1]], axis=0).astype(jnp.float32)
    before = jnp.concatenate([edge, rows[:-2]], axis=0).astype(jnp.float32)
    total = short_filter[0] * rows.astype(jnp.float32)
    total = total + short_filter[1] * previous
    return total + short_filter[2] * before


def _gate_kernel(fw_ref, bias_ref, sf_ref, edge_ref, halo_ref, gate_ref, second_ref, carrier_ref, out_ref):
    lanes = out_ref.shape[1]
    per_tile = fw_ref.shape[0]
    group = lanes // per_tile
    row_count = out_ref.shape[0]
    blocks = row_count // BLOCK
    row = lax.broadcasted_iota(jnp.int32, (row_count, lanes), 0)

    def mixed(k, ref):
        x = ref[...].astype(jnp.float32)
        edge = edge_ref[k].astype(jnp.float32)
        taps = sf_ref[k]
        previous = jnp.where(row == 0, edge[1:2], pltpu.roll(x, 1, 0))
        before = jnp.where(row == 0, edge[0:1], jnp.where(row == 1, edge[1:2], pltpu.roll(x, 2, 0)))
        total = taps[0:1] * x
        total = total + taps[1:2] * previous
        return total + taps[2:3] * before

    gate_rows = mixed(0, gate_ref)
    carried = (mixed(1, second_ref) * mixed(2, carrier_ref)).astype(jnp.bfloat16)

    owner = lax.broadcasted_iota(jnp.int32, (1, lanes), 1) // group
    toeplitz = []
    for i in range(per_tile):
        v = jnp.broadcast_to(fw_ref[i : i + 1, :], (BLOCK, fw_ref.shape[1]))
        rolled = pltpu.roll(v, 0, 1, stride=1, stride_axis=0)
        toeplitz.append(rolled[:, : 2 * BLOCK].astype(jnp.bfloat16))
    stacked = jnp.concatenate(toeplitz, axis=1)
    columns = []
    for b in range(blocks):
        before = halo_ref[...] if b == 0 else carried[BLOCK * (b - 1) : BLOCK * b]
        window = jnp.concatenate([before, carried[BLOCK * b : BLOCK * (b + 1)]], axis=0)
        zero = jnp.zeros_like(window)
        columns.append(jnp.concatenate([jnp.where(owner == i, window, zero) for i in range(per_tile)], axis=0))
    conv = jnp.dot(stacked, jnp.concatenate(columns, axis=1), preferred_element_type=jnp.float32)
    bias = bias_ref[...]
    for b in range(blocks):
        current = carried[BLOCK * b : BLOCK * (b + 1)]
        gate = gate_rows[BLOCK * b : BLOCK * (b + 1)]
        direct = bias * current.astype(jnp.float32)
        acc = conv[:, BLOCK * b : BLOCK * (b + 1)]
        out_ref[BLOCK * b : BLOCK * (b + 1), :] = (gate * (acc + direct)).astype(out_ref.dtype)


def hyena_gate(halo, edge, projected, short_filter, long_filter, conv_bias, part, parts):
    groups, taps = long_filter.shape
    row_count = projected.shape[0]
    channels = halo.shape[1]
    per_tile = LANES // (channels // groups)
    tiles = channels // LANES
    share = tiles // parts
    first = part * share
    fw = jnp.pad(long_filter[:, ::-1].astype(jnp.float32), ((0, 0), (1, 3 * BLOCK - 1 - taps)))
    edges = edge.reshape(2, 3, channels).transpose(1, 0, 2)
    filters = short_filter.reshape(3, 3, channels).transpose(1, 0, 2)
    column = lambda k: pl.BlockSpec((row_count, LANES), lambda j: (0, first + j + k * tiles))
    return pl.pallas_call(
        _gate_kernel,
        grid=(share,),
        in_specs=[
            pl.BlockSpec((per_tile, 3 * BLOCK), lambda j: (first + j, 0)),
            pl.BlockSpec((1, LANES), lambda j: (0, first + j)),
            pl.BlockSpec((3, 3, LANES), lambda j: (0, 0, first + j)),
            pl.BlockSpec((3, 2, LANES), lambda j: (0, 0, first + j)),
            pl.BlockSpec((BLOCK, LANES), lambda j: (0, first + j)),
            column(0),
            column(1),
            column(2),
        ],
        out_specs=pl.BlockSpec((row_count, LANES), lambda j: (0, j)),
        out_shape=jax.ShapeDtypeStruct((row_count, share * LANES), jnp.bfloat16),
    )(fw, conv_bias.reshape(1, channels), filters, edges, halo, projected, projected, projected)


def ring_place(c, chips):
    return jnp.where(c % 2 == 0, c // 2, chips - 1 - c // 2)


def ring_chip(q, chips):
    return jnp.where(q < chips // 2, 2 * q, 2 * (chips - 1 - q) + 1)


def carried_of(second, carrier):
    return (second * carrier).astype(jnp.bfloat16)


def on_device(tokens, projected, short_filter, long_filter, conv_bias, out_weight):
    row_count = tokens.shape[0]
    channels = out_weight.shape[0]
    chips = lax.axis_size("chip")
    width = out_weight.shape[1]
    ring = chips == 8

    chip = lax.axis_index("chip")
    core = lax.axis_index("core")
    position = ring_place(chip, chips)
    order = ring_order(chips)
    forward = [(order[i], order[(i + 1) % chips]) for i in range(chips)]
    backward = [(order[(i + 1) % chips], order[i]) for i in range(chips)]
    swap = [(0, 1), (1, 0)]
    steps = chips // 2

    weight = jnp.zeros((chips * 2 * width, channels), out_weight.dtype)

    def place(weight, piece, owner_chip, row=0):
        other = lax.ppermute(piece, "core", swap)
        for k, part in ((core, piece), (1 - core, other)):
            weight = lax.dynamic_update_slice(weight, part, ((owner_chip * 2 + k) * width, row))
        return weight

    def ring_step(step, weight, ahead, behind):
        if step == steps:
            half = channels // 2
            ahead = lax.ppermute(ahead[:, :half], "chip", forward)
            behind = lax.ppermute(behind[:, half:], "chip", backward)
            source = ring_chip((position - step) % chips, chips)
            weight = place(weight, ahead, source, 0)
            weight = place(weight, behind, source, half)
        else:
            ahead = lax.ppermute(ahead, "chip", forward)
            behind = lax.ppermute(behind, "chip", backward)
            weight = place(weight, ahead, ring_chip((position - step) % chips, chips))
            weight = place(weight, behind, ring_chip((position + step) % chips, chips))
        return weight, ahead, behind

    ahead = behind = out_weight.T
    if ring:
        weight = place(weight, ahead, chip)
        weight, ahead, behind = ring_step(1, weight, ahead, behind)

    tail = projected[row_count - BLOCK - 2 :]
    tail_mixed = [
        short_mixed(tail[:2, k * channels : (k + 1) * channels], tail[2:, k * channels : (k + 1) * channels], short_filter[:, k * channels : (k + 1) * channels])
        for k in (1, 2)
    ]
    halo = shifted(carried_of(*tail_mixed), 1)
    edge = shifted(projected[row_count - 2 :], 1)
    halo, edge, ahead, behind = lax.optimization_barrier((halo, edge, ahead, behind))
    if ring and steps >= 2:
        weight, ahead, behind = ring_step(2, weight, ahead, behind)

    inputs = (halo, edge, projected, short_filter, long_filter, conv_bias)
    first = hyena_gate(*inputs, 0, 2)
    if ring:
        first, ahead, behind, inputs = lax.optimization_barrier((first, ahead, behind, inputs))
        if steps >= 3:
            weight, ahead, behind = ring_step(3, weight, ahead, behind)
    second = hyena_gate(*inputs, 1, 2)
    gated = jnp.concatenate([first, second], axis=1)
    if not ring:
        weight = lax.all_gather(out_weight.T, CTX, axis=0, tiled=True)
        branch = lax.dot_general(gated, weight, (((1,), (1,)), ((), ())), preferred_element_type=jnp.float32)
        return (tokens.astype(jnp.float32) + branch).astype(jnp.bfloat16)
    gated, ahead, behind = lax.optimization_barrier((gated, ahead, behind))
    half = channels // 2
    ahead = lax.ppermute(ahead[:, :half], "chip", forward)
    behind = lax.ppermute(behind[:, half:], "chip", backward)
    source = ring_chip((position - steps) % chips, chips)
    branch = lax.dot_general(gated, weight, (((1,), (1,)), ((), ())), preferred_element_type=jnp.float32)
    mine = jnp.concatenate([ahead, behind], axis=1)
    other = lax.ppermute(mine, "core", swap)
    pair = jnp.where(core == 0, jnp.concatenate([mine, other]), jnp.concatenate([other, mine]))
    last = lax.dot_general(gated, pair, (((1,), (1,)), ((), ())), preferred_element_type=jnp.float32)
    branch = lax.dynamic_update_slice(branch, last, (0, source * 2 * width))
    return (tokens.astype(jnp.float32) + branch).astype(jnp.bfloat16)


def solution(mesh):
    inner = split_mesh(mesh)
    rows = P(("groups",) + CTX, None)
    placed = (rows, rows, P(), P(), P(), P(None, CTX))
    return jax.shard_map(on_device, mesh=inner, in_specs=placed, out_specs=rows, check_vma=False)
```

```python
import jax
import jax.numpy as jnp
from jax import lax
from jax.experimental import pallas as pl
from jax.experimental.pallas import tpu as pltpu
from jax.sharding import Mesh
from jax.sharding import PartitionSpec as P

CTX = ("chip", "core")
BLOCK = 128
LANES = 128


def split_mesh(mesh):
    groups, ctx = mesh.devices.shape
    return Mesh(mesh.devices.reshape(groups, ctx // 2, 2), ("groups",) + CTX)


def shifted(block, distance):
    devices = range(lax.axis_size(CTX))
    route = [(i - distance, i) for i in devices if i - distance in devices]
    return lax.ppermute(block, CTX, route)


def ring_order(chips):
    down = [2 * i for i in range(chips // 2)]
    up = [2 * i + 1 for i in reversed(range(chips // 2))]
    return down + up


def short_mixed(edge, rows, short_filter):
    previous = jnp.concatenate([edge[1:], rows[:-1]], axis=0).astype(jnp.float32)
    before = jnp.concatenate([edge, rows[:-2]], axis=0).astype(jnp.float32)
    total = short_filter[0] * rows.astype(jnp.float32)
    total = total + short_filter[1] * previous
    return total + short_filter[2] * before


def _gate_kernel(fw_ref, bias_ref, sf_ref, edge_ref, halo_ref, gate_ref, second_ref, carrier_ref, out_ref):
    lanes = out_ref.shape[1]
    per_tile = fw_ref.shape[0]
    group = lanes // per_tile
    row_count = out_ref.shape[0]
    blocks = row_count // BLOCK
    row = lax.broadcasted_iota(jnp.int32, (row_count, lanes), 0)

    def mixed(k, ref):
        x = ref[...].astype(jnp.float32)
        edge = edge_ref[k].astype(jnp.float32)
        taps = sf_ref[k]
        previous = jnp.where(row == 0, edge[1:2], pltpu.roll(x, 1, 0))
        before = jnp.where(row == 0, edge[0:1], jnp.where(row == 1, edge[1:2], pltpu.roll(x, 2, 0)))
        total = taps[0:1] * x
        total = total + taps[1:2] * previous
        return total + taps[2:3] * before

    gate_rows = mixed(0, gate_ref)
    carried = (mixed(1, second_ref) * mixed(2, carrier_ref)).astype(jnp.bfloat16)

    owner = lax.broadcasted_iota(jnp.int32, (1, lanes), 1) // group
    toeplitz = []
    for i in range(per_tile):
        v = jnp.broadcast_to(fw_ref[i : i + 1, :], (BLOCK, fw_ref.shape[1]))
        rolled = pltpu.roll(v, 0, 1, stride=1, stride_axis=0)
        toeplitz.append(rolled[:, : 2 * BLOCK].astype(jnp.bfloat16))
    stacked = jnp.concatenate(toeplitz, axis=1)
    columns = []
    for b in range(blocks):
        before = halo_ref[...] if b == 0 else carried[BLOCK * (b - 1) : BLOCK * b]
        window = jnp.concatenate([before, carried[BLOCK * b : BLOCK * (b + 1)]], axis=0)
        zero = jnp.zeros_like(window)
        columns.append(jnp.concatenate([jnp.where(owner == i, window, zero) for i in range(per_tile)], axis=0))
    conv = jnp.dot(stacked, jnp.concatenate(columns, axis=1), preferred_element_type=jnp.float32)
    bias = bias_ref[...]
    for b in range(blocks):
        current = carried[BLOCK * b : BLOCK * (b + 1)]
        gate = gate_rows[BLOCK * b : BLOCK * (b + 1)]
        direct = bias * current.astype(jnp.float32)
        acc = conv[:, BLOCK * b : BLOCK * (b + 1)]
        out_ref[BLOCK * b : BLOCK * (b + 1), :] = (gate * (acc + direct)).astype(out_ref.dtype)


def hyena_gate(halo, edge, projected, short_filter, long_filter, conv_bias, part, parts):
    groups, taps = long_filter.shape
    row_count = projected.shape[0]
    channels = halo.shape[1]
    per_tile = LANES // (channels // groups)
    tiles = channels // LANES
    share = tiles // parts
    first = part * share
    fw = jnp.pad(long_filter[:, ::-1].astype(jnp.float32), ((0, 0), (1, 3 * BLOCK - 1 - taps)))
    edges = edge.reshape(2, 3, channels).transpose(1, 0, 2)
    filters = short_filter.reshape(3, 3, channels).transpose(1, 0, 2)
    column = lambda k: pl.BlockSpec((row_count, LANES), lambda j: (0, first + j + k * tiles))
    return pl.pallas_call(
        _gate_kernel,
        grid=(share,),
        in_specs=[
            pl.BlockSpec((per_tile, 3 * BLOCK), lambda j: (first + j, 0)),
            pl.BlockSpec((1, LANES), lambda j: (0, first + j)),
            pl.BlockSpec((3, 3, LANES), lambda j: (0, 0, first + j)),
            pl.BlockSpec((3, 2, LANES), lambda j: (0, 0, first + j)),
            pl.BlockSpec((BLOCK, LANES), lambda j: (0, first + j)),
            column(0),
            column(1),
            column(2),
        ],
        out_specs=pl.BlockSpec((row_count, LANES), lambda j: (0, j)),
        out_shape=jax.ShapeDtypeStruct((row_count, share * LANES), jnp.bfloat16),
    )(fw, conv_bias.reshape(1, channels), filters, edges, halo, projected, projected, projected)


def ring_place(c, chips):
    return jnp.where(c % 2 == 0, c // 2, chips - 1 - c // 2)


def ring_chip(q, chips):
    return jnp.where(q < chips // 2, 2 * q, 2 * (chips - 1 - q) + 1)


def carried_of(second, carrier):
    return (second * carrier).astype(jnp.bfloat16)


def on_device(tokens, projected, short_filter, long_filter, conv_bias, out_weight):
    row_count = tokens.shape[0]
    channels = out_weight.shape[0]
    chips = lax.axis_size("chip")
    width = out_weight.shape[1]
    ring = chips == 8

    chip = lax.axis_index("chip")
    core = lax.axis_index("core")
    position = ring_place(chip, chips)
    order = ring_order(chips)
    forward = [(order[i], order[(i + 1) % chips]) for i in range(chips)]
    backward = [(order[(i + 1) % chips], order[i]) for i in range(chips)]
    swap = [(0, 1), (1, 0)]
    steps = chips // 2

    weight = jnp.zeros((chips * 2 * width, channels), out_weight.dtype)

    def place(weight, piece, owner_chip, row=0):
        other = lax.ppermute(piece, "core", swap)
        for k, part in ((core, piece), (1 - core, other)):
            weight = lax.dynamic_update_slice(weight, part, ((owner_chip * 2 + k) * width, row))
        return weight

    def ring_step(step, weight, ahead, behind):
        if step == steps:
            half = channels // 2
            ahead = lax.ppermute(ahead[:, :half], "chip", forward)
            behind = lax.ppermute(behind[:, half:], "chip", backward)
            source = ring_chip((position - step) % chips, chips)
            weight = place(weight, ahead, source, 0)
            weight = place(weight, behind, source, half)
        else:
            ahead = lax.ppermute(ahead, "chip", forward)
            behind = lax.ppermute(behind, "chip", backward)
            weight = place(weight, ahead, ring_chip((position - step) % chips, chips))
            weight = place(weight, behind, ring_chip((position + step) % chips, chips))
        return weight, ahead, behind

    ahead = behind = out_weight.T
    if ring:
        weight = place(weight, ahead, chip)
        weight, ahead, behind = ring_step(1, weight, ahead, behind)

    tail = projected[row_count - BLOCK - 2 :]
    tail_mixed = [
        short_mixed(tail[:2, k * channels : (k + 1) * channels], tail[2:, k * channels : (k + 1) * channels], short_filter[:, k * channels : (k + 1) * channels])
        for k in (1, 2)
    ]
    halo = shifted(carried_of(*tail_mixed), 1)
    edge = shifted(projected[row_count - 2 :], 1)
    halo, edge, ahead, behind = lax.optimization_barrier((halo, edge, ahead, behind))
    if ring and steps >= 2:
        weight, ahead, behind = ring_step(2, weight, ahead, behind)

    inputs = (halo, edge, projected, short_filter, long_filter, conv_bias)
    first = hyena_gate(*inputs, 0, 2)
    if ring:
        first, ahead, behind, inputs = lax.optimization_barrier((first, ahead, behind, inputs))
        ahead = lax.ppermute(ahead, "chip", forward)
        behind = lax.ppermute(behind, "chip", backward)
        late = [(ahead, ring_chip((position - 3) % chips, chips)), (behind, ring_chip((position + 3) % chips, chips))]
    second = hyena_gate(*inputs, 1, 2)
    gated = jnp.concatenate([first, second], axis=1)
    if not ring:
        weight = lax.all_gather(out_weight.T, CTX, axis=0, tiled=True)
        branch = lax.dot_general(gated, weight, (((1,), (1,)), ((), ())), preferred_element_type=jnp.float32)
        return (tokens.astype(jnp.float32) + branch).astype(jnp.bfloat16)
    gated, ahead, behind = lax.optimization_barrier((gated, ahead, behind))
    half = channels // 2
    ahead = lax.ppermute(ahead[:, :half], "chip", forward)
    behind = lax.ppermute(behind[:, half:], "chip", backward)
    source = ring_chip((position - steps) % chips, chips)
    branch = lax.dot_general(gated, weight, (((1,), (1,)), ((), ())), preferred_element_type=jnp.float32)
    late.append((jnp.concatenate([ahead, behind], axis=1), source))
    for mine, owner_chip in late:
        other = lax.ppermute(mine, "core", swap)
        pair = jnp.where(core == 0, jnp.concatenate([mine, other]), jnp.concatenate([other, mine]))
        part = lax.dot_general(gated, pair, (((1,), (1,)), ((), ())), preferred_element_type=jnp.float32)
        branch = lax.dynamic_update_slice(branch, part, (0, owner_chip * 2 * width))
    return (tokens.astype(jnp.float32) + branch).astype(jnp.bfloat16)


def solution(mesh):
    inner = split_mesh(mesh)
    rows = P(("groups",) + CTX, None)
    placed = (rows, rows, P(), P(), P(), P(None, CTX))
    return jax.shard_map(on_device, mesh=inner, in_specs=placed, out_specs=rows, check_vma=False)
```

```python
import jax
import jax.numpy as jnp
from jax import lax
from jax.experimental import pallas as pl
from jax.experimental.pallas import tpu as pltpu
from jax.sharding import Mesh
from jax.sharding import PartitionSpec as P

CTX = ("chip", "core")
BLOCK = 128
LANES = 128


def split_mesh(mesh):
    groups, ctx = mesh.devices.shape
    return Mesh(mesh.devices.reshape(groups, ctx // 2, 2), ("groups",) + CTX)


def shifted(block, distance):
    devices = range(lax.axis_size(CTX))
    route = [(i - distance, i) for i in devices if i - distance in devices]
    return lax.ppermute(block, CTX, route)


def ring_order(chips):
    down = [2 * i for i in range(chips // 2)]
    up = [2 * i + 1 for i in reversed(range(chips // 2))]
    return down + up


def short_mixed(edge, rows, short_filter):
    previous = jnp.concatenate([edge[1:], rows[:-1]], axis=0).astype(jnp.float32)
    before = jnp.concatenate([edge, rows[:-2]], axis=0).astype(jnp.float32)
    total = short_filter[0] * rows.astype(jnp.float32)
    total = total + short_filter[1] * previous
    return total + short_filter[2] * before


def _gate_kernel(fw_ref, bias_ref, sf_ref, edge_ref, halo_ref, gate_ref, second_ref, carrier_ref, out_ref):
    lanes = out_ref.shape[1]
    per_tile = fw_ref.shape[0]
    group = lanes // per_tile
    row_count = out_ref.shape[0]
    blocks = row_count // BLOCK
    row = lax.broadcasted_iota(jnp.int32, (row_count, lanes), 0)

    def mixed(k, ref):
        x = ref[...].astype(jnp.float32)
        edge = edge_ref[k].astype(jnp.float32)
        taps = sf_ref[k]
        previous = jnp.where(row == 0, edge[1:2], pltpu.roll(x, 1, 0))
        before = jnp.where(row == 0, edge[0:1], jnp.where(row == 1, edge[1:2], pltpu.roll(x, 2, 0)))
        total = taps[0:1] * x
        total = total + taps[1:2] * previous
        return total + taps[2:3] * before

    gate_rows = mixed(0, gate_ref)
    carried = (mixed(1, second_ref) * mixed(2, carrier_ref)).astype(jnp.bfloat16)

    owner = lax.broadcasted_iota(jnp.int32, (1, lanes), 1) // group
    toeplitz = []
    for i in range(per_tile):
        v = jnp.broadcast_to(fw_ref[i : i + 1, :], (BLOCK, fw_ref.shape[1]))
        rolled = pltpu.roll(v, 0, 1, stride=1, stride_axis=0)
        toeplitz.append(rolled[:, : 2 * BLOCK].astype(jnp.bfloat16))
    stacked = jnp.concatenate(toeplitz, axis=1)
    columns = []
    for b in range(blocks):
        before = halo_ref[...] if b == 0 else carried[BLOCK * (b - 1) : BLOCK * b]
        window = jnp.concatenate([before, carried[BLOCK * b : BLOCK * (b + 1)]], axis=0)
        zero = jnp.zeros_like(window)
        columns.append(jnp.concatenate([jnp.where(owner == i, window, zero) for i in range(per_tile)], axis=0))
    conv = jnp.dot(stacked, jnp.concatenate(columns, axis=1), preferred_element_type=jnp.float32)
    bias = bias_ref[...]
    for b in range(blocks):
        current = carried[BLOCK * b : BLOCK * (b + 1)]
        gate = gate_rows[BLOCK * b : BLOCK * (b + 1)]
        direct = bias * current.astype(jnp.float32)
        acc = conv[:, BLOCK * b : BLOCK * (b + 1)]
        out_ref[BLOCK * b : BLOCK * (b + 1), :] = (gate * (acc + direct)).astype(out_ref.dtype)


def gate_operands(edge, short_filter, long_filter):
    taps = long_filter.shape[1]
    channels = edge.shape[1]
    fw = jnp.pad(long_filter[:, ::-1].astype(jnp.float32), ((0, 0), (1, 3 * BLOCK - 1 - taps)))
    edges = edge.reshape(2, 3, channels).transpose(1, 0, 2)
    filters = short_filter.reshape(3, 3, channels).transpose(1, 0, 2)
    return fw, edges, filters


def hyena_gate(halo, projected, fw, edges, filters, conv_bias, part, parts):
    groups = fw.shape[0]
    row_count = projected.shape[0]
    channels = halo.shape[1]
    per_tile = LANES // (channels // groups)
    tiles = channels // LANES
    share = tiles // parts
    first = part * share
    column = lambda k: pl.BlockSpec((row_count, LANES), lambda j: (0, first + j + k * tiles))
    return pl.pallas_call(
        _gate_kernel,
        grid=(share,),
        in_specs=[
            pl.BlockSpec((per_tile, 3 * BLOCK), lambda j: (first + j, 0)),
            pl.BlockSpec((1, LANES), lambda j: (0, first + j)),
            pl.BlockSpec((3, 3, LANES), lambda j: (0, 0, first + j)),
            pl.BlockSpec((3, 2, LANES), lambda j: (0, 0, first + j)),
            pl.BlockSpec((BLOCK, LANES), lambda j: (0, first + j)),
            column(0),
            column(1),
            column(2),
        ],
        out_specs=pl.BlockSpec((row_count, LANES), lambda j: (0, j)),
        out_shape=jax.ShapeDtypeStruct((row_count, share * LANES), jnp.bfloat16),
    )(fw, conv_bias.reshape(1, channels), filters, edges, halo, projected, projected, projected)


def ring_place(c, chips):
    return jnp.where(c % 2 == 0, c // 2, chips - 1 - c // 2)


def ring_chip(q, chips):
    return jnp.where(q < chips // 2, 2 * q, 2 * (chips - 1 - q) + 1)


def carried_of(second, carrier):
    return (second * carrier).astype(jnp.bfloat16)


def on_device(tokens, projected, short_filter, long_filter, conv_bias, out_weight):
    row_count = tokens.shape[0]
    channels = out_weight.shape[0]
    chips = lax.axis_size("chip")
    width = out_weight.shape[1]
    ring = chips == 8

    chip = lax.axis_index("chip")
    core = lax.axis_index("core")
    position = ring_place(chip, chips)
    order = ring_order(chips)
    forward = [(order[i], order[(i + 1) % chips]) for i in range(chips)]
    backward = [(order[(i + 1) % chips], order[i]) for i in range(chips)]
    swap = [(0, 1), (1, 0)]
    steps = chips // 2

    weight = jnp.zeros((chips * 2 * width, channels), out_weight.dtype)

    def place(weight, piece, owner_chip, row=0):
        other = lax.ppermute(piece, "core", swap)
        for k, part in ((core, piece), (1 - core, other)):
            weight = lax.dynamic_update_slice(weight, part, ((owner_chip * 2 + k) * width, row))
        return weight

    def ring_step(step, weight, ahead, behind):
        if step == steps:
            half = channels // 2
            ahead = lax.ppermute(ahead[:, :half], "chip", forward)
            behind = lax.ppermute(behind[:, half:], "chip", backward)
            source = ring_chip((position - step) % chips, chips)
            weight = place(weight, ahead, source, 0)
            weight = place(weight, behind, source, half)
        else:
            ahead = lax.ppermute(ahead, "chip", forward)
            behind = lax.ppermute(behind, "chip", backward)
            weight = place(weight, ahead, ring_chip((position - step) % chips, chips))
            weight = place(weight, behind, ring_chip((position + step) % chips, chips))
        return weight, ahead, behind

    ahead = behind = out_weight.T
    if ring:
        weight = place(weight, ahead, chip)
        weight, ahead, behind = ring_step(1, weight, ahead, behind)

    tail = projected[row_count - BLOCK - 2 :]
    tail_mixed = [
        short_mixed(tail[:2, k * channels : (k + 1) * channels], tail[2:, k * channels : (k + 1) * channels], short_filter[:, k * channels : (k + 1) * channels])
        for k in (1, 2)
    ]
    packed = jnp.concatenate([carried_of(*tail_mixed), projected[row_count - 2 :].reshape(-1, channels)], axis=0)
    packed = shifted(packed, 1)
    halo, edge = packed[:BLOCK], packed[BLOCK:]
    halo, edge, ahead, behind = lax.optimization_barrier((halo, edge, ahead, behind))
    if ring and steps >= 2:
        weight, ahead, behind = ring_step(2, weight, ahead, behind)

    inputs = (halo, projected) + gate_operands(edge, short_filter, long_filter) + (conv_bias,)
    first = hyena_gate(*inputs, 0, 2)
    if ring:
        first, ahead, behind, inputs = lax.optimization_barrier((first, ahead, behind, inputs))
        if steps >= 3:
            weight, ahead, behind = ring_step(3, weight, ahead, behind)
    second = hyena_gate(*inputs, 1, 2)
    gated = jnp.concatenate([first, second], axis=1)
    if not ring:
        weight = lax.all_gather(out_weight.T, CTX, axis=0, tiled=True)
        branch = lax.dot_general(gated, weight, (((1,), (1,)), ((), ())), preferred_element_type=jnp.float32)
        return (tokens.astype(jnp.float32) + branch).astype(jnp.bfloat16)
    gated, ahead, behind = lax.optimization_barrier((gated, ahead, behind))
    half = channels // 2
    ahead = lax.ppermute(ahead[:, :half], "chip", forward)
    behind = lax.ppermute(behind[:, half:], "chip", backward)
    source = ring_chip((position - steps) % chips, chips)
    branch = lax.dot_general(gated, weight, (((1,), (1,)), ((), ())), preferred_element_type=jnp.float32)
    mine = jnp.concatenate([ahead, behind], axis=1)
    other = lax.ppermute(mine, "core", swap)
    pair = jnp.where(core == 0, jnp.concatenate([mine, other]), jnp.concatenate([other, mine]))
    last = lax.dot_general(gated, pair, (((1,), (1,)), ((), ())), preferred_element_type=jnp.float32)
    branch = lax.dynamic_update_slice(branch, last, (0, source * 2 * width))
    return (tokens.astype(jnp.float32) + branch).astype(jnp.bfloat16)


def solution(mesh):
    inner = split_mesh(mesh)
    rows = P(("groups",) + CTX, None)
    placed = (rows, rows, P(), P(), P(), P(None, CTX))
    return jax.shard_map(on_device, mesh=inner, in_specs=placed, out_specs=rows, check_vma=False)
```

```python
import jax
import jax.numpy as jnp
from jax import lax
from jax.experimental import pallas as pl
from jax.experimental.pallas import tpu as pltpu
from jax.sharding import Mesh
from jax.sharding import PartitionSpec as P

CTX = ("chip", "core")
BLOCK = 128
LANES = 128


def split_mesh(mesh):
    groups, ctx = mesh.devices.shape
    return Mesh(mesh.devices.reshape(groups, ctx // 2, 2), ("groups",) + CTX)


def shifted(block, distance):
    devices = range(lax.axis_size(CTX))
    route = [(i - distance, i) for i in devices if i - distance in devices]
    return lax.ppermute(block, CTX, route)


def ring_order(chips):
    down = [2 * i for i in range(chips // 2)]
    up = [2 * i + 1 for i in reversed(range(chips // 2))]
    return down + up


def short_mixed(edge, rows, short_filter):
    previous = jnp.concatenate([edge[1:], rows[:-1]], axis=0).astype(jnp.float32)
    before = jnp.concatenate([edge, rows[:-2]], axis=0).astype(jnp.float32)
    total = short_filter[0] * rows.astype(jnp.float32)
    total = total + short_filter[1] * previous
    return total + short_filter[2] * before


def _gate_kernel(fw_ref, bias_ref, sf_ref, edge_ref, halo_ref, gate_ref, second_ref, carrier_ref, out_ref):
    lanes = out_ref.shape[1]
    per_tile = fw_ref.shape[0]
    group = lanes // per_tile
    row_count = out_ref.shape[0]
    blocks = row_count // BLOCK
    row = lax.broadcasted_iota(jnp.int32, (row_count, lanes), 0)

    def mixed(k, ref):
        x = ref[...].astype(jnp.float32)
        edge = edge_ref[k].astype(jnp.float32)
        taps = sf_ref[k]
        previous = jnp.where(row == 0, edge[1:2], pltpu.roll(x, 1, 0))
        before = jnp.where(row == 0, edge[0:1], jnp.where(row == 1, edge[1:2], pltpu.roll(x, 2, 0)))
        total = taps[0:1] * x
        total = total + taps[1:2] * previous
        return total + taps[2:3] * before

    gate_rows = mixed(0, gate_ref)
    carried = (mixed(1, second_ref) * mixed(2, carrier_ref)).astype(jnp.bfloat16)

    owner = lax.broadcasted_iota(jnp.int32, (1, lanes), 1) // group
    toeplitz = []
    for i in range(per_tile):
        v = jnp.broadcast_to(fw_ref[i : i + 1, :], (BLOCK, fw_ref.shape[1]))
        rolled = pltpu.roll(v, 0, 1, stride=1, stride_axis=0)
        toeplitz.append(rolled[:, : 2 * BLOCK].astype(jnp.bfloat16))
    stacked = jnp.concatenate(toeplitz, axis=1)
    columns = []
    for b in range(blocks):
        before = halo_ref[...] if b == 0 else carried[BLOCK * (b - 1) : BLOCK * b]
        window = jnp.concatenate([before, carried[BLOCK * b : BLOCK * (b + 1)]], axis=0)
        zero = jnp.zeros_like(window)
        columns.append(jnp.concatenate([jnp.where(owner == i, window, zero) for i in range(per_tile)], axis=0))
    conv = jnp.dot(stacked, jnp.concatenate(columns, axis=1), preferred_element_type=jnp.float32)
    bias = bias_ref[...]
    for b in range(blocks):
        current = carried[BLOCK * b : BLOCK * (b + 1)]
        gate = gate_rows[BLOCK * b : BLOCK * (b + 1)]
        direct = bias * current.astype(jnp.float32)
        acc = conv[:, BLOCK * b : BLOCK * (b + 1)]
        out_ref[BLOCK * b : BLOCK * (b + 1), :] = (gate * (acc + direct)).astype(out_ref.dtype)


def hyena_gate(halo, edge, projected, short_filter, long_filter, conv_bias, part, parts):
    groups, taps = long_filter.shape
    row_count = projected.shape[0]
    channels = halo.shape[1]
    per_tile = LANES // (channels // groups)
    tiles = channels // LANES
    share = tiles // parts
    first = part * share
    fw = jnp.pad(long_filter[:, ::-1].astype(jnp.float32), ((0, 0), (1, 3 * BLOCK - 1 - taps)))
    edges = edge.reshape(2, 3, channels).transpose(1, 0, 2)
    filters = short_filter.reshape(3, 3, channels).transpose(1, 0, 2)
    column = lambda k: pl.BlockSpec((row_count, LANES), lambda j: (0, first + j + k * tiles))
    return pl.pallas_call(
        _gate_kernel,
        grid=(share,),
        in_specs=[
            pl.BlockSpec((per_tile, 3 * BLOCK), lambda j: (first + j, 0)),
            pl.BlockSpec((1, LANES), lambda j: (0, first + j)),
            pl.BlockSpec((3, 3, LANES), lambda j: (0, 0, first + j)),
            pl.BlockSpec((3, 2, LANES), lambda j: (0, 0, first + j)),
            pl.BlockSpec((BLOCK, LANES), lambda j: (0, first + j)),
            column(0),
            column(1),
            column(2),
        ],
        out_specs=pl.BlockSpec((row_count, LANES), lambda j: (0, j)),
        out_shape=jax.ShapeDtypeStruct((row_count, share * LANES), jnp.bfloat16),
    )(fw, conv_bias.reshape(1, channels), filters, edges, halo, projected, projected, projected)


def ring_place(c, chips):
    return jnp.where(c % 2 == 0, c // 2, chips - 1 - c // 2)


def ring_chip(q, chips):
    return jnp.where(q < chips // 2, 2 * q, 2 * (chips - 1 - q) + 1)


def carried_of(second, carrier):
    return (second * carrier).astype(jnp.bfloat16)


def on_device(tokens, projected, short_filter, long_filter, conv_bias, out_weight):
    row_count = tokens.shape[0]
    channels = out_weight.shape[0]
    chips = lax.axis_size("chip")
    width = out_weight.shape[1]
    ring = chips == 8

    chip = lax.axis_index("chip")
    core = lax.axis_index("core")
    position = ring_place(chip, chips)
    order = ring_order(chips)
    forward = [(order[i], order[(i + 1) % chips]) for i in range(chips)]
    backward = [(order[(i + 1) % chips], order[i]) for i in range(chips)]
    swap = [(0, 1), (1, 0)]
    steps = chips // 2

    late = []

    def ring_step(step, ahead, behind):
        ahead = lax.ppermute(ahead, "chip", forward)
        behind = lax.ppermute(behind, "chip", backward)
        late.append((ahead, lax.ppermute(ahead, "core", swap), ring_chip((position - step) % chips, chips)))
        late.append((behind, lax.ppermute(behind, "core", swap), ring_chip((position + step) % chips, chips)))
        return ahead, behind

    ahead = behind = out_weight.T
    if ring:
        late.append((ahead, lax.ppermute(ahead, "core", swap), chip))
        ahead, behind = ring_step(1, ahead, behind)

    tail = projected[row_count - BLOCK - 2 :]
    tail_mixed = [
        short_mixed(tail[:2, k * channels : (k + 1) * channels], tail[2:, k * channels : (k + 1) * channels], short_filter[:, k * channels : (k + 1) * channels])
        for k in (1, 2)
    ]
    halo = shifted(carried_of(*tail_mixed), 1)
    edge = shifted(projected[row_count - 2 :], 1)
    halo, edge, ahead, behind = lax.optimization_barrier((halo, edge, ahead, behind))
    if ring:
        ahead, behind = ring_step(2, ahead, behind)

    inputs = (halo, edge, projected, short_filter, long_filter, conv_bias)
    first = hyena_gate(*inputs, 0, 2)
    if ring:
        first, ahead, behind, inputs = lax.optimization_barrier((first, ahead, behind, inputs))
        ahead, behind = ring_step(3, ahead, behind)
    second = hyena_gate(*inputs, 1, 2)
    gated = jnp.concatenate([first, second], axis=1)
    if not ring:
        weight = lax.all_gather(out_weight.T, CTX, axis=0, tiled=True)
        branch = lax.dot_general(gated, weight, (((1,), (1,)), ((), ())), preferred_element_type=jnp.float32)
        return (tokens.astype(jnp.float32) + branch).astype(jnp.bfloat16)
    gated, ahead, behind = lax.optimization_barrier((gated, ahead, behind))
    half = channels // 2
    ahead = lax.ppermute(ahead[:, :half], "chip", forward)
    behind = lax.ppermute(behind[:, half:], "chip", backward)
    source = ring_chip((position - steps) % chips, chips)
    branch = jnp.zeros((row_count, chips * 2 * width), jnp.float32)
    last = jnp.concatenate([ahead, behind], axis=1)
    late.append((last, lax.ppermute(last, "core", swap), source))
    for mine, other, owner_chip in late:
        pair = jnp.where(core == 0, jnp.concatenate([mine, other]), jnp.concatenate([other, mine]))
        part = lax.dot_general(gated, pair, (((1,), (1,)), ((), ())), preferred_element_type=jnp.float32)
        branch = lax.dynamic_update_slice(branch, part, (0, owner_chip * 2 * width))
    return (tokens.astype(jnp.float32) + branch).astype(jnp.bfloat16)


def solution(mesh):
    inner = split_mesh(mesh)
    rows = P(("groups",) + CTX, None)
    placed = (rows, rows, P(), P(), P(), P(None, CTX))
    return jax.shard_map(on_device, mesh=inner, in_specs=placed, out_specs=rows, check_vma=False)
```

```python
import jax
import jax.numpy as jnp
from jax import lax
from jax.experimental import pallas as pl
from jax.experimental.pallas import tpu as pltpu
from jax.sharding import Mesh
from jax.sharding import PartitionSpec as P

CTX = ("chip", "core")
BLOCK = 128
LANES = 128


def split_mesh(mesh):
    groups, ctx = mesh.devices.shape
    return Mesh(mesh.devices.reshape(groups, ctx // 2, 2), ("groups",) + CTX)


def shifted(block, distance):
    devices = range(lax.axis_size(CTX))
    route = [(i - distance, i) for i in devices if i - distance in devices]
    return lax.ppermute(block, CTX, route)


def ring_order(chips):
    down = [2 * i for i in range(chips // 2)]
    up = [2 * i + 1 for i in reversed(range(chips // 2))]
    return down + up


def short_mixed(edge, rows, short_filter):
    previous = jnp.concatenate([edge[1:], rows[:-1]], axis=0).astype(jnp.float32)
    before = jnp.concatenate([edge, rows[:-2]], axis=0).astype(jnp.float32)
    total = short_filter[0] * rows.astype(jnp.float32)
    total = total + short_filter[1] * previous
    return total + short_filter[2] * before


def _gate_kernel(fw_ref, bias_ref, sf_ref, edge_ref, halo_ref, gate_ref, second_ref, carrier_ref, out_ref):
    lanes = out_ref.shape[1]
    per_tile = fw_ref.shape[0]
    group = lanes // per_tile
    row_count = out_ref.shape[0]
    blocks = row_count // BLOCK
    row = lax.broadcasted_iota(jnp.int32, (row_count, lanes), 0)

    def mixed(k, ref):
        x = ref[...].astype(jnp.float32)
        edge = edge_ref[k].astype(jnp.float32)
        taps = sf_ref[k]
        previous = jnp.where(row == 0, edge[1:2], pltpu.roll(x, 1, 0))
        before = jnp.where(row == 0, edge[0:1], jnp.where(row == 1, edge[1:2], pltpu.roll(x, 2, 0)))
        total = taps[0:1] * x
        total = total + taps[1:2] * previous
        return total + taps[2:3] * before

    gate_rows = mixed(0, gate_ref)
    carried = (mixed(1, second_ref) * mixed(2, carrier_ref)).astype(jnp.bfloat16)

    owner = lax.broadcasted_iota(jnp.int32, (1, lanes), 1) // group
    toeplitz = []
    for i in range(per_tile):
        v = jnp.broadcast_to(fw_ref[i : i + 1, :], (BLOCK, fw_ref.shape[1]))
        rolled = pltpu.roll(v, 0, 1, stride=1, stride_axis=0)
        toeplitz.append(rolled[:, : 2 * BLOCK].astype(jnp.bfloat16))
    stacked = jnp.concatenate(toeplitz, axis=1)
    columns = []
    for b in range(blocks):
        before = halo_ref[...] if b == 0 else carried[BLOCK * (b - 1) : BLOCK * b]
        window = jnp.concatenate([before, carried[BLOCK * b : BLOCK * (b + 1)]], axis=0)
        zero = jnp.zeros_like(window)
        columns.append(jnp.concatenate([jnp.where(owner == i, window, zero) for i in range(per_tile)], axis=0))
    conv = jnp.dot(stacked, jnp.concatenate(columns, axis=1), preferred_element_type=jnp.float32)
    bias = bias_ref[...]
    for b in range(blocks):
        current = carried[BLOCK * b : BLOCK * (b + 1)]
        gate = gate_rows[BLOCK * b : BLOCK * (b + 1)]
        direct = bias * current.astype(jnp.float32)
        acc = conv[:, BLOCK * b : BLOCK * (b + 1)]
        out_ref[BLOCK * b : BLOCK * (b + 1), :] = (gate * (acc + direct)).astype(out_ref.dtype)


def hyena_gate(halo, edge, projected, short_filter, long_filter, conv_bias, part, parts):
    groups, taps = long_filter.shape
    row_count = projected.shape[0]
    channels = halo.shape[1]
    per_tile = LANES // (channels // groups)
    tiles = channels // LANES
    share = tiles // parts
    first = part * share
    fw = jnp.pad(long_filter[:, ::-1].astype(jnp.float32), ((0, 0), (1, 3 * BLOCK - 1 - taps)))
    edges = edge.reshape(2, 3, channels).transpose(1, 0, 2)
    filters = short_filter.reshape(3, 3, channels).transpose(1, 0, 2)
    column = lambda k: pl.BlockSpec((row_count, LANES), lambda j: (0, first + j + k * tiles))
    return pl.pallas_call(
        _gate_kernel,
        grid=(share,),
        in_specs=[
            pl.BlockSpec((per_tile, 3 * BLOCK), lambda j: (first + j, 0)),
            pl.BlockSpec((1, LANES), lambda j: (0, first + j)),
            pl.BlockSpec((3, 3, LANES), lambda j: (0, 0, first + j)),
            pl.BlockSpec((3, 2, LANES), lambda j: (0, 0, first + j)),
            pl.BlockSpec((BLOCK, LANES), lambda j: (0, first + j)),
            column(0),
            column(1),
            column(2),
        ],
        out_specs=pl.BlockSpec((row_count, LANES), lambda j: (0, j)),
        out_shape=jax.ShapeDtypeStruct((row_count, share * LANES), jnp.bfloat16),
    )(fw, conv_bias.reshape(1, channels), filters, edges, halo, projected, projected, projected)


def ring_place(c, chips):
    return jnp.where(c % 2 == 0, c // 2, chips - 1 - c // 2)


def ring_chip(q, chips):
    return jnp.where(q < chips // 2, 2 * q, 2 * (chips - 1 - q) + 1)


def carried_of(second, carrier):
    return (second * carrier).astype(jnp.bfloat16)


def on_device(tokens, projected, short_filter, long_filter, conv_bias, out_weight):
    row_count = tokens.shape[0]
    channels = out_weight.shape[0]
    chips = lax.axis_size("chip")
    width = out_weight.shape[1]
    ring = chips == 8

    chip = lax.axis_index("chip")
    core = lax.axis_index("core")
    position = ring_place(chip, chips)
    order = ring_order(chips)
    forward = [(order[i], order[(i + 1) % chips]) for i in range(chips)]
    backward = [(order[(i + 1) % chips], order[i]) for i in range(chips)]
    swap = [(0, 1), (1, 0)]
    steps = chips // 2

    late = []

    def ring_step(step, ahead, behind):
        ahead = lax.ppermute(ahead, "chip", forward)
        behind = lax.ppermute(behind, "chip", backward)
        late.append((ahead, lax.ppermute(ahead, "core", swap), ring_chip((position - step) % chips, chips)))
        late.append((behind, lax.ppermute(behind, "core", swap), ring_chip((position + step) % chips, chips)))
        return ahead, behind

    ahead = behind = out_weight.T
    if ring:
        late.append((ahead, lax.ppermute(ahead, "core", swap), chip))
        ahead, behind = ring_step(1, ahead, behind)

    tail = projected[row_count - BLOCK - 2 :]
    tail_mixed = [
        short_mixed(tail[:2, k * channels : (k + 1) * channels], tail[2:, k * channels : (k + 1) * channels], short_filter[:, k * channels : (k + 1) * channels])
        for k in (1, 2)
    ]
    halo = shifted(carried_of(*tail_mixed), 1)
    edge = shifted(projected[row_count - 2 :], 1)
    halo, edge, ahead, behind = lax.optimization_barrier((halo, edge, ahead, behind))
    if ring:
        ahead, behind = ring_step(2, ahead, behind)

    inputs = (halo, edge, projected, short_filter, long_filter, conv_bias)
    first = hyena_gate(*inputs, 0, 2)
    if ring:
        first, ahead, behind, inputs = lax.optimization_barrier((first, ahead, behind, inputs))
        ahead, behind = ring_step(3, ahead, behind)
    second = hyena_gate(*inputs, 1, 2)
    gated = jnp.concatenate([first, second], axis=1)
    if not ring:
        weight = lax.all_gather(out_weight.T, CTX, axis=0, tiled=True)
        branch = lax.dot_general(gated, weight, (((1,), (1,)), ((), ())), preferred_element_type=jnp.float32)
        return (tokens.astype(jnp.float32) + branch).astype(jnp.bfloat16)
    gated, ahead, behind = lax.optimization_barrier((gated, ahead, behind))
    half = channels // 2
    ahead = lax.ppermute(ahead[:, :half], "chip", forward)
    behind = lax.ppermute(behind[:, half:], "chip", backward)
    source = ring_chip((position - steps) % chips, chips)
    result = tokens
    last = jnp.concatenate([ahead, behind], axis=1)
    late.append((last, lax.ppermute(last, "core", swap), source))
    for mine, other, owner_chip in late:
        pair = jnp.where(core == 0, jnp.concatenate([mine, other]), jnp.concatenate([other, mine]))
        part = lax.dot_general(gated, pair, (((1,), (1,)), ((), ())), preferred_element_type=jnp.float32)
        column = owner_chip * 2 * width
        rows = lax.dynamic_slice_in_dim(tokens, column, 2 * width, 1).astype(jnp.float32)
        result = lax.dynamic_update_slice(result, (rows + part).astype(jnp.bfloat16), (0, column))
    return result


def solution(mesh):
    inner = split_mesh(mesh)
    rows = P(("groups",) + CTX, None)
    placed = (rows, rows, P(), P(), P(), P(None, CTX))
    return jax.shard_map(on_device, mesh=inner, in_specs=placed, out_specs=rows, check_vma=False)
```

```python
import jax
import jax.numpy as jnp
from jax import lax
from jax.experimental import pallas as pl
from jax.experimental.pallas import tpu as pltpu
from jax.sharding import Mesh
from jax.sharding import PartitionSpec as P

CTX = ("chip", "core")
BLOCK = 128
LANES = 128


def split_mesh(mesh):
    groups, ctx = mesh.devices.shape
    return Mesh(mesh.devices.reshape(groups, ctx // 2, 2), ("groups",) + CTX)


def shifted(block, distance):
    devices = range(lax.axis_size(CTX))
    route = [(i - distance, i) for i in devices if i - distance in devices]
    return lax.ppermute(block, CTX, route)


def ring_order(chips):
    down = [2 * i for i in range(chips // 2)]
    up = [2 * i + 1 for i in reversed(range(chips // 2))]
    return down + up


def short_mixed(edge, rows, short_filter):
    previous = jnp.concatenate([edge[1:], rows[:-1]], axis=0).astype(jnp.float32)
    before = jnp.concatenate([edge, rows[:-2]], axis=0).astype(jnp.float32)
    total = short_filter[0] * rows.astype(jnp.float32)
    total = total + short_filter[1] * previous
    return total + short_filter[2] * before


def _gate_kernel(fw_ref, bias_ref, sf_ref, edge_ref, halo_ref, gate_ref, second_ref, carrier_ref, out_ref):
    lanes = out_ref.shape[1]
    per_tile = fw_ref.shape[0]
    group = lanes // per_tile
    row_count = out_ref.shape[0]
    blocks = row_count // BLOCK
    row = lax.broadcasted_iota(jnp.int32, (row_count, lanes), 0)

    def mixed(k, ref):
        x = ref[...].astype(jnp.float32)
        edge = edge_ref[k].astype(jnp.float32)
        taps = sf_ref[k]
        previous = jnp.where(row == 0, edge[1:2], pltpu.roll(x, 1, 0))
        before = jnp.where(row == 0, edge[0:1], jnp.where(row == 1, edge[1:2], pltpu.roll(x, 2, 0)))
        total = taps[0:1] * x
        total = total + taps[1:2] * previous
        return total + taps[2:3] * before

    gate_rows = mixed(0, gate_ref)
    carried = (mixed(1, second_ref) * mixed(2, carrier_ref)).astype(jnp.bfloat16)

    owner = lax.broadcasted_iota(jnp.int32, (1, lanes), 1) // group
    toeplitz = []
    for i in range(per_tile):
        v = jnp.broadcast_to(fw_ref[i : i + 1, :], (BLOCK, fw_ref.shape[1]))
        rolled = pltpu.roll(v, 0, 1, stride=1, stride_axis=0)
        toeplitz.append(rolled[:, : 2 * BLOCK].astype(jnp.bfloat16))
    stacked = jnp.concatenate(toeplitz, axis=1)
    columns = []
    for b in range(blocks):
        before = halo_ref[...] if b == 0 else carried[BLOCK * (b - 1) : BLOCK * b]
        window = jnp.concatenate([before, carried[BLOCK * b : BLOCK * (b + 1)]], axis=0)
        zero = jnp.zeros_like(window)
        columns.append(jnp.concatenate([jnp.where(owner == i, window, zero) for i in range(per_tile)], axis=0))
    conv = jnp.dot(stacked, jnp.concatenate(columns, axis=1), preferred_element_type=jnp.float32)
    bias = bias_ref[...]
    for b in range(blocks):
        current = carried[BLOCK * b : BLOCK * (b + 1)]
        gate = gate_rows[BLOCK * b : BLOCK * (b + 1)]
        direct = bias * current.astype(jnp.float32)
        acc = conv[:, BLOCK * b : BLOCK * (b + 1)]
        out_ref[BLOCK * b : BLOCK * (b + 1), :] = (gate * (acc + direct)).astype(out_ref.dtype)


def hyena_gate(halo, edge, projected, short_filter, long_filter, conv_bias, part, parts):
    groups, taps = long_filter.shape
    row_count = projected.shape[0]
    channels = halo.shape[1]
    per_tile = LANES // (channels // groups)
    tiles = channels // LANES
    share = tiles // parts
    first = part * share
    fw = jnp.pad(long_filter[:, ::-1].astype(jnp.float32), ((0, 0), (1, 3 * BLOCK - 1 - taps)))
    edges = edge.reshape(2, 3, channels).transpose(1, 0, 2)
    filters = short_filter.reshape(3, 3, channels).transpose(1, 0, 2)
    column = lambda k: pl.BlockSpec((row_count, LANES), lambda j: (0, first + j + k * tiles))
    return pl.pallas_call(
        _gate_kernel,
        grid=(share,),
        in_specs=[
            pl.BlockSpec((per_tile, 3 * BLOCK), lambda j: (first + j, 0)),
            pl.BlockSpec((1, LANES), lambda j: (0, first + j)),
            pl.BlockSpec((3, 3, LANES), lambda j: (0, 0, first + j)),
            pl.BlockSpec((3, 2, LANES), lambda j: (0, 0, first + j)),
            pl.BlockSpec((BLOCK, LANES), lambda j: (0, first + j)),
            column(0),
            column(1),
            column(2),
        ],
        out_specs=pl.BlockSpec((row_count, LANES), lambda j: (0, j)),
        out_shape=jax.ShapeDtypeStruct((row_count, share * LANES), jnp.bfloat16),
    )(fw, conv_bias.reshape(1, channels), filters, edges, halo, projected, projected, projected)


def ring_place(c, chips):
    return jnp.where(c % 2 == 0, c // 2, chips - 1 - c // 2)


def ring_chip(q, chips):
    return jnp.where(q < chips // 2, 2 * q, 2 * (chips - 1 - q) + 1)


def carried_of(second, carrier):
    return (second * carrier).astype(jnp.bfloat16)


def on_device(tokens, projected, short_filter, long_filter, conv_bias, out_weight):
    row_count = tokens.shape[0]
    channels = out_weight.shape[0]
    chips = lax.axis_size("chip")
    width = out_weight.shape[1]
    ring = chips == 8

    chip = lax.axis_index("chip")
    core = lax.axis_index("core")
    position = ring_place(chip, chips)
    order = ring_order(chips)
    forward = [(order[i], order[(i + 1) % chips]) for i in range(chips)]
    backward = [(order[(i + 1) % chips], order[i]) for i in range(chips)]
    swap = [(0, 1), (1, 0)]
    steps = chips // 2

    late = []

    def ring_step(step, ahead, behind):
        ahead = lax.ppermute(ahead, "chip", forward)
        behind = lax.ppermute(behind, "chip", backward)
        late.append((ahead, lax.ppermute(ahead, "core", swap), ring_chip((position - step) % chips, chips)))
        late.append((behind, lax.ppermute(behind, "core", swap), ring_chip((position + step) % chips, chips)))
        return ahead, behind

    ahead = behind = out_weight.T
    if ring:
        late.append((ahead, lax.ppermute(ahead, "core", swap), chip))
        ahead, behind = ring_step(1, ahead, behind)

    tail = projected[row_count - BLOCK - 2 :]
    tail_mixed = [
        short_mixed(tail[:2, k * channels : (k + 1) * channels], tail[2:, k * channels : (k + 1) * channels], short_filter[:, k * channels : (k + 1) * channels])
        for k in (1, 2)
    ]
    halo = shifted(carried_of(*tail_mixed), 1)
    edge = shifted(projected[row_count - 2 :], 1)
    halo, edge, ahead, behind = lax.optimization_barrier((halo, edge, ahead, behind))
    if ring:
        ahead, behind = ring_step(2, ahead, behind)

    inputs = (halo, edge, projected, short_filter, long_filter, conv_bias)
    first = hyena_gate(*inputs, 0, 2)
    if ring:
        first, ahead, behind, inputs = lax.optimization_barrier((first, ahead, behind, inputs))
        ahead, behind = ring_step(3, ahead, behind)
    second = hyena_gate(*inputs, 1, 2)
    gated = jnp.concatenate([first, second], axis=1)
    if not ring:
        weight = lax.all_gather(out_weight.T, CTX, axis=0, tiled=True)
        branch = lax.dot_general(gated, weight, (((1,), (1,)), ((), ())), preferred_element_type=jnp.float32)
        return (tokens.astype(jnp.float32) + branch).astype(jnp.bfloat16)
    half = channels // 2
    ahead = lax.ppermute(ahead[:, :half], "chip", forward)
    behind = lax.ppermute(behind[:, half:], "chip", backward)
    source = ring_chip((position - steps) % chips, chips)
    result = tokens
    last = jnp.concatenate([ahead, behind], axis=1)
    late.append((last, lax.ppermute(last, "core", swap), source))
    for mine, other, owner_chip in late:
        pair = jnp.where(core == 0, jnp.concatenate([mine, other]), jnp.concatenate([other, mine]))
        part = lax.dot_general(gated, pair, (((1,), (1,)), ((), ())), preferred_element_type=jnp.float32)
        column = owner_chip * 2 * width
        rows = lax.dynamic_slice_in_dim(tokens, column, 2 * width, 1).astype(jnp.float32)
        result = lax.dynamic_update_slice(result, (rows + part).astype(jnp.bfloat16), (0, column))
    return result


def solution(mesh):
    inner = split_mesh(mesh)
    rows = P(("groups",) + CTX, None)
    placed = (rows, rows, P(), P(), P(), P(None, CTX))
    return jax.shard_map(on_device, mesh=inner, in_specs=placed, out_specs=rows, check_vma=False)
```
